32 devices in a mesh: dp: 8 (over z, x), tensor: 4 (over y, core).
Axes of the slice: x: 2, y: 2, z: 4, core: 2. Of those that a mesh axis runs over, the one named last changes fastest.
Arguments:
- tokens: bfloat16 [2048, 4096], P('dp', 'tensor'), may hold values from -6 to 6
- norm_gain: float32 [4096], replicated, may hold values from 0.15 to 5.4, as said below
- w_query: bfloat16 [4096, 4096], P(None, 'tensor'), may hold values from -0.09375 to 0.09375
- key_weight: bfloat16 [4096, 1024], P(None, 'tensor'), may hold values from -0.09375 to 0.09375
- value_weight: bfloat16 [4096, 1024], P(None, 'tensor'), may hold values from -0.09375 to 0.09375
- w_out: bfloat16 [4096, 4096], P('tensor'), may hold values from -0.25 to 0.25
- grad_output: bfloat16 [2048, 4096], P('dp', 'tensor'), may hold values from -6 to 6
- doc_lengths: int32 [8, 2], P('dp'), may hold values from 0 to 256, as said below
- block_owner: int32 [8, 8], replicated, may hold values from 0 to 7, as said below
Outputs:
- relaid_output: bfloat16 [2048, 4096], P('dp', 'tensor')
- input_grad: bfloat16 [2048, 4096], P('dp', 'tensor')
The draws below stay inside these ranges and needn't reach their ends.
Inputs may be any that keep to these rules, and one draw needn't show every extreme that they name: `doc_lengths`: each row lists the lengths of the documents packed on that dp index in order: multiples of 128, the nonzero ones first, summing to 256. In every draw some dp index holds a single document of 256 tokens. `block_owner`: every dp index owns exactly one block of each position j < 8 and exactly one block from each dp index. `norm_gain`: positive gains.
All inputs are finite; a program needn't handle non-finite values.
Results may differ from the reference program's by a relative error of at most 0.015.
Values may be sent and summed in bfloat16 or wider, within the bound.
No kernel may reach another device: no remote copies, remote signals or barrier semaphores. Data moves between devices by JAX's collectives and lax.ppermute only.
A program may use at most 128 MiB of HBM per device.

```python
import math
import jax
import jax.numpy as jnp
from jax import lax

MODEL_WIDTH = 4096
QUERY_HEADS = 32
KEY_VALUE_HEADS = 8
HEAD_SIZE = 128
TOK_DEV = 256
UNIT = 128
BLK = 32
NBLK = 8
SOURCES = 8
TOKENS = 2048


def draw_norm_gain(key, part):
    base_key = jax.random.fold_in(key, 37)
    feature_pos = jnp.arange(MODEL_WIDTH, dtype=jnp.float32) / (MODEL_WIDTH - 1)
    ramp = jnp.exp(jnp.log(0.35) + jnp.log(8.0) * feature_pos)
    rough = jax.random.uniform(base_key, (MODEL_WIDTH,), jnp.float32, 0.7, 1.3)
    return (ramp * rough).astype(jnp.float32)


def draw_doc_lengths(key, part):
    base_key = jax.random.fold_in(key, 11)
    flag_key, pick_key = jax.random.split(base_key)
    unit_total = TOK_DEV // UNIT
    breaks = jax.random.randint(flag_key, (SOURCES, unit_total), 0, 2).astype(jnp.int32)
    chosen = jax.random.randint(pick_key, (), 0, SOURCES).astype(jnp.int32)
    device_rows = jnp.arange(SOURCES, dtype=jnp.int32)
    unit_columns = jnp.arange(unit_total, dtype=jnp.int32)
    leading = (unit_columns[None, :] == 0).astype(jnp.int32)
    starts = jnp.where(unit_columns[None, :] == 0, 1, breaks)
    starts = jnp.where(device_rows[:, None] == chosen, leading, starts)
    doc_index = (jnp.cumsum(starts, axis=1) - 1).astype(jnp.int32)
    member = (doc_index[:, :, None] == unit_columns[None, None, :]).astype(jnp.int32)
    return (UNIT * jnp.sum(member, axis=1)).astype(jnp.int32)


def draw_block_owner(key, part):
    base_key = jax.random.fold_in(key, 23)
    first_key, second_key, third_key = jax.random.split(base_key, 3)
    order_in = jax.random.permutation(first_key, SOURCES).astype(jnp.int32)
    order_out = jax.random.permutation(second_key, SOURCES).astype(jnp.int32)
    shifts = jax.random.permutation(third_key, SOURCES).astype(jnp.int32)[:NBLK]
    placed = (order_in[:, None] + shifts[None, :]) % SOURCES
    return order_out[placed].astype(jnp.int32)


def block_levels(key, dims, cuts, low, high):
    def one(dim, shards_of):
        heights = jax.random.uniform(jax.random.fold_in(jax.random.fold_in(key, 6), dim), (shards_of,), jnp.float32, low / len(cuts), high / len(cuts))
        return jnp.repeat(jnp.exp(heights), dims[dim] // shards_of).reshape((-1,) + (1,) * (len(dims) - dim - 1))

    level = one(*cuts[0])
    for cut in cuts[1:]:
        level = level * one(*cut)
    return level


def scatter_about(stream_key, shape, scale, bound, cuts=(), held_as=jnp.bfloat16):
    drawn = scale * jax.random.normal(stream_key, shape, jnp.float32)
    if cuts:
        drawn = drawn * block_levels(stream_key, shape, cuts, -0.22, 0.18)
    return jnp.clip(drawn, -bound, bound).astype(held_as)


def setup_inputs(seed: int = 0) -> dict:
    splits = jax.random.split(jax.random.key(seed), 10)
    tokens = scatter_about(splits[0], (TOKENS, MODEL_WIDTH), 1.0, 6.0, ((0, 8), (1, 4)))
    norm_gain = draw_norm_gain(jax.random.fold_in(splits[9], 71), 0)
    w_query = scatter_about(splits[2], (MODEL_WIDTH, QUERY_HEADS * HEAD_SIZE), MODEL_WIDTH ** -0.5, 0.09375, ((1, 4),))
    key_weight = scatter_about(splits[3], (MODEL_WIDTH, KEY_VALUE_HEADS * HEAD_SIZE), MODEL_WIDTH ** -0.5, 0.09375, ((1, 4),))
    value_weight = scatter_about(splits[4], (MODEL_WIDTH, KEY_VALUE_HEADS * HEAD_SIZE), MODEL_WIDTH ** -0.5, 0.09375, ((1, 4),))
    w_out = scatter_about(splits[5], (QUERY_HEADS * HEAD_SIZE, MODEL_WIDTH), (QUERY_HEADS * HEAD_SIZE // 8) ** -0.5, 0.25, ((0, 4),))
    grad_output = scatter_about(splits[6], (TOKENS, MODEL_WIDTH), 1.0, 6.0, ((0, 8), (1, 4)))
    doc_lengths = draw_doc_lengths(jax.random.fold_in(splits[9], 71), 0)
    block_owner = draw_block_owner(jax.random.fold_in(splits[9], 71), 0)
    return dict(tokens=tokens, norm_gain=norm_gain, w_query=w_query, key_weight=key_weight, value_weight=value_weight, w_out=w_out, grad_output=grad_output, doc_lengths=doc_lengths, block_owner=block_owner)


ROPE_BASE = 500000.0
NORM_EPSILON = 1e-05

def doc_tables(lengths_row, token_row_count):
    ends = jnp.cumsum(lengths_row).astype(jnp.int32)
    token_index = jnp.arange(token_row_count, dtype=jnp.int32)
    passed = (token_index[:, None] >= ends[None, :]).astype(jnp.int32)
    doc_ids = lax.optimization_barrier(jnp.sum(passed, axis=1)).astype(jnp.int32)
    starts = lax.optimization_barrier(jnp.max(jnp.where(passed > 0, ends[None, :], 0), axis=1)).astype(jnp.int32)
    return (doc_ids, token_index - starts)

def rope_tables(positions, head_size):
    half_dim = head_size // 2
    steps = jnp.arange(half_dim, dtype=jnp.float32)
    inverse_freq = jnp.power(ROPE_BASE, -2.0 * steps / head_size)
    angles = positions.astype(jnp.float32)[:, None] * inverse_freq[None, :]
    return (jnp.cos(angles), jnp.sin(angles))

def rotate(vectors, cosine, sine_table):
    half_dim = vectors.shape[-1] // 2
    former = vectors[..., :half_dim]
    latter = vectors[..., half_dim:]
    cos_part = cosine[:, None, :]
    sin_part = sine_table[:, None, :]
    return jnp.concatenate([former * cos_part - latter * sin_part, latter * cos_part + former * sin_part], axis=-1)

def unrotate(vectors, cosine, sine_table):
    half_dim = vectors.shape[-1] // 2
    former = vectors[..., :half_dim]
    latter = vectors[..., half_dim:]
    cos_part = cosine[:, None, :]
    sin_part = sine_table[:, None, :]
    return jnp.concatenate([former * cos_part + latter * sin_part, latter * cos_part - former * sin_part], axis=-1)

def device_pass(x_rows, grad_rows, lengths_row, norm_gain, w_query, key_weight, value_weight, w_out):
    token_row_count = x_rows.shape[0]
    query_group_width = QUERY_HEADS // KEY_VALUE_HEADS
    scale_factor = 1.0 / math.sqrt(HEAD_SIZE)
    doc_ids, positions = doc_tables(lengths_row, token_row_count)
    token_index = jnp.arange(token_row_count, dtype=jnp.int32)
    allowed = (doc_ids[:, None] == doc_ids[None, :]) & (token_index[None, :] <= token_index[:, None])
    x_float = x_rows.astype(jnp.float32)
    inverse = lax.rsqrt(lax.optimization_barrier(jnp.mean(x_float * x_float, axis=1)) + NORM_EPSILON)
    normed_input = (x_float * inverse[:, None] * norm_gain[None, :]).astype(jnp.bfloat16)
    cosine, sine_table = rope_tables(positions, HEAD_SIZE)
    query_raw = jnp.dot(normed_input, w_query, preferred_element_type=jnp.float32).reshape(token_row_count, QUERY_HEADS, HEAD_SIZE)
    unrotated_key = jnp.dot(normed_input, key_weight, preferred_element_type=jnp.float32).reshape(token_row_count, KEY_VALUE_HEADS, HEAD_SIZE)
    value_rows = jnp.dot(normed_input, value_weight, preferred_element_type=jnp.float32).astype(jnp.bfloat16).reshape(token_row_count, KEY_VALUE_HEADS, HEAD_SIZE)
    query_rows = rotate(query_raw, cosine, sine_table).astype(jnp.bfloat16)
    keys = rotate(unrotated_key, cosine, sine_table).astype(jnp.bfloat16)
    grouped_query = query_rows.reshape(token_row_count, KEY_VALUE_HEADS, query_group_width, HEAD_SIZE)
    scores = jnp.einsum('qkgd,skd->kgqs', grouped_query.astype(jnp.float32), keys.astype(jnp.float32)) * scale_factor
    weights = jnp.where(allowed[None, None], jnp.exp(scores), 0.0)
    probs = weights / lax.optimization_barrier(jnp.sum(weights, axis=-1, keepdims=True))
    probs_low = probs.astype(jnp.bfloat16)
    attended = jnp.einsum('kgqs,skd->qkgd', probs_low.astype(jnp.float32), value_rows.astype(jnp.float32)).astype(jnp.bfloat16)
    attended_flat = attended.reshape(token_row_count, QUERY_HEADS * HEAD_SIZE)
    mixed = jnp.dot(attended_flat, w_out, preferred_element_type=jnp.float32)
    output_home = (x_float + mixed).astype(jnp.bfloat16)
    attended_gradient = jnp.dot(grad_rows, w_out.T, preferred_element_type=jnp.float32).astype(jnp.bfloat16)
    grouped_gradient = attended_gradient.reshape(token_row_count, KEY_VALUE_HEADS, query_group_width, HEAD_SIZE)
    delta = lax.optimization_barrier(jnp.sum(grouped_gradient.astype(jnp.float32) * attended.astype(jnp.float32), axis=-1))
    grad_probs = jnp.einsum('qkgd,skd->kgqs', grouped_gradient.astype(jnp.float32), value_rows.astype(jnp.float32))
    grad_scores = (probs * (grad_probs - jnp.transpose(delta, (1, 2, 0))[..., None])).astype(jnp.bfloat16)
    grad_query_rot = jnp.einsum('kgqs,skd->qkgd', grad_scores.astype(jnp.float32), keys.astype(jnp.float32)) * scale_factor
    grad_keys_rot = jnp.einsum('kgqs,qkgd->skd', grad_scores.astype(jnp.float32), grouped_query.astype(jnp.float32)) * scale_factor
    value_gradient = jnp.einsum('kgqs,qkgd->skd', probs_low.astype(jnp.float32), grouped_gradient.astype(jnp.float32))
    grad_query = unrotate(grad_query_rot.reshape(token_row_count, QUERY_HEADS, HEAD_SIZE), cosine, sine_table).astype(jnp.bfloat16)
    key_gradient = unrotate(grad_keys_rot, cosine, sine_table).astype(jnp.bfloat16)
    value_gradient = value_gradient.astype(jnp.bfloat16)
    normed_gradient = jnp.dot(grad_query.reshape(token_row_count, QUERY_HEADS * HEAD_SIZE), w_query.T, preferred_element_type=jnp.float32)
    normed_gradient = normed_gradient + jnp.dot(key_gradient.reshape(token_row_count, KEY_VALUE_HEADS * HEAD_SIZE), key_weight.T, preferred_element_type=jnp.float32)
    normed_gradient = normed_gradient + jnp.dot(value_gradient.reshape(token_row_count, KEY_VALUE_HEADS * HEAD_SIZE), value_weight.T, preferred_element_type=jnp.float32)
    stat = lax.optimization_barrier(jnp.sum(normed_gradient * norm_gain[None, :] * x_float, axis=1)) / MODEL_WIDTH
    cubed = inverse * inverse * inverse
    grad_x = grad_rows.astype(jnp.float32) + inverse[:, None] * norm_gain[None, :] * normed_gradient - x_float * cubed[:, None] * stat[:, None]
    return (output_home, grad_x.astype(jnp.bfloat16))

def reference(tokens, norm_gain, w_query, key_weight, value_weight, w_out, grad_output, doc_lengths, block_owner):
    owner_flat = block_owner.reshape(-1).astype(jnp.int32)
    block_total = owner_flat.shape[0]
    block_index = jnp.arange(block_total, dtype=jnp.int32)
    earlier = (owner_flat[None, :] == owner_flat[:, None]) & (block_index[None, :] < block_index[:, None])
    ranking = lax.optimization_barrier(jnp.sum(earlier.astype(jnp.int32), axis=1)).astype(jnp.int32)
    target = (owner_flat * NBLK + ranking).astype(jnp.int32)
    grad_blocks = grad_output.reshape(block_total, BLK, MODEL_WIDTH)[target]
    grad_home = grad_blocks.reshape(SOURCES, TOK_DEV, MODEL_WIDTH)

    def one_device(device_pack):
        x_rows, grad_rows, lengths_row = device_pack
        return device_pass(x_rows, grad_rows, lengths_row, norm_gain, w_query, key_weight, value_weight, w_out)
    outputs, grads = lax.map(one_device, (tokens.reshape(SOURCES, TOK_DEV, MODEL_WIDTH), grad_home, doc_lengths))
    out_blocks = outputs.reshape(block_total, BLK, MODEL_WIDTH)
    relaid = jnp.zeros_like(out_blocks).at[target].set(out_blocks)
    return (relaid.reshape(TOKENS, MODEL_WIDTH), grads.reshape(TOKENS, MODEL_WIDTH))
```

```python
import math

import jax
import jax.numpy as jnp
from jax import lax
from jax.sharding import PartitionSpec as P

HEAD_SIZE = 128


ROPE_BASE = 500000.0
NORM_EPSILON = 1e-05


def doc_tables(lengths_row, token_row_count):
    ends = jnp.cumsum(lengths_row)
    token_index = jnp.arange(token_row_count, dtype=jnp.int32)
    passed = (token_index[:, None] >= ends[None, :]).astype(jnp.int32)
    doc_ids = jnp.sum(passed, axis=1)
    starts = jnp.max(jnp.where(passed > 0, ends[None, :], 0), axis=1)
    return (doc_ids, token_index - starts)


def rope_tables(positions, head_size):
    half_dim = head_size // 2
    steps = jnp.arange(half_dim, dtype=jnp.float32)
    inverse_freq = jnp.power(ROPE_BASE, -2.0 * steps / head_size)
    angles = positions.astype(jnp.float32)[:, None] * inverse_freq[None, :]
    return (jnp.cos(angles), jnp.sin(angles))


def rotate(vectors, cosine, sine_table):
    half_dim = vectors.shape[-1] // 2
    former = vectors[..., :half_dim]
    latter = vectors[..., half_dim:]
    cos_part = cosine[:, None, :]
    sin_part = sine_table[:, None, :]
    return jnp.concatenate(
        [former * cos_part - latter * sin_part, latter * cos_part + former * sin_part], axis=-1
    )


def unrotate(vectors, cosine, sine_table):
    half_dim = vectors.shape[-1] // 2
    former = vectors[..., :half_dim]
    latter = vectors[..., half_dim:]
    cos_part = cosine[:, None, :]
    sin_part = sine_table[:, None, :]
    return jnp.concatenate(
        [former * cos_part + latter * sin_part, latter * cos_part - former * sin_part], axis=-1
    )


def _is_pow2(n):
    return n > 1 and (n & (n - 1)) == 0


def _xor_pairs(size, bit):
    return [(i, i ^ bit) for i in range(size)]


def _xor_reorder(stack, position, size):
    bit = 1
    while bit < size:
        swapped = stack[:, [m ^ bit for m in range(size)], :]
        stack = jnp.where((position & bit) != 0, swapped, stack)
        bit <<= 1
    return stack


def gather_features(shard, axis_name, size, position):
    if not _is_pow2(size):
        full = lax.all_gather(shard, axis_name, axis=1, tiled=True)
        return full.reshape(shard.shape[0], size, shard.shape[1])
    held = shard[:, None, :]
    masks = [0]
    bit = size >> 1
    while bit:
        incoming = lax.ppermute(held, axis_name, _xor_pairs(size, bit))
        held = jnp.concatenate([held, incoming], axis=1)
        masks = masks + [m ^ bit for m in masks]
        bit >>= 1
    held = held[:, [masks.index(m) for m in range(size)], :]
    return _xor_reorder(held, position, size)


def scatter_features(partial, axis_name, size, position):
    if not _is_pow2(size):
        summed = lax.psum_scatter(
            partial.astype(jnp.bfloat16), axis_name, scatter_dimension=1, tiled=True
        )
        return summed[:, 0, :].astype(jnp.float32)
    held = _xor_reorder(partial, position, size)
    masks = list(range(size))
    bit = 1
    while bit < size:
        keep = [i for i, m in enumerate(masks) if not m & bit]
        send = [i for i, m in enumerate(masks) if m & bit]
        outgoing = held[:, send, :].astype(jnp.bfloat16)
        incoming = lax.ppermute(outgoing, axis_name, _xor_pairs(size, bit))
        sent_masks = [masks[i] ^ bit for i in send]
        order = [sent_masks.index(masks[i]) for i in keep]
        held = held[:, keep, :] + incoming[:, order, :].astype(jnp.float32)
        masks = [masks[i] for i in keep]
        bit <<= 1
    return held[:, 0, :]


def sum_over(values, axis_name, size):
    if not _is_pow2(size):
        return lax.psum(values, axis_name)
    bit = 1
    while bit < size:
        values = values + lax.ppermute(values, axis_name, _xor_pairs(size, bit))
        bit <<= 1
    return values


def per_device(
    tokens,
    norm_gain,
    w_query,
    key_weight,
    value_weight,
    w_out,
    grad_output,
    doc_lengths,
    block_owner,
):
    token_row_count, width_part = tokens.shape
    full_width = norm_gain.shape[0]
    sources = lax.axis_size("dp")
    tensor_size = lax.axis_size("tensor")
    data_index = lax.axis_index("dp")
    tensor_index = lax.axis_index("tensor")
    query_width = w_query.shape[1]
    key_width = key_weight.shape[1]
    heads_local = query_width // HEAD_SIZE
    kv_local = key_width // HEAD_SIZE
    query_group_width = heads_local // kv_local
    scale_factor = 1.0 / math.sqrt(HEAD_SIZE)
    gain_part = lax.dynamic_slice_in_dim(norm_gain, tensor_index * width_part, width_part)
    x_float = tokens.astype(jnp.float32)

    block_count = block_owner.shape[1]
    owner_row = lax.dynamic_slice_in_dim(block_owner, data_index, 1, 0)[0]
    slot_index = jnp.arange(sources, dtype=jnp.int32)
    send_table = (owner_row[None, :] == slot_index[:, None]).astype(jnp.bfloat16)

    owned_blocks = grad_output.reshape(block_count, -1)
    arrived = lax.all_to_all(owned_blocks, "dp", split_axis=0, concat_axis=0, tiled=True)
    grad_home = (
        lax.dot_general(
            send_table, arrived, (((0,), (0,)), ((), ())), preferred_element_type=jnp.float32
        )
        .astype(jnp.bfloat16)
        .reshape(token_row_count, width_part)
    )

    gathered = gather_features(tokens, "tensor", tensor_size, tensor_index).reshape(
        token_row_count, full_width
    )
    gathered_float = gathered.astype(jnp.float32)
    inverse = lax.rsqrt(jnp.mean(gathered_float * gathered_float, axis=1) + NORM_EPSILON)
    normed_input = (gathered_float * inverse[:, None] * norm_gain[None, :]).astype(jnp.bfloat16)
    query_raw = jnp.dot(normed_input, w_query, preferred_element_type=jnp.float32)
    key_raw = jnp.dot(normed_input, key_weight, preferred_element_type=jnp.float32)
    value_raw = jnp.dot(normed_input, value_weight, preferred_element_type=jnp.float32)
    doc_ids, positions = doc_tables(doc_lengths[0], token_row_count)
    token_index = jnp.arange(token_row_count, dtype=jnp.int32)
    allowed = (doc_ids[:, None] == doc_ids[None, :]) & (
        token_index[None, :] <= token_index[:, None]
    )
    cosine, sine_table = rope_tables(positions, HEAD_SIZE)
    query_rows = rotate(
        query_raw.reshape(token_row_count, heads_local, HEAD_SIZE), cosine, sine_table
    ).astype(jnp.bfloat16)
    keys = rotate(
        key_raw.reshape(token_row_count, kv_local, HEAD_SIZE), cosine, sine_table
    ).astype(jnp.bfloat16)
    value_rows = value_raw.astype(jnp.bfloat16).reshape(token_row_count, kv_local, HEAD_SIZE)
    grouped_query = query_rows.reshape(token_row_count, kv_local, query_group_width, HEAD_SIZE)
    scores = (
        jnp.einsum("qkgd,skd->kgqs", grouped_query, keys, preferred_element_type=jnp.float32)
        * scale_factor
    )
    weights = jnp.where(allowed[None, None], jnp.exp(scores), 0.0)
    probs = weights / jnp.sum(weights, axis=-1, keepdims=True)
    probs_low = probs.astype(jnp.bfloat16)
    attended = jnp.einsum(
        "kgqs,skd->qkgd", probs_low, value_rows, preferred_element_type=jnp.float32
    ).astype(jnp.bfloat16)
    attended_flat = attended.reshape(token_row_count, query_width)
    mixed_partial = jnp.dot(attended_flat, w_out, preferred_element_type=jnp.float32).reshape(
        token_row_count, tensor_size, width_part
    )
    mixed = scatter_features(mixed_partial, "tensor", tensor_size, tensor_index)
    output_home = (x_float + mixed).astype(jnp.bfloat16)
    home_blocks = output_home.reshape(block_count, -1)
    outgoing = jnp.dot(send_table, home_blocks, preferred_element_type=jnp.float32).astype(
        jnp.bfloat16
    )
    relaid = lax.all_to_all(outgoing, "dp", split_axis=0, concat_axis=0, tiled=True).reshape(
        token_row_count, width_part
    )

    grad_full = gather_features(grad_home, "tensor", tensor_size, tensor_index).reshape(
        token_row_count, full_width
    )
    attended_gradient = lax.dot_general(
        grad_full,
        w_out,
        (((1,), (1,)), ((), ())),
        preferred_element_type=jnp.float32,
    ).astype(jnp.bfloat16)
    grouped_gradient = attended_gradient.reshape(
        token_row_count, kv_local, query_group_width, HEAD_SIZE
    )
    delta = jnp.sum(grouped_gradient.astype(jnp.float32) * attended.astype(jnp.float32), axis=-1)
    grad_probs = jnp.einsum(
        "qkgd,skd->kgqs", grouped_gradient, value_rows, preferred_element_type=jnp.float32
    )
    grad_scores = (probs * (grad_probs - jnp.transpose(delta, (1, 2, 0))[..., None])).astype(
        jnp.bfloat16
    )
    grad_query_rot = (
        jnp.einsum("kgqs,skd->qkgd", grad_scores, keys, preferred_element_type=jnp.float32)
        * scale_factor
    )
    grad_keys_rot = (
        jnp.einsum("kgqs,qkgd->skd", grad_scores, grouped_query, preferred_element_type=jnp.float32)
        * scale_factor
    )
    value_gradient = jnp.einsum(
        "kgqs,qkgd->skd", probs_low, grouped_gradient, preferred_element_type=jnp.float32
    )
    grad_query = unrotate(
        grad_query_rot.reshape(token_row_count, heads_local, HEAD_SIZE), cosine, sine_table
    ).astype(jnp.bfloat16)
    key_gradient = unrotate(grad_keys_rot, cosine, sine_table).astype(jnp.bfloat16)
    contract_out = (((1,), (1,)), ((), ()))
    normed_partial = (
        lax.dot_general(
            grad_query.reshape(token_row_count, query_width),
            w_query,
            contract_out,
            preferred_element_type=jnp.float32,
        )
        + lax.dot_general(
            key_gradient.reshape(token_row_count, key_width),
            key_weight,
            contract_out,
            preferred_element_type=jnp.float32,
        )
        + lax.dot_general(
            value_gradient.astype(jnp.bfloat16).reshape(token_row_count, key_width),
            value_weight,
            contract_out,
            preferred_element_type=jnp.float32,
        )
    )
    stat_partial = jnp.sum(normed_partial * norm_gain[None, :] * gathered_float, axis=1)
    stat = sum_over(stat_partial, "tensor", tensor_size) / full_width
    normed_gradient = scatter_features(
        normed_partial.reshape(token_row_count, tensor_size, width_part),
        "tensor",
        tensor_size,
        tensor_index,
    )
    cubed = inverse * inverse * inverse
    grad_x = (
        grad_home.astype(jnp.float32)
        + inverse[:, None] * gain_part[None, :] * normed_gradient
        - x_float * cubed[:, None] * stat[:, None]
    )
    return (relaid, grad_x.astype(jnp.bfloat16))


def solution(mesh):
    placed = (
        P("dp", "tensor"),
        P(),
        P(None, "tensor"),
        P(None, "tensor"),
        P(None, "tensor"),
        P("tensor", None),
        P("dp", "tensor"),
        P("dp", None),
        P(),
    )
    return jax.shard_map(
        per_device,
        mesh=mesh,
        in_specs=placed,
        out_specs=(P("dp", "tensor"), P("dp", "tensor")),
        check_vma=False,
    )
```

```python
import math

import jax
import jax.numpy as jnp
from jax import lax
from jax.sharding import PartitionSpec as P

HEAD_SIZE = 128


ROPE_BASE = 500000.0
NORM_EPSILON = 1e-05


def doc_tables(lengths_row, token_row_count):
    ends = jnp.cumsum(lengths_row)
    token_index = jnp.arange(token_row_count, dtype=jnp.int32)
    passed = (token_index[:, None] >= ends[None, :]).astype(jnp.int32)
    doc_ids = jnp.sum(passed, axis=1)
    starts = jnp.max(jnp.where(passed > 0, ends[None, :], 0), axis=1)
    return (doc_ids, token_index - starts)


def rope_tables(positions, head_size):
    half_dim = head_size // 2
    steps = jnp.arange(half_dim, dtype=jnp.float32)
    inverse_freq = jnp.power(ROPE_BASE, -2.0 * steps / head_size)
    angles = positions.astype(jnp.float32)[:, None] * inverse_freq[None, :]
    return (jnp.cos(angles), jnp.sin(angles))


def rotate(vectors, cosine, sine_table):
    half_dim = vectors.shape[-1] // 2
    former = vectors[..., :half_dim]
    latter = vectors[..., half_dim:]
    cos_part = cosine[:, None, :]
    sin_part = sine_table[:, None, :]
    return jnp.concatenate(
        [former * cos_part - latter * sin_part, latter * cos_part + former * sin_part], axis=-1
    )


def unrotate(vectors, cosine, sine_table):
    half_dim = vectors.shape[-1] // 2
    former = vectors[..., :half_dim]
    latter = vectors[..., half_dim:]
    cos_part = cosine[:, None, :]
    sin_part = sine_table[:, None, :]
    return jnp.concatenate(
        [former * cos_part + latter * sin_part, latter * cos_part - former * sin_part], axis=-1
    )


def _is_pow2(n):
    return n > 1 and (n & (n - 1)) == 0


def _xor_pairs(size, bit):
    return [(i, i ^ bit) for i in range(size)]


def gather_features(shard, axis_name, size, position):
    if not _is_pow2(size):
        return lax.all_gather(shard, axis_name, axis=1, tiled=True)
    held = shard[None]
    masks = [0]
    bit = size >> 1
    while bit:
        incoming = lax.ppermute(held, axis_name, _xor_pairs(size, bit))
        held = jnp.concatenate([held, incoming], axis=0)
        masks = masks + [m ^ bit for m in masks]
        bit >>= 1
    table = jnp.asarray([masks.index(m) for m in range(size)], jnp.int32)
    blocks = [
        lax.dynamic_index_in_dim(held, table[s ^ position], axis=0, keepdims=False)
        for s in range(size)
    ]
    return jnp.concatenate(blocks, axis=1)


def scatter_features(partial, axis_name, size, position):
    width = partial.shape[1] // size
    if not _is_pow2(size):
        summed = lax.psum_scatter(
            partial.astype(jnp.bfloat16), axis_name, scatter_dimension=1, tiled=True
        )
        return summed.astype(jnp.float32)
    held = [
        lax.dynamic_slice_in_dim(partial, (position ^ m) * width, width, axis=1)
        for m in range(size)
    ]
    masks = list(range(size))
    bit = 1
    while bit < size:
        keep = [i for i, m in enumerate(masks) if not m & bit]
        send = [i for i, m in enumerate(masks) if m & bit]
        outgoing = jnp.stack([held[i] for i in send]).astype(jnp.bfloat16)
        incoming = lax.ppermute(outgoing, axis_name, _xor_pairs(size, bit))
        sent_masks = [masks[i] ^ bit for i in send]
        held = [
            held[i] + incoming[sent_masks.index(masks[i])].astype(jnp.float32) for i in keep
        ]
        masks = [masks[i] for i in keep]
        bit <<= 1
    return held[0]


def sum_over(values, axis_name, size):
    if not _is_pow2(size):
        return lax.psum(values, axis_name)
    bit = 1
    while bit < size:
        values = values + lax.ppermute(values, axis_name, _xor_pairs(size, bit))
        bit <<= 1
    return values


def per_device(
    tokens,
    norm_gain,
    w_query,
    key_weight,
    value_weight,
    w_out,
    grad_output,
    doc_lengths,
    block_owner,
):
    token_row_count, width_part = tokens.shape
    full_width = norm_gain.shape[0]
    sources = lax.axis_size("dp")
    tensor_size = lax.axis_size("tensor")
    data_index = lax.axis_index("dp")
    tensor_index = lax.axis_index("tensor")
    query_width = w_query.shape[1]
    key_width = key_weight.shape[1]
    heads_local = query_width // HEAD_SIZE
    kv_local = key_width // HEAD_SIZE
    query_group_width = heads_local // kv_local
    scale_factor = 1.0 / math.sqrt(HEAD_SIZE)
    gain_part = lax.dynamic_slice_in_dim(norm_gain, tensor_index * width_part, width_part)
    x_float = tokens.astype(jnp.float32)

    block_count = block_owner.shape[1]
    owner_row = lax.dynamic_slice_in_dim(block_owner, data_index, 1, 0)[0]
    slot_index = jnp.arange(sources, dtype=jnp.int32)
    send_table = (owner_row[None, :] == slot_index[:, None]).astype(jnp.bfloat16)

    owned_blocks = grad_output.reshape(block_count, -1)
    arrived = lax.all_to_all(owned_blocks, "dp", split_axis=0, concat_axis=0, tiled=True)
    grad_home = (
        lax.dot_general(
            send_table, arrived, (((0,), (0,)), ((), ())), preferred_element_type=jnp.float32
        )
        .astype(jnp.bfloat16)
        .reshape(token_row_count, width_part)
    )

    gathered = gather_features(tokens, "tensor", tensor_size, tensor_index)
    gathered_float = gathered.astype(jnp.float32)
    inverse = lax.rsqrt(jnp.mean(gathered_float * gathered_float, axis=1) + NORM_EPSILON)
    normed_input = (gathered_float * inverse[:, None] * norm_gain[None, :]).astype(jnp.bfloat16)
    query_raw = jnp.dot(normed_input, w_query, preferred_element_type=jnp.float32)
    key_raw = jnp.dot(normed_input, key_weight, preferred_element_type=jnp.float32)
    value_raw = jnp.dot(normed_input, value_weight, preferred_element_type=jnp.float32)
    doc_ids, positions = doc_tables(doc_lengths[0], token_row_count)
    token_index = jnp.arange(token_row_count, dtype=jnp.int32)
    allowed = (doc_ids[:, None] == doc_ids[None, :]) & (
        token_index[None, :] <= token_index[:, None]
    )
    cosine, sine_table = rope_tables(positions, HEAD_SIZE)
    query_rows = rotate(
        query_raw.reshape(token_row_count, heads_local, HEAD_SIZE), cosine, sine_table
    ).astype(jnp.bfloat16)
    keys = rotate(
        key_raw.reshape(token_row_count, kv_local, HEAD_SIZE), cosine, sine_table
    ).astype(jnp.bfloat16)
    value_rows = value_raw.astype(jnp.bfloat16).reshape(token_row_count, kv_local, HEAD_SIZE)
    grouped_query = query_rows.reshape(token_row_count, kv_local, query_group_width, HEAD_SIZE)
    scores = (
        jnp.einsum("qkgd,skd->kgqs", grouped_query, keys, preferred_element_type=jnp.float32)
        * scale_factor
    )
    weights = jnp.where(allowed[None, None], jnp.exp(scores), 0.0)
    probs = weights / jnp.sum(weights, axis=-1, keepdims=True)
    probs_low = probs.astype(jnp.bfloat16)
    attended = jnp.einsum(
        "kgqs,skd->qkgd", probs_low, value_rows, preferred_element_type=jnp.float32
    ).astype(jnp.bfloat16)
    attended_flat = attended.reshape(token_row_count, query_width)
    mixed_partial = jnp.dot(attended_flat, w_out, preferred_element_type=jnp.float32)
    mixed = scatter_features(mixed_partial, "tensor", tensor_size, tensor_index)
    output_home = (x_float + mixed).astype(jnp.bfloat16)
    home_blocks = output_home.reshape(block_count, -1)
    outgoing = jnp.dot(send_table, home_blocks, preferred_element_type=jnp.float32).astype(
        jnp.bfloat16
    )
    relaid = lax.all_to_all(outgoing, "dp", split_axis=0, concat_axis=0, tiled=True).reshape(
        token_row_count, width_part
    )

    grad_full = gather_features(grad_home, "tensor", tensor_size, tensor_index)
    attended_gradient = lax.dot_general(
        grad_full,
        w_out,
        (((1,), (1,)), ((), ())),
        preferred_element_type=jnp.float32,
    ).astype(jnp.bfloat16)
    grouped_gradient = attended_gradient.reshape(
        token_row_count, kv_local, query_group_width, HEAD_SIZE
    )
    delta = jnp.sum(grouped_gradient.astype(jnp.float32) * attended.astype(jnp.float32), axis=-1)
    grad_probs = jnp.einsum(
        "qkgd,skd->kgqs", grouped_gradient, value_rows, preferred_element_type=jnp.float32
    )
    grad_scores = (probs * (grad_probs - jnp.transpose(delta, (1, 2, 0))[..., None])).astype(
        jnp.bfloat16
    )
    grad_query_rot = (
        jnp.einsum("kgqs,skd->qkgd", grad_scores, keys, preferred_element_type=jnp.float32)
        * scale_factor
    )
    grad_keys_rot = (
        jnp.einsum("kgqs,qkgd->skd", grad_scores, grouped_query, preferred_element_type=jnp.float32)
        * scale_factor
    )
    value_gradient = jnp.einsum(
        "kgqs,qkgd->skd", probs_low, grouped_gradient, preferred_element_type=jnp.float32
    )
    grad_query = unrotate(
        grad_query_rot.reshape(token_row_count, heads_local, HEAD_SIZE), cosine, sine_table
    ).astype(jnp.bfloat16)
    key_gradient = unrotate(grad_keys_rot, cosine, sine_table).astype(jnp.bfloat16)
    contract_out = (((1,), (1,)), ((), ()))
    normed_partial = (
        lax.dot_general(
            grad_query.reshape(token_row_count, query_width),
            w_query,
            contract_out,
            preferred_element_type=jnp.float32,
        )
        + lax.dot_general(
            key_gradient.reshape(token_row_count, key_width),
            key_weight,
            contract_out,
            preferred_element_type=jnp.float32,
        )
        + lax.dot_general(
            value_gradient.astype(jnp.bfloat16).reshape(token_row_count, key_width),
            value_weight,
            contract_out,
            preferred_element_type=jnp.float32,
        )
    )
    stat_partial = jnp.sum(normed_partial * norm_gain[None, :] * gathered_float, axis=1)
    stat = sum_over(stat_partial, "tensor", tensor_size) / full_width
    normed_gradient = scatter_features(
        normed_partial,
        "tensor",
        tensor_size,
        tensor_index,
    )
    cubed = inverse * inverse * inverse
    grad_x = (
        grad_home.astype(jnp.float32)
        + inverse[:, None] * gain_part[None, :] * normed_gradient
        - x_float * cubed[:, None] * stat[:, None]
    )
    return (relaid, grad_x.astype(jnp.bfloat16))


def solution(mesh):
    placed = (
        P("dp", "tensor"),
        P(),
        P(None, "tensor"),
        P(None, "tensor"),
        P(None, "tensor"),
        P("tensor", None),
        P("dp", "tensor"),
        P("dp", None),
        P(),
    )
    return jax.shard_map(
        per_device,
        mesh=mesh,
        in_specs=placed,
        out_specs=(P("dp", "tensor"), P("dp", "tensor")),
        check_vma=False,
    )
```

```python
import math

import jax
import jax.numpy as jnp
from jax import lax
from jax.sharding import PartitionSpec as P

HEAD_SIZE = 128


ROPE_BASE = 500000.0
NORM_EPSILON = 1e-05


def doc_tables(lengths_row, token_row_count):
    ends = jnp.cumsum(lengths_row)
    token_index = jnp.arange(token_row_count, dtype=jnp.int32)
    passed = (token_index[:, None] >= ends[None, :]).astype(jnp.int32)
    doc_ids = jnp.sum(passed, axis=1)
    starts = jnp.max(jnp.where(passed > 0, ends[None, :], 0), axis=1)
    return (doc_ids, token_index - starts)


def rope_tables(positions, head_size):
    half_dim = head_size // 2
    steps = jnp.arange(half_dim, dtype=jnp.float32)
    inverse_freq = jnp.power(ROPE_BASE, -2.0 * steps / head_size)
    angles = positions.astype(jnp.float32)[:, None] * inverse_freq[None, :]
    return (jnp.cos(angles), jnp.sin(angles))


def rotate(vectors, cosine, sine_table):
    half_dim = vectors.shape[-1] // 2
    former = vectors[..., :half_dim]
    latter = vectors[..., half_dim:]
    cos_part = cosine[:, None, :]
    sin_part = sine_table[:, None, :]
    return jnp.concatenate(
        [former * cos_part - latter * sin_part, latter * cos_part + former * sin_part], axis=-1
    )


def unrotate(vectors, cosine, sine_table):
    half_dim = vectors.shape[-1] // 2
    former = vectors[..., :half_dim]
    latter = vectors[..., half_dim:]
    cos_part = cosine[:, None, :]
    sin_part = sine_table[:, None, :]
    return jnp.concatenate(
        [former * cos_part + latter * sin_part, latter * cos_part - former * sin_part], axis=-1
    )


def _is_pow2(n):
    return n > 1 and (n & (n - 1)) == 0


def _xor_pairs(size, bit):
    return [(i, i ^ bit) for i in range(size)]


def gather_features(shard, axis_name, size, position):
    if not _is_pow2(size):
        return lax.all_gather(shard, axis_name, axis=1, tiled=True)
    held = shard[None]
    masks = [0]
    bit = size >> 1
    while bit:
        incoming = lax.ppermute(held, axis_name, _xor_pairs(size, bit))
        held = jnp.concatenate([held, incoming], axis=0)
        masks = masks + [m ^ bit for m in masks]
        bit >>= 1
    table = jnp.asarray([masks.index(m) for m in range(size)], jnp.int32)
    blocks = [
        lax.dynamic_index_in_dim(held, table[s ^ position], axis=0, keepdims=False)
        for s in range(size)
    ]
    return jnp.concatenate(blocks, axis=1)


def scatter_features(partial, axis_name, size, position):
    width = partial.shape[1] // size
    if not _is_pow2(size):
        summed = lax.psum_scatter(
            partial.astype(jnp.bfloat16), axis_name, scatter_dimension=1, tiled=True
        )
        return summed.astype(jnp.float32)
    held = [
        lax.dynamic_slice_in_dim(partial, (position ^ m) * width, width, axis=1)
        for m in range(size)
    ]
    masks = list(range(size))
    bit = 1
    while bit < size:
        keep = [i for i, m in enumerate(masks) if not m & bit]
        send = [i for i, m in enumerate(masks) if m & bit]
        outgoing = jnp.stack([held[i] for i in send]).astype(jnp.bfloat16)
        incoming = lax.ppermute(outgoing, axis_name, _xor_pairs(size, bit))
        sent_masks = [masks[i] ^ bit for i in send]
        held = [
            held[i] + incoming[sent_masks.index(masks[i])].astype(jnp.float32) for i in keep
        ]
        masks = [masks[i] for i in keep]
        bit <<= 1
    return held[0]


def sum_over(values, axis_name, size):
    if not _is_pow2(size):
        return lax.psum(values, axis_name)
    bit = 1
    while bit < size:
        values = values + lax.ppermute(values, axis_name, _xor_pairs(size, bit))
        bit <<= 1
    return values


def per_device(
    tokens,
    norm_gain,
    w_query,
    key_weight,
    value_weight,
    w_out,
    grad_output,
    doc_lengths,
    block_owner,
):
    token_row_count, width_part = tokens.shape
    full_width = norm_gain.shape[0]
    sources = lax.axis_size("dp")
    tensor_size = lax.axis_size("tensor")
    data_index = lax.axis_index("dp")
    tensor_index = lax.axis_index("tensor")
    query_width = w_query.shape[1]
    key_width = key_weight.shape[1]
    heads_local = query_width // HEAD_SIZE
    kv_local = key_width // HEAD_SIZE
    query_group_width = heads_local // kv_local
    scale_factor = 1.0 / math.sqrt(HEAD_SIZE)
    gain_part = lax.dynamic_slice_in_dim(norm_gain, tensor_index * width_part, width_part)
    x_float = tokens.astype(jnp.float32)

    block_count = block_owner.shape[1]
    owner_row = lax.dynamic_slice_in_dim(block_owner, data_index, 1, 0)[0]
    slot_index = jnp.arange(sources, dtype=jnp.int32)
    send_table = (owner_row[None, :] == slot_index[:, None]).astype(jnp.bfloat16)

    home_rows = token_row_count // block_count
    owned_blocks = grad_output.reshape(block_count, home_rows, width_part)
    if sources <= 16:
        returned = [lax.dynamic_index_in_dim(owned_blocks, data_index, 0, keepdims=False)]
        for shift in range(1, sources):
            pairs = [(a, (a + shift) % sources) for a in range(sources)]
            piece = lax.dynamic_index_in_dim(
                owned_blocks, (data_index + shift) % sources, 0, keepdims=False
            )
            returned.append(lax.ppermute(piece, "dp", pairs))
        returned = jnp.stack(returned)
        grad_home = jnp.concatenate(
            [
                lax.dynamic_index_in_dim(
                    returned, (data_index - owner_row[j]) % sources, 0, keepdims=False
                )
                for j in range(block_count)
            ],
            axis=0,
        )
    else:
        arrived = lax.all_to_all(
            owned_blocks.reshape(block_count, -1), "dp", split_axis=0, concat_axis=0, tiled=True
        )
        grad_home = (
            lax.dot_general(
                send_table, arrived, (((0,), (0,)), ((), ())), preferred_element_type=jnp.float32
            )
            .astype(jnp.bfloat16)
            .reshape(token_row_count, width_part)
        )

    gathered = gather_features(tokens, "tensor", tensor_size, tensor_index)
    gathered_float = gathered.astype(jnp.float32)
    inverse = lax.rsqrt(jnp.mean(gathered_float * gathered_float, axis=1) + NORM_EPSILON)
    normed_input = (gathered_float * inverse[:, None] * norm_gain[None, :]).astype(jnp.bfloat16)
    query_raw = jnp.dot(normed_input, w_query, preferred_element_type=jnp.float32)
    key_raw = jnp.dot(normed_input, key_weight, preferred_element_type=jnp.float32)
    value_raw = jnp.dot(normed_input, value_weight, preferred_element_type=jnp.float32)
    doc_ids, positions = doc_tables(doc_lengths[0], token_row_count)
    token_index = jnp.arange(token_row_count, dtype=jnp.int32)
    allowed = (doc_ids[:, None] == doc_ids[None, :]) & (
        token_index[None, :] <= token_index[:, None]
    )
    cosine, sine_table = rope_tables(positions, HEAD_SIZE)
    query_rows = rotate(
        query_raw.reshape(token_row_count, heads_local, HEAD_SIZE), cosine, sine_table
    ).astype(jnp.bfloat16)
    keys = rotate(
        key_raw.reshape(token_row_count, kv_local, HEAD_SIZE), cosine, sine_table
    ).astype(jnp.bfloat16)
    value_rows = value_raw.astype(jnp.bfloat16).reshape(token_row_count, kv_local, HEAD_SIZE)
    grouped_query = query_rows.reshape(token_row_count, kv_local, query_group_width, HEAD_SIZE)
    scores = (
        jnp.einsum("qkgd,skd->kgqs", grouped_query, keys, preferred_element_type=jnp.float32)
        * scale_factor
    )
    weights = jnp.where(allowed[None, None], jnp.exp(scores), 0.0)
    probs = weights / jnp.sum(weights, axis=-1, keepdims=True)
    probs_low = probs.astype(jnp.bfloat16)
    attended = jnp.einsum(
        "kgqs,skd->qkgd", probs_low, value_rows, preferred_element_type=jnp.float32
    ).astype(jnp.bfloat16)
    attended_flat = attended.reshape(token_row_count, query_width)
    mixed_partial = jnp.dot(attended_flat, w_out, preferred_element_type=jnp.float32)
    mixed = scatter_features(mixed_partial, "tensor", tensor_size, tensor_index)
    output_home = (x_float + mixed).astype(jnp.bfloat16)
    home_blocks = output_home.reshape(block_count, home_rows, width_part)
    if sources <= 16:
        block_for = jnp.sum(
            jnp.where(send_table > 0, jnp.arange(block_count, dtype=jnp.int32)[None, :], 0), axis=1
        )
        landed = [
            lax.dynamic_index_in_dim(home_blocks, block_for[data_index], 0, keepdims=False)
        ]
        for shift in range(1, sources):
            pairs = [(a, (a + shift) % sources) for a in range(sources)]
            piece = lax.dynamic_index_in_dim(
                home_blocks, block_for[(data_index + shift) % sources], 0, keepdims=False
            )
            landed.append(lax.ppermute(piece, "dp", pairs))
        landed = jnp.stack(landed)
        relaid = jnp.concatenate(
            [
                lax.dynamic_index_in_dim(
                    landed, (data_index - b) % sources, 0, keepdims=False
                )
                for b in range(sources)
            ],
            axis=0,
        )
    else:
        outgoing = jnp.dot(
            send_table, home_blocks.reshape(block_count, -1), preferred_element_type=jnp.float32
        ).astype(jnp.bfloat16)
        relaid = lax.all_to_all(outgoing, "dp", split_axis=0, concat_axis=0, tiled=True).reshape(
            token_row_count, width_part
        )

    grad_full = gather_features(grad_home, "tensor", tensor_size, tensor_index)
    attended_gradient = lax.dot_general(
        grad_full,
        w_out,
        (((1,), (1,)), ((), ())),
        preferred_element_type=jnp.float32,
    ).astype(jnp.bfloat16)
    grouped_gradient = attended_gradient.reshape(
        token_row_count, kv_local, query_group_width, HEAD_SIZE
    )
    delta = jnp.sum(grouped_gradient.astype(jnp.float32) * attended.astype(jnp.float32), axis=-1)
    grad_probs = jnp.einsum(
        "qkgd,skd->kgqs", grouped_gradient, value_rows, preferred_element_type=jnp.float32
    )
    grad_scores = (probs * (grad_probs - jnp.transpose(delta, (1, 2, 0))[..., None])).astype(
        jnp.bfloat16
    )
    grad_query_rot = (
        jnp.einsum("kgqs,skd->qkgd", grad_scores, keys, preferred_element_type=jnp.float32)
        * scale_factor
    )
    grad_keys_rot = (
        jnp.einsum("kgqs,qkgd->skd", grad_scores, grouped_query, preferred_element_type=jnp.float32)
        * scale_factor
    )
    value_gradient = jnp.einsum(
        "kgqs,qkgd->skd", probs_low, grouped_gradient, preferred_element_type=jnp.float32
    )
    grad_query = unrotate(
        grad_query_rot.reshape(token_row_count, heads_local, HEAD_SIZE), cosine, sine_table
    ).astype(jnp.bfloat16)
    key_gradient = unrotate(grad_keys_rot, cosine, sine_table).astype(jnp.bfloat16)
    contract_out = (((1,), (1,)), ((), ()))
    normed_partial = (
        lax.dot_general(
            grad_query.reshape(token_row_count, query_width),
            w_query,
            contract_out,
            preferred_element_type=jnp.float32,
        )
        + lax.dot_general(
            key_gradient.reshape(token_row_count, key_width),
            key_weight,
            contract_out,
            preferred_element_type=jnp.float32,
        )
        + lax.dot_general(
            value_gradient.astype(jnp.bfloat16).reshape(token_row_count, key_width),
            value_weight,
            contract_out,
            preferred_element_type=jnp.float32,
        )
    )
    stat_partial = jnp.sum(normed_partial * norm_gain[None, :] * gathered_float, axis=1)
    stat = sum_over(stat_partial, "tensor", tensor_size) / full_width
    normed_gradient = scatter_features(
        normed_partial,
        "tensor",
        tensor_size,
        tensor_index,
    )
    cubed = inverse * inverse * inverse
    grad_x = (
        grad_home.astype(jnp.float32)
        + inverse[:, None] * gain_part[None, :] * normed_gradient
        - x_float * cubed[:, None] * stat[:, None]
    )
    return (relaid, grad_x.astype(jnp.bfloat16))


def solution(mesh):
    placed = (
        P("dp", "tensor"),
        P(),
        P(None, "tensor"),
        P(None, "tensor"),
        P(None, "tensor"),
        P("tensor", None),
        P("dp", "tensor"),
        P("dp", None),
        P(),
    )
    return jax.shard_map(
        per_device,
        mesh=mesh,
        in_specs=placed,
        out_specs=(P("dp", "tensor"), P("dp", "tensor")),
        check_vma=False,
    )
```

```python
import math

import jax
import jax.numpy as jnp
from jax import lax
from jax.sharding import PartitionSpec as P

HEAD_SIZE = 128


ROPE_BASE = 500000.0
NORM_EPSILON = 1e-05


def doc_tables(lengths_row, token_row_count):
    ends = jnp.cumsum(lengths_row)
    token_index = jnp.arange(token_row_count, dtype=jnp.int32)
    passed = (token_index[:, None] >= ends[None, :]).astype(jnp.int32)
    doc_ids = jnp.sum(passed, axis=1)
    starts = jnp.max(jnp.where(passed > 0, ends[None, :], 0), axis=1)
    return (doc_ids, token_index - starts)


def rope_tables(positions, head_size):
    half_dim = head_size // 2
    steps = jnp.arange(half_dim, dtype=jnp.float32)
    inverse_freq = jnp.power(ROPE_BASE, -2.0 * steps / head_size)
    angles = positions.astype(jnp.float32)[:, None] * inverse_freq[None, :]
    return (jnp.cos(angles), jnp.sin(angles))


def rotate(vectors, cosine, sine_table):
    half_dim = vectors.shape[-1] // 2
    former = vectors[..., :half_dim]
    latter = vectors[..., half_dim:]
    cos_part = cosine[:, None, :]
    sin_part = sine_table[:, None, :]
    return jnp.concatenate(
        [former * cos_part - latter * sin_part, latter * cos_part + former * sin_part], axis=-1
    )


def unrotate(vectors, cosine, sine_table):
    half_dim = vectors.shape[-1] // 2
    former = vectors[..., :half_dim]
    latter = vectors[..., half_dim:]
    cos_part = cosine[:, None, :]
    sin_part = sine_table[:, None, :]
    return jnp.concatenate(
        [former * cos_part + latter * sin_part, latter * cos_part - former * sin_part], axis=-1
    )


def _is_pow2(n):
    return n > 1 and (n & (n - 1)) == 0


def _xor_pairs(size, bit):
    return [(i, i ^ bit) for i in range(size)]


def gather_features(shard, axis_name, size, position, tied=None):
    if not _is_pow2(size):
        return lax.all_gather(shard, axis_name, axis=1, tiled=True), tied
    held = shard[None]
    masks = [0]
    bit = size >> 1
    while bit:
        incoming = lax.ppermute(held, axis_name, _xor_pairs(size, bit))
        if tied is not None:
            incoming, tied = lax.optimization_barrier((incoming, tied))
        held = jnp.concatenate([held, incoming], axis=0)
        masks = masks + [m ^ bit for m in masks]
        bit >>= 1
    table = jnp.asarray([masks.index(m) for m in range(size)], jnp.int32)
    blocks = [
        lax.dynamic_index_in_dim(held, table[s ^ position], axis=0, keepdims=False)
        for s in range(size)
    ]
    return jnp.concatenate(blocks, axis=1), tied


def scatter_features(partial, axis_name, size, position, extra=None):
    width = partial.shape[1] // size
    if not _is_pow2(size):
        summed = lax.psum_scatter(
            partial.astype(jnp.bfloat16), axis_name, scatter_dimension=1, tiled=True
        )
        if extra is not None:
            extra = lax.psum(extra, axis_name)
        return summed.astype(jnp.float32), extra
    held = [
        lax.dynamic_slice_in_dim(partial, (position ^ m) * width, width, axis=1)
        for m in range(size)
    ]
    masks = list(range(size))
    bit = 1
    while bit < size:
        keep = [i for i, m in enumerate(masks) if not m & bit]
        send = [i for i, m in enumerate(masks) if m & bit]
        outgoing = jnp.stack([held[i] for i in send]).astype(jnp.bfloat16)
        if extra is None:
            incoming = lax.ppermute(outgoing, axis_name, _xor_pairs(size, bit))
        else:
            incoming, extra_in = lax.ppermute((outgoing, extra), axis_name, _xor_pairs(size, bit))
            extra = extra + extra_in
        sent_masks = [masks[i] ^ bit for i in send]
        held = [
            held[i] + incoming[sent_masks.index(masks[i])].astype(jnp.float32) for i in keep
        ]
        masks = [masks[i] for i in keep]
        bit <<= 1
    return held[0], extra


def relay_blocks(blocks, select, place, axis_name, size):
    held = jnp.einsum(
        "mn,nrw->mrw", select, blocks, preferred_element_type=jnp.float32
    ).astype(blocks.dtype)
    items = [held[m] for m in range(size)]
    dst = list(range(size))
    src = [0] * size
    bit = 1
    while bit < size:
        send = [k for k in range(len(items)) if dst[k] & bit]
        keep = [k for k in range(len(items)) if not dst[k] & bit]
        incoming = lax.ppermute(
            jnp.stack([items[k] for k in send]), axis_name, _xor_pairs(size, bit)
        )
        items = [items[k] for k in keep] + [incoming[n] for n in range(len(send))]
        dst, src = (
            [dst[k] for k in keep] + [dst[k] ^ bit for k in send],
            [src[k] for k in keep] + [src[k] ^ bit for k in send],
        )
        bit <<= 1
    arrived = jnp.stack(items)
    ordered = jnp.einsum("bk,krw->brw", place(src), arrived, preferred_element_type=jnp.float32)
    return ordered.astype(blocks.dtype)


def per_device(
    tokens,
    norm_gain,
    w_query,
    key_weight,
    value_weight,
    w_out,
    grad_output,
    doc_lengths,
    block_owner,
):
    token_row_count, width_part = tokens.shape
    full_width = norm_gain.shape[0]
    sources = lax.axis_size("dp")
    tensor_size = lax.axis_size("tensor")
    data_index = lax.axis_index("dp")
    tensor_index = lax.axis_index("tensor")
    query_width = w_query.shape[1]
    key_width = key_weight.shape[1]
    heads_local = query_width // HEAD_SIZE
    kv_local = key_width // HEAD_SIZE
    query_group_width = heads_local // kv_local
    scale_factor = 1.0 / math.sqrt(HEAD_SIZE)
    gain_part = lax.dynamic_slice_in_dim(norm_gain, tensor_index * width_part, width_part)
    x_float = tokens.astype(jnp.float32)

    block_count = block_owner.shape[1]
    owner_row = lax.dynamic_slice_in_dim(block_owner, data_index, 1, 0)[0]
    slot_index = jnp.arange(sources, dtype=jnp.int32)
    send_table = (owner_row[None, :] == slot_index[:, None]).astype(jnp.bfloat16)

    home_rows = token_row_count // block_count
    gathered, grad_output = gather_features(
        tokens, "tensor", tensor_size, tensor_index, tied=grad_output
    )
    owned_blocks = grad_output.reshape(block_count, home_rows, width_part)
    if _is_pow2(sources) and sources <= 16 and block_count == sources:
        mask_index = jnp.arange(sources, dtype=jnp.int32)
        pick_home = (
            (mask_index[:, None] ^ data_index) == jnp.arange(block_count)[None, :]
        ).astype(jnp.bfloat16)

        def home_order(source_masks):
            masks = jnp.asarray(source_masks, jnp.int32)
            return ((owner_row[:, None] ^ data_index) == masks[None, :]).astype(jnp.bfloat16)

        grad_home = relay_blocks(owned_blocks, pick_home, home_order, "dp", sources).reshape(
            token_row_count, width_part
        )
    else:
        arrived = lax.all_to_all(
            owned_blocks.reshape(block_count, -1), "dp", split_axis=0, concat_axis=0, tiled=True
        )
        grad_home = (
            lax.dot_general(
                send_table, arrived, (((0,), (0,)), ((), ())), preferred_element_type=jnp.float32
            )
            .astype(jnp.bfloat16)
            .reshape(token_row_count, width_part)
        )

    gathered_float = gathered.astype(jnp.float32)
    inverse = lax.rsqrt(jnp.mean(gathered_float * gathered_float, axis=1) + NORM_EPSILON)
    normed_input = (gathered_float * inverse[:, None] * norm_gain[None, :]).astype(jnp.bfloat16)
    query_raw = jnp.dot(normed_input, w_query, preferred_element_type=jnp.float32)
    key_raw = jnp.dot(normed_input, key_weight, preferred_element_type=jnp.float32)
    value_raw = jnp.dot(normed_input, value_weight, preferred_element_type=jnp.float32)
    doc_ids, positions = doc_tables(doc_lengths[0], token_row_count)
    token_index = jnp.arange(token_row_count, dtype=jnp.int32)
    allowed = (doc_ids[:, None] == doc_ids[None, :]) & (
        token_index[None, :] <= token_index[:, None]
    )
    cosine, sine_table = rope_tables(positions, HEAD_SIZE)
    query_rows = rotate(
        query_raw.reshape(token_row_count, heads_local, HEAD_SIZE), cosine, sine_table
    ).astype(jnp.bfloat16)
    keys = rotate(
        key_raw.reshape(token_row_count, kv_local, HEAD_SIZE), cosine, sine_table
    ).astype(jnp.bfloat16)
    value_rows = value_raw.astype(jnp.bfloat16).reshape(token_row_count, kv_local, HEAD_SIZE)
    grouped_query = query_rows.reshape(token_row_count, kv_local, query_group_width, HEAD_SIZE)
    scores = (
        jnp.einsum("qkgd,skd->kgqs", grouped_query, keys, preferred_element_type=jnp.float32)
        * scale_factor
    )
    weights = jnp.where(allowed[None, None], jnp.exp(scores), 0.0)
    probs = weights / jnp.sum(weights, axis=-1, keepdims=True)
    probs_low = probs.astype(jnp.bfloat16)
    attended = jnp.einsum(
        "kgqs,skd->qkgd", probs_low, value_rows, preferred_element_type=jnp.float32
    ).astype(jnp.bfloat16)
    attended_flat = attended.reshape(token_row_count, query_width)
    mixed_partial = jnp.dot(attended_flat, w_out, preferred_element_type=jnp.float32)
    mixed, _ = scatter_features(mixed_partial, "tensor", tensor_size, tensor_index)
    output_home = (x_float + mixed).astype(jnp.bfloat16)
    home_blocks = output_home.reshape(block_count, home_rows, width_part)
    if _is_pow2(sources) and sources <= 16 and block_count == sources:
        mask_index = jnp.arange(sources, dtype=jnp.int32)
        pick_owner = (owner_row[None, :] == (mask_index[:, None] ^ data_index)).astype(
            jnp.bfloat16
        )

        def owner_order(source_masks):
            masks = jnp.asarray(source_masks, jnp.int32)
            return ((mask_index[:, None] ^ data_index) == masks[None, :]).astype(jnp.bfloat16)

        relaid = relay_blocks(home_blocks, pick_owner, owner_order, "dp", sources).reshape(
            token_row_count, width_part
        )
    else:
        outgoing = jnp.dot(
            send_table, home_blocks.reshape(block_count, -1), preferred_element_type=jnp.float32
        ).astype(jnp.bfloat16)
        relaid = lax.all_to_all(outgoing, "dp", split_axis=0, concat_axis=0, tiled=True).reshape(
            token_row_count, width_part
        )

    grad_full, _ = gather_features(grad_home, "tensor", tensor_size, tensor_index)
    attended_gradient = lax.dot_general(
        grad_full,
        w_out,
        (((1,), (1,)), ((), ())),
        preferred_element_type=jnp.float32,
    ).astype(jnp.bfloat16)
    grouped_gradient = attended_gradient.reshape(
        token_row_count, kv_local, query_group_width, HEAD_SIZE
    )
    delta = jnp.sum(grouped_gradient.astype(jnp.float32) * attended.astype(jnp.float32), axis=-1)
    grad_probs = jnp.einsum(
        "qkgd,skd->kgqs", grouped_gradient, value_rows, preferred_element_type=jnp.float32
    )
    grad_scores = (probs * (grad_probs - jnp.transpose(delta, (1, 2, 0))[..., None])).astype(
        jnp.bfloat16
    )
    grad_query_rot = (
        jnp.einsum("kgqs,skd->qkgd", grad_scores, keys, preferred_element_type=jnp.float32)
        * scale_factor
    )
    grad_keys_rot = (
        jnp.einsum("kgqs,qkgd->skd", grad_scores, grouped_query, preferred_element_type=jnp.float32)
        * scale_factor
    )
    value_gradient = jnp.einsum(
        "kgqs,qkgd->skd", probs_low, grouped_gradient, preferred_element_type=jnp.float32
    )
    grad_query = unrotate(
        grad_query_rot.reshape(token_row_count, heads_local, HEAD_SIZE), cosine, sine_table
    ).astype(jnp.bfloat16)
    key_gradient = unrotate(grad_keys_rot, cosine, sine_table).astype(jnp.bfloat16)
    contract_out = (((1,), (1,)), ((), ()))
    normed_partial = (
        lax.dot_general(
            grad_query.reshape(token_row_count, query_width),
            w_query,
            contract_out,
            preferred_element_type=jnp.float32,
        )
        + lax.dot_general(
            key_gradient.reshape(token_row_count, key_width),
            key_weight,
            contract_out,
            preferred_element_type=jnp.float32,
        )
        + lax.dot_general(
            value_gradient.astype(jnp.bfloat16).reshape(token_row_count, key_width),
            value_weight,
            contract_out,
            preferred_element_type=jnp.float32,
        )
    )
    stat_partial = jnp.sum(normed_partial * norm_gain[None, :] * gathered_float, axis=1)
    relaid, normed_partial = lax.optimization_barrier((relaid, normed_partial))
    normed_gradient, stat_sum = scatter_features(
        normed_partial, "tensor", tensor_size, tensor_index, extra=stat_partial
    )
    stat = stat_sum / full_width
    cubed = inverse * inverse * inverse
    grad_x = (
        grad_home.astype(jnp.float32)
        + inverse[:, None] * gain_part[None, :] * normed_gradient
        - x_float * cubed[:, None] * stat[:, None]
    )
    return (relaid, grad_x.astype(jnp.bfloat16))


def solution(mesh):
    placed = (
        P("dp", "tensor"),
        P(),
        P(None, "tensor"),
        P(None, "tensor"),
        P(None, "tensor"),
        P("tensor", None),
        P("dp", "tensor"),
        P("dp", None),
        P(),
    )
    return jax.shard_map(
        per_device,
        mesh=mesh,
        in_specs=placed,
        out_specs=(P("dp", "tensor"), P("dp", "tensor")),
        check_vma=False,
    )
```

```python
import math

import jax
import jax.numpy as jnp
from jax import lax
from jax.sharding import PartitionSpec as P

HEAD_SIZE = 128


ROPE_BASE = 500000.0
NORM_EPSILON = 1e-05


def doc_tables(lengths_row, token_row_count):
    ends = jnp.cumsum(lengths_row)
    token_index = jnp.arange(token_row_count, dtype=jnp.int32)
    passed = (token_index[:, None] >= ends[None, :]).astype(jnp.int32)
    doc_ids = jnp.sum(passed, axis=1)
    starts = jnp.max(jnp.where(passed > 0, ends[None, :], 0), axis=1)
    return (doc_ids, token_index - starts)


def rope_tables(positions, head_size):
    half_dim = head_size // 2
    steps = jnp.arange(half_dim, dtype=jnp.float32)
    inverse_freq = jnp.power(ROPE_BASE, -2.0 * steps / head_size)
    angles = positions.astype(jnp.float32)[:, None] * inverse_freq[None, :]
    return (jnp.cos(angles), jnp.sin(angles))


def rotate(vectors, cosine, sine_table):
    half_dim = vectors.shape[-1] // 2
    former = vectors[..., :half_dim]
    latter = vectors[..., half_dim:]
    cos_part = cosine[:, None, :]
    sin_part = sine_table[:, None, :]
    return jnp.concatenate(
        [former * cos_part - latter * sin_part, latter * cos_part + former * sin_part], axis=-1
    )


def unrotate(vectors, cosine, sine_table):
    half_dim = vectors.shape[-1] // 2
    former = vectors[..., :half_dim]
    latter = vectors[..., half_dim:]
    cos_part = cosine[:, None, :]
    sin_part = sine_table[:, None, :]
    return jnp.concatenate(
        [former * cos_part + latter * sin_part, latter * cos_part - former * sin_part], axis=-1
    )


def _is_pow2(n):
    return n > 1 and (n & (n - 1)) == 0


def _xor_pairs(size, bit):
    return [(i, i ^ bit) for i in range(size)]


def gather_features(shard, axis_name, size, position):
    if not _is_pow2(size):
        return lax.all_gather(shard, axis_name, axis=1, tiled=True)
    held = shard[None]
    masks = [0]
    bit = size >> 1
    while bit:
        incoming = lax.ppermute(held, axis_name, _xor_pairs(size, bit))
        held = jnp.concatenate([held, incoming], axis=0)
        masks = masks + [m ^ bit for m in masks]
        bit >>= 1
    table = jnp.asarray([masks.index(m) for m in range(size)], jnp.int32)
    blocks = [
        lax.dynamic_index_in_dim(held, table[s ^ position], axis=0, keepdims=False)
        for s in range(size)
    ]
    return jnp.concatenate(blocks, axis=1)


def scatter_features(partial, axis_name, size, position, extra=None):
    width = partial.shape[1] // size
    if not _is_pow2(size):
        summed = lax.psum_scatter(
            partial.astype(jnp.bfloat16), axis_name, scatter_dimension=1, tiled=True
        )
        if extra is not None:
            extra = lax.psum(extra, axis_name)
        return summed.astype(jnp.float32), extra
    held = [
        lax.dynamic_slice_in_dim(partial, (position ^ m) * width, width, axis=1)
        for m in range(size)
    ]
    masks = list(range(size))
    bit = 1
    while bit < size:
        keep = [i for i, m in enumerate(masks) if not m & bit]
        send = [i for i, m in enumerate(masks) if m & bit]
        outgoing = jnp.stack([held[i] for i in send]).astype(jnp.bfloat16)
        if extra is None:
            incoming = lax.ppermute(outgoing, axis_name, _xor_pairs(size, bit))
        else:
            incoming, extra_in = lax.ppermute((outgoing, extra), axis_name, _xor_pairs(size, bit))
            extra = extra + extra_in
        sent_masks = [masks[i] ^ bit for i in send]
        held = [
            held[i] + incoming[sent_masks.index(masks[i])].astype(jnp.float32) for i in keep
        ]
        masks = [masks[i] for i in keep]
        bit <<= 1
    return held[0], extra


def per_device(
    tokens,
    norm_gain,
    w_query,
    key_weight,
    value_weight,
    w_out,
    grad_output,
    doc_lengths,
    block_owner,
):
    token_row_count, width_part = tokens.shape
    full_width = norm_gain.shape[0]
    sources = lax.axis_size("dp")
    tensor_size = lax.axis_size("tensor")
    data_index = lax.axis_index("dp")
    tensor_index = lax.axis_index("tensor")
    query_width = w_query.shape[1]
    key_width = key_weight.shape[1]
    heads_local = query_width // HEAD_SIZE
    kv_local = key_width // HEAD_SIZE
    query_group_width = heads_local // kv_local
    scale_factor = 1.0 / math.sqrt(HEAD_SIZE)
    gain_part = lax.dynamic_slice_in_dim(norm_gain, tensor_index * width_part, width_part)
    x_float = tokens.astype(jnp.float32)

    block_count = block_owner.shape[1]
    owner_row = lax.dynamic_slice_in_dim(block_owner, data_index, 1, 0)[0]
    slot_index = jnp.arange(sources, dtype=jnp.int32)
    send_table = (owner_row[None, :] == slot_index[:, None]).astype(jnp.bfloat16)

    home_rows = token_row_count // block_count
    owned_blocks = grad_output.reshape(block_count, home_rows, width_part)
    if sources <= 16:
        returned = [lax.dynamic_index_in_dim(owned_blocks, data_index, 0, keepdims=False)]
        for shift in range(1, sources):
            pairs = [(a, (a + shift) % sources) for a in range(sources)]
            piece = lax.dynamic_index_in_dim(
                owned_blocks, (data_index + shift) % sources, 0, keepdims=False
            )
            returned.append(lax.ppermute(piece, "dp", pairs))
        returned = jnp.stack(returned)
        came_over = (
            ((data_index - owner_row) % sources)[:, None] == slot_index[None, :]
        ).astype(jnp.bfloat16)
        grad_home = (
            jnp.einsum("js,srw->jrw", came_over, returned, preferred_element_type=jnp.float32)
            .astype(jnp.bfloat16)
            .reshape(token_row_count, width_part)
        )
    else:
        arrived = lax.all_to_all(
            owned_blocks.reshape(block_count, -1), "dp", split_axis=0, concat_axis=0, tiled=True
        )
        grad_home = (
            lax.dot_general(
                send_table, arrived, (((0,), (0,)), ((), ())), preferred_element_type=jnp.float32
            )
            .astype(jnp.bfloat16)
            .reshape(token_row_count, width_part)
        )

    gathered = lax.all_gather(tokens, "tensor", axis=1, tiled=True)
    gathered_float = gathered.astype(jnp.float32)
    inverse = lax.rsqrt(jnp.mean(gathered_float * gathered_float, axis=1) + NORM_EPSILON)
    normed_input = (gathered_float * inverse[:, None] * norm_gain[None, :]).astype(jnp.bfloat16)
    query_raw = jnp.dot(normed_input, w_query, preferred_element_type=jnp.float32)
    key_raw = jnp.dot(normed_input, key_weight, preferred_element_type=jnp.float32)
    value_raw = jnp.dot(normed_input, value_weight, preferred_element_type=jnp.float32)
    doc_ids, positions = doc_tables(doc_lengths[0], token_row_count)
    token_index = jnp.arange(token_row_count, dtype=jnp.int32)
    allowed = (doc_ids[:, None] == doc_ids[None, :]) & (
        token_index[None, :] <= token_index[:, None]
    )
    cosine, sine_table = rope_tables(positions, HEAD_SIZE)
    query_rows = rotate(
        query_raw.reshape(token_row_count, heads_local, HEAD_SIZE), cosine, sine_table
    ).astype(jnp.bfloat16)
    keys = rotate(
        key_raw.reshape(token_row_count, kv_local, HEAD_SIZE), cosine, sine_table
    ).astype(jnp.bfloat16)
    value_rows = value_raw.astype(jnp.bfloat16).reshape(token_row_count, kv_local, HEAD_SIZE)
    grouped_query = query_rows.reshape(token_row_count, kv_local, query_group_width, HEAD_SIZE)
    scores = (
        jnp.einsum("qkgd,skd->kgqs", grouped_query, keys, preferred_element_type=jnp.float32)
        * scale_factor
    )
    weights = jnp.where(allowed[None, None], jnp.exp(scores), 0.0)
    probs = weights / jnp.sum(weights, axis=-1, keepdims=True)
    probs_low = probs.astype(jnp.bfloat16)
    attended = jnp.einsum(
        "kgqs,skd->qkgd", probs_low, value_rows, preferred_element_type=jnp.float32
    ).astype(jnp.bfloat16)
    attended_flat = attended.reshape(token_row_count, query_width)
    mixed_partial = jnp.dot(attended_flat, w_out, preferred_element_type=jnp.float32)
    mixed, _ = scatter_features(mixed_partial, "tensor", tensor_size, tensor_index)
    output_home = (x_float + mixed).astype(jnp.bfloat16)
    grad_full = lax.all_gather(grad_home, "tensor", axis=1, tiled=True)
    attended_gradient = lax.dot_general(
        grad_full,
        w_out,
        (((1,), (1,)), ((), ())),
        preferred_element_type=jnp.float32,
    ).astype(jnp.bfloat16)
    grouped_gradient = attended_gradient.reshape(
        token_row_count, kv_local, query_group_width, HEAD_SIZE
    )
    delta = jnp.sum(grouped_gradient.astype(jnp.float32) * attended.astype(jnp.float32), axis=-1)
    grad_probs = jnp.einsum(
        "qkgd,skd->kgqs", grouped_gradient, value_rows, preferred_element_type=jnp.float32
    )
    grad_scores = (probs * (grad_probs - jnp.transpose(delta, (1, 2, 0))[..., None])).astype(
        jnp.bfloat16
    )
    grad_query_rot = (
        jnp.einsum("kgqs,skd->qkgd", grad_scores, keys, preferred_element_type=jnp.float32)
        * scale_factor
    )
    grad_keys_rot = (
        jnp.einsum("kgqs,qkgd->skd", grad_scores, grouped_query, preferred_element_type=jnp.float32)
        * scale_factor
    )
    value_gradient = jnp.einsum(
        "kgqs,qkgd->skd", probs_low, grouped_gradient, preferred_element_type=jnp.float32
    )
    grad_query = unrotate(
        grad_query_rot.reshape(token_row_count, heads_local, HEAD_SIZE), cosine, sine_table
    ).astype(jnp.bfloat16)
    key_gradient = unrotate(grad_keys_rot, cosine, sine_table).astype(jnp.bfloat16)
    output_home, grad_query, key_gradient, value_gradient = lax.optimization_barrier(
        (output_home, grad_query, key_gradient, value_gradient)
    )
    home_blocks = output_home.reshape(block_count, home_rows, width_part)
    if sources <= 16:
        block_for = jnp.sum(
            jnp.where(send_table > 0, jnp.arange(block_count, dtype=jnp.int32)[None, :], 0), axis=1
        )
        landed = [
            lax.dynamic_index_in_dim(home_blocks, block_for[data_index], 0, keepdims=False)
        ]
        for shift in range(1, sources):
            pairs = [(a, (a + shift) % sources) for a in range(sources)]
            piece = lax.dynamic_index_in_dim(
                home_blocks, block_for[(data_index + shift) % sources], 0, keepdims=False
            )
            landed.append(lax.ppermute(piece, "dp", pairs))
        landed = jnp.stack(landed)
        came_over = (
            ((data_index - slot_index) % sources)[:, None] == slot_index[None, :]
        ).astype(jnp.bfloat16)
        relaid = (
            jnp.einsum("bs,srw->brw", came_over, landed, preferred_element_type=jnp.float32)
            .astype(jnp.bfloat16)
            .reshape(token_row_count, width_part)
        )
    else:
        outgoing = jnp.dot(
            send_table, home_blocks.reshape(block_count, -1), preferred_element_type=jnp.float32
        ).astype(jnp.bfloat16)
        relaid = lax.all_to_all(outgoing, "dp", split_axis=0, concat_axis=0, tiled=True).reshape(
            token_row_count, width_part
        )

    contract_out = (((1,), (1,)), ((), ()))
    normed_partial = (
        lax.dot_general(
            grad_query.reshape(token_row_count, query_width),
            w_query,
            contract_out,
            preferred_element_type=jnp.float32,
        )
        + lax.dot_general(
            key_gradient.reshape(token_row_count, key_width),
            key_weight,
            contract_out,
            preferred_element_type=jnp.float32,
        )
        + lax.dot_general(
            value_gradient.astype(jnp.bfloat16).reshape(token_row_count, key_width),
            value_weight,
            contract_out,
            preferred_element_type=jnp.float32,
        )
    )
    stat_partial = jnp.sum(normed_partial * norm_gain[None, :] * gathered_float, axis=1)
    normed_gradient, stat_sum = scatter_features(
        normed_partial, "tensor", tensor_size, tensor_index, extra=stat_partial
    )
    stat = stat_sum / full_width
    cubed = inverse * inverse * inverse
    grad_x = (
        grad_home.astype(jnp.float32)
        + inverse[:, None] * gain_part[None, :] * normed_gradient
        - x_float * cubed[:, None] * stat[:, None]
    )
    return (relaid, grad_x.astype(jnp.bfloat16))


def solution(mesh):
    placed = (
        P("dp", "tensor"),
        P(),
        P(None, "tensor"),
        P(None, "tensor"),
        P(None, "tensor"),
        P("tensor", None),
        P("dp", "tensor"),
        P("dp", None),
        P(),
    )
    return jax.shard_map(
        per_device,
        mesh=mesh,
        in_specs=placed,
        out_specs=(P("dp", "tensor"), P("dp", "tensor")),
        check_vma=False,
    )
```

```python
import math

import jax
import jax.numpy as jnp
from jax import lax
from jax.sharding import PartitionSpec as P

HEAD_SIZE = 128


ROPE_BASE = 500000.0
NORM_EPSILON = 1e-05


def doc_tables(lengths_row, token_row_count):
    ends = jnp.cumsum(lengths_row)
    token_index = jnp.arange(token_row_count, dtype=jnp.int32)
    passed = (token_index[:, None] >= ends[None, :]).astype(jnp.int32)
    doc_ids = jnp.sum(passed, axis=1)
    starts = jnp.max(jnp.where(passed > 0, ends[None, :], 0), axis=1)
    return (doc_ids, token_index - starts)


def rope_tables(positions, head_size):
    half_dim = head_size // 2
    steps = jnp.arange(half_dim, dtype=jnp.float32)
    inverse_freq = jnp.power(ROPE_BASE, -2.0 * steps / head_size)
    angles = positions.astype(jnp.float32)[:, None] * inverse_freq[None, :]
    return (jnp.cos(angles), jnp.sin(angles))


def rotate(vectors, cosine, sine_table):
    half_dim = vectors.shape[-1] // 2
    former = vectors[..., :half_dim]
    latter = vectors[..., half_dim:]
    cos_part = cosine[:, None, :]
    sin_part = sine_table[:, None, :]
    return jnp.concatenate(
        [former * cos_part - latter * sin_part, latter * cos_part + former * sin_part], axis=-1
    )


def unrotate(vectors, cosine, sine_table):
    half_dim = vectors.shape[-1] // 2
    former = vectors[..., :half_dim]
    latter = vectors[..., half_dim:]
    cos_part = cosine[:, None, :]
    sin_part = sine_table[:, None, :]
    return jnp.concatenate(
        [former * cos_part + latter * sin_part, latter * cos_part - former * sin_part], axis=-1
    )


def _is_pow2(n):
    return n > 1 and (n & (n - 1)) == 0


def _xor_pairs(size, bit):
    return [(i, i ^ bit) for i in range(size)]


def gather_features(shard, axis_name, size, position):
    if not _is_pow2(size):
        return lax.all_gather(shard, axis_name, axis=1, tiled=True)
    held = shard[None]
    masks = [0]
    bit = size >> 1
    while bit:
        incoming = lax.ppermute(held, axis_name, _xor_pairs(size, bit))
        held = jnp.concatenate([held, incoming], axis=0)
        masks = masks + [m ^ bit for m in masks]
        bit >>= 1
    table = jnp.asarray([masks.index(m) for m in range(size)], jnp.int32)
    blocks = [
        lax.dynamic_index_in_dim(held, table[s ^ position], axis=0, keepdims=False)
        for s in range(size)
    ]
    return jnp.concatenate(blocks, axis=1)


def scatter_features(partial, axis_name, size, position, extra=None):
    width = partial.shape[1] // size
    if not _is_pow2(size):
        summed = lax.psum_scatter(
            partial.astype(jnp.bfloat16), axis_name, scatter_dimension=1, tiled=True
        )
        if extra is not None:
            extra = lax.psum(extra, axis_name)
        return summed.astype(jnp.float32), extra
    held = [
        lax.dynamic_slice_in_dim(partial, (position ^ m) * width, width, axis=1)
        for m in range(size)
    ]
    masks = list(range(size))
    bit = 1
    while bit < size:
        keep = [i for i, m in enumerate(masks) if not m & bit]
        send = [i for i, m in enumerate(masks) if m & bit]
        outgoing = jnp.stack([held[i] for i in send]).astype(jnp.bfloat16)
        if extra is None:
            incoming = lax.ppermute(outgoing, axis_name, _xor_pairs(size, bit))
        else:
            incoming, extra_in = lax.ppermute((outgoing, extra), axis_name, _xor_pairs(size, bit))
            extra = extra + extra_in
        sent_masks = [masks[i] ^ bit for i in send]
        held = [
            held[i] + incoming[sent_masks.index(masks[i])].astype(jnp.float32) for i in keep
        ]
        masks = [masks[i] for i in keep]
        bit <<= 1
    return held[0], extra


def per_device(
    tokens,
    norm_gain,
    w_query,
    key_weight,
    value_weight,
    w_out,
    grad_output,
    doc_lengths,
    block_owner,
):
    token_row_count, width_part = tokens.shape
    full_width = norm_gain.shape[0]
    sources = lax.axis_size("dp")
    tensor_size = lax.axis_size("tensor")
    data_index = lax.axis_index("dp")
    tensor_index = lax.axis_index("tensor")
    query_width = w_query.shape[1]
    key_width = key_weight.shape[1]
    heads_local = query_width // HEAD_SIZE
    kv_local = key_width // HEAD_SIZE
    query_group_width = heads_local // kv_local
    scale_factor = 1.0 / math.sqrt(HEAD_SIZE)
    gain_part = lax.dynamic_slice_in_dim(norm_gain, tensor_index * width_part, width_part)
    x_float = tokens.astype(jnp.float32)

    block_count = block_owner.shape[1]
    owner_row = lax.dynamic_slice_in_dim(block_owner, data_index, 1, 0)[0]
    slot_index = jnp.arange(sources, dtype=jnp.int32)
    send_table = (owner_row[None, :] == slot_index[:, None]).astype(jnp.bfloat16)

    home_rows = token_row_count // block_count
    owned_blocks = grad_output.reshape(block_count, home_rows, width_part)
    if sources <= 16:
        returned = [lax.dynamic_index_in_dim(owned_blocks, data_index, 0, keepdims=False)]
        for shift in range(1, sources):
            pairs = [(a, (a + shift) % sources) for a in range(sources)]
            piece = lax.dynamic_index_in_dim(
                owned_blocks, (data_index + shift) % sources, 0, keepdims=False
            )
            returned.append(lax.ppermute(piece, "dp", pairs))
        returned = jnp.stack(returned)
        came_over = (
            ((data_index - owner_row) % sources)[:, None] == slot_index[None, :]
        ).astype(jnp.bfloat16)
        grad_home = (
            jnp.einsum("js,srw->jrw", came_over, returned, preferred_element_type=jnp.float32)
            .astype(jnp.bfloat16)
            .reshape(token_row_count, width_part)
        )
    else:
        arrived = lax.all_to_all(
            owned_blocks.reshape(block_count, -1), "dp", split_axis=0, concat_axis=0, tiled=True
        )
        grad_home = (
            lax.dot_general(
                send_table, arrived, (((0,), (0,)), ((), ())), preferred_element_type=jnp.float32
            )
            .astype(jnp.bfloat16)
            .reshape(token_row_count, width_part)
        )

    gathered = lax.all_gather(tokens, "tensor", axis=1, tiled=True)
    gathered_float = gathered.astype(jnp.float32)
    inverse = lax.rsqrt(jnp.mean(gathered_float * gathered_float, axis=1) + NORM_EPSILON)
    normed_input = (gathered_float * inverse[:, None] * norm_gain[None, :]).astype(jnp.bfloat16)
    query_raw = jnp.dot(normed_input, w_query, preferred_element_type=jnp.float32)
    key_raw = jnp.dot(normed_input, key_weight, preferred_element_type=jnp.float32)
    value_raw = jnp.dot(normed_input, value_weight, preferred_element_type=jnp.float32)
    doc_ids, positions = doc_tables(doc_lengths[0], token_row_count)
    token_index = jnp.arange(token_row_count, dtype=jnp.int32)
    allowed = (doc_ids[:, None] == doc_ids[None, :]) & (
        token_index[None, :] <= token_index[:, None]
    )
    cosine, sine_table = rope_tables(positions, HEAD_SIZE)
    query_rows = rotate(
        query_raw.reshape(token_row_count, heads_local, HEAD_SIZE), cosine, sine_table
    ).astype(jnp.bfloat16)
    keys = rotate(
        key_raw.reshape(token_row_count, kv_local, HEAD_SIZE), cosine, sine_table
    ).astype(jnp.bfloat16)
    value_rows = value_raw.astype(jnp.bfloat16).reshape(token_row_count, kv_local, HEAD_SIZE)
    grouped_query = query_rows.reshape(token_row_count, kv_local, query_group_width, HEAD_SIZE)
    scores = (
        jnp.einsum("qkgd,skd->kgqs", grouped_query, keys, preferred_element_type=jnp.float32)
        * scale_factor
    )
    weights = jnp.where(allowed[None, None], jnp.exp(scores), 0.0)
    probs = weights / jnp.sum(weights, axis=-1, keepdims=True)
    probs_low = probs.astype(jnp.bfloat16)
    attended = jnp.einsum(
        "kgqs,skd->qkgd", probs_low, value_rows, preferred_element_type=jnp.float32
    ).astype(jnp.bfloat16)
    attended_flat = attended.reshape(token_row_count, query_width)
    mixed = (
        lax.psum_scatter(
            lax.dot_general(
                w_out, attended_flat, (((0,), (1,)), ((), ())), preferred_element_type=jnp.float32
            ).astype(jnp.bfloat16),
            "tensor",
            scatter_dimension=0,
            tiled=True,
        )
        .astype(jnp.float32)
        .T
    )
    output_home = (x_float + mixed).astype(jnp.bfloat16)
    grad_full = lax.all_gather(grad_home, "tensor", axis=1, tiled=True)
    attended_gradient = lax.dot_general(
        grad_full,
        w_out,
        (((1,), (1,)), ((), ())),
        preferred_element_type=jnp.float32,
    ).astype(jnp.bfloat16)
    grouped_gradient = attended_gradient.reshape(
        token_row_count, kv_local, query_group_width, HEAD_SIZE
    )
    delta = jnp.sum(grouped_gradient.astype(jnp.float32) * attended.astype(jnp.float32), axis=-1)
    grad_probs = jnp.einsum(
        "qkgd,skd->kgqs", grouped_gradient, value_rows, preferred_element_type=jnp.float32
    )
    grad_scores = (probs * (grad_probs - jnp.transpose(delta, (1, 2, 0))[..., None])).astype(
        jnp.bfloat16
    )
    grad_query_rot = (
        jnp.einsum("kgqs,skd->qkgd", grad_scores, keys, preferred_element_type=jnp.float32)
        * scale_factor
    )
    grad_keys_rot = (
        jnp.einsum("kgqs,qkgd->skd", grad_scores, grouped_query, preferred_element_type=jnp.float32)
        * scale_factor
    )
    value_gradient = jnp.einsum(
        "kgqs,qkgd->skd", probs_low, grouped_gradient, preferred_element_type=jnp.float32
    )
    grad_query = unrotate(
        grad_query_rot.reshape(token_row_count, heads_local, HEAD_SIZE), cosine, sine_table
    ).astype(jnp.bfloat16)
    key_gradient = unrotate(grad_keys_rot, cosine, sine_table).astype(jnp.bfloat16)
    output_home, grad_query, key_gradient, value_gradient = lax.optimization_barrier(
        (output_home, grad_query, key_gradient, value_gradient)
    )
    home_blocks = output_home.reshape(block_count, home_rows, width_part)
    if sources <= 16:
        block_for = jnp.sum(
            jnp.where(send_table > 0, jnp.arange(block_count, dtype=jnp.int32)[None, :], 0), axis=1
        )
        landed = [
            lax.dynamic_index_in_dim(home_blocks, block_for[data_index], 0, keepdims=False)
        ]
        for shift in range(1, sources):
            pairs = [(a, (a + shift) % sources) for a in range(sources)]
            piece = lax.dynamic_index_in_dim(
                home_blocks, block_for[(data_index + shift) % sources], 0, keepdims=False
            )
            landed.append(lax.ppermute(piece, "dp", pairs))
        landed = jnp.stack(landed)
        came_over = (
            ((data_index - slot_index) % sources)[:, None] == slot_index[None, :]
        ).astype(jnp.bfloat16)
        relaid = (
            jnp.einsum("bs,srw->brw", came_over, landed, preferred_element_type=jnp.float32)
            .astype(jnp.bfloat16)
            .reshape(token_row_count, width_part)
        )
    else:
        outgoing = jnp.dot(
            send_table, home_blocks.reshape(block_count, -1), preferred_element_type=jnp.float32
        ).astype(jnp.bfloat16)
        relaid = lax.all_to_all(outgoing, "dp", split_axis=0, concat_axis=0, tiled=True).reshape(
            token_row_count, width_part
        )

    contract_out = (((1,), (1,)), ((), ()))
    normed_partial = (
        lax.dot_general(
            grad_query.reshape(token_row_count, query_width),
            w_query,
            contract_out,
            preferred_element_type=jnp.float32,
        )
        + lax.dot_general(
            key_gradient.reshape(token_row_count, key_width),
            key_weight,
            contract_out,
            preferred_element_type=jnp.float32,
        )
        + lax.dot_general(
            value_gradient.astype(jnp.bfloat16).reshape(token_row_count, key_width),
            value_weight,
            contract_out,
            preferred_element_type=jnp.float32,
        )
    )
    stat_partial = jnp.sum(normed_partial * norm_gain[None, :] * gathered_float, axis=1)
    normed_gradient, stat_sum = scatter_features(
        normed_partial, "tensor", tensor_size, tensor_index, extra=stat_partial
    )
    stat = stat_sum / full_width
    cubed = inverse * inverse * inverse
    grad_x = (
        grad_home.astype(jnp.float32)
        + inverse[:, None] * gain_part[None, :] * normed_gradient
        - x_float * cubed[:, None] * stat[:, None]
    )
    return (relaid, grad_x.astype(jnp.bfloat16))


def solution(mesh):
    placed = (
        P("dp", "tensor"),
        P(),
        P(None, "tensor"),
        P(None, "tensor"),
        P(None, "tensor"),
        P("tensor", None),
        P("dp", "tensor"),
        P("dp", None),
        P(),
    )
    return jax.shard_map(
        per_device,
        mesh=mesh,
        in_specs=placed,
        out_specs=(P("dp", "tensor"), P("dp", "tensor")),
        check_vma=False,
    )
```

```python
import math

import jax
import jax.numpy as jnp
from jax import lax
from jax.sharding import PartitionSpec as P

HEAD_SIZE = 128


ROPE_BASE = 500000.0
NORM_EPSILON = 1e-05


def doc_tables(lengths_row, token_row_count):
    ends = jnp.cumsum(lengths_row)
    token_index = jnp.arange(token_row_count, dtype=jnp.int32)
    passed = (token_index[:, None] >= ends[None, :]).astype(jnp.int32)
    doc_ids = jnp.sum(passed, axis=1)
    starts = jnp.max(jnp.where(passed > 0, ends[None, :], 0), axis=1)
    return (doc_ids, token_index - starts)


def rope_tables(positions, head_size):
    half_dim = head_size // 2
    steps = jnp.arange(half_dim, dtype=jnp.float32)
    inverse_freq = jnp.power(ROPE_BASE, -2.0 * steps / head_size)
    angles = positions.astype(jnp.float32)[:, None] * inverse_freq[None, :]
    return (jnp.cos(angles), jnp.sin(angles))


def rotate(vectors, cosine, sine_table):
    half_dim = vectors.shape[-1] // 2
    former = vectors[..., :half_dim]
    latter = vectors[..., half_dim:]
    cos_part = cosine[:, None, :]
    sin_part = sine_table[:, None, :]
    return jnp.concatenate(
        [former * cos_part - latter * sin_part, latter * cos_part + former * sin_part], axis=-1
    )


def unrotate(vectors, cosine, sine_table):
    half_dim = vectors.shape[-1] // 2
    former = vectors[..., :half_dim]
    latter = vectors[..., half_dim:]
    cos_part = cosine[:, None, :]
    sin_part = sine_table[:, None, :]
    return jnp.concatenate(
        [former * cos_part + latter * sin_part, latter * cos_part - former * sin_part], axis=-1
    )


def _is_pow2(n):
    return n > 1 and (n & (n - 1)) == 0


def _xor_pairs(size, bit):
    return [(i, i ^ bit) for i in range(size)]


def gather_features(shard, axis_name, size, position):
    if not _is_pow2(size):
        return lax.all_gather(shard, axis_name, axis=1, tiled=True)
    held = shard[None]
    masks = [0]
    bit = size >> 1
    while bit:
        incoming = lax.ppermute(held, axis_name, _xor_pairs(size, bit))
        held = jnp.concatenate([held, incoming], axis=0)
        masks = masks + [m ^ bit for m in masks]
        bit >>= 1
    table = jnp.asarray([masks.index(m) for m in range(size)], jnp.int32)
    blocks = [
        lax.dynamic_index_in_dim(held, table[s ^ position], axis=0, keepdims=False)
        for s in range(size)
    ]
    return jnp.concatenate(blocks, axis=1)


def scatter_features(partial, axis_name, size, position, extra=None):
    width = partial.shape[1] // size
    if not _is_pow2(size):
        summed = lax.psum_scatter(
            partial.astype(jnp.bfloat16), axis_name, scatter_dimension=1, tiled=True
        )
        if extra is not None:
            extra = lax.psum(extra, axis_name)
        return summed.astype(jnp.float32), extra
    held = [
        lax.dynamic_slice_in_dim(partial, (position ^ m) * width, width, axis=1)
        for m in range(size)
    ]
    masks = list(range(size))
    bit = 1
    while bit < size:
        keep = [i for i, m in enumerate(masks) if not m & bit]
        send = [i for i, m in enumerate(masks) if m & bit]
        outgoing = jnp.stack([held[i] for i in send]).astype(jnp.bfloat16)
        if extra is None:
            incoming = lax.ppermute(outgoing, axis_name, _xor_pairs(size, bit))
        else:
            incoming, extra_in = lax.ppermute((outgoing, extra), axis_name, _xor_pairs(size, bit))
            extra = extra + extra_in
        sent_masks = [masks[i] ^ bit for i in send]
        held = [
            held[i] + incoming[sent_masks.index(masks[i])].astype(jnp.float32) for i in keep
        ]
        masks = [masks[i] for i in keep]
        bit <<= 1
    return held[0], extra


def per_device(
    tokens,
    norm_gain,
    w_query,
    key_weight,
    value_weight,
    w_out,
    grad_output,
    doc_lengths,
    block_owner,
):
    token_row_count, width_part = tokens.shape
    full_width = norm_gain.shape[0]
    sources = lax.axis_size("dp")
    tensor_size = lax.axis_size("tensor")
    data_index = lax.axis_index("dp")
    tensor_index = lax.axis_index("tensor")
    query_width = w_query.shape[1]
    key_width = key_weight.shape[1]
    heads_local = query_width // HEAD_SIZE
    kv_local = key_width // HEAD_SIZE
    query_group_width = heads_local // kv_local
    scale_factor = 1.0 / math.sqrt(HEAD_SIZE)
    gain_part = lax.dynamic_slice_in_dim(norm_gain, tensor_index * width_part, width_part)
    x_float = tokens.astype(jnp.float32)

    block_count = block_owner.shape[1]
    owner_row = lax.dynamic_slice_in_dim(block_owner, data_index, 1, 0)[0]
    slot_index = jnp.arange(sources, dtype=jnp.int32)
    send_table = (owner_row[None, :] == slot_index[:, None]).astype(jnp.bfloat16)

    home_rows = token_row_count // block_count
    owned_blocks = grad_output.reshape(block_count, home_rows, width_part)
    if sources <= 16:
        returned = [lax.dynamic_index_in_dim(owned_blocks, data_index, 0, keepdims=False)]
        for shift in range(1, sources):
            pairs = [(a, (a + shift) % sources) for a in range(sources)]
            piece = lax.dynamic_index_in_dim(
                owned_blocks, (data_index + shift) % sources, 0, keepdims=False
            )
            returned.append(lax.ppermute(piece, "dp", pairs))
        returned = jnp.stack(returned)
        came_over = (
            ((data_index - owner_row) % sources)[:, None] == slot_index[None, :]
        ).astype(jnp.bfloat16)
        grad_home = (
            jnp.einsum("js,srw->jrw", came_over, returned, preferred_element_type=jnp.float32)
            .astype(jnp.bfloat16)
            .reshape(token_row_count, width_part)
        )
    else:
        arrived = lax.all_to_all(
            owned_blocks.reshape(block_count, -1), "dp", split_axis=0, concat_axis=0, tiled=True
        )
        grad_home = (
            lax.dot_general(
                send_table, arrived, (((0,), (0,)), ((), ())), preferred_element_type=jnp.float32
            )
            .astype(jnp.bfloat16)
            .reshape(token_row_count, width_part)
        )

    gathered = lax.all_gather(tokens, "tensor", axis=1, tiled=True)
    gathered_float = gathered.astype(jnp.float32)
    inverse = lax.rsqrt(jnp.mean(gathered_float * gathered_float, axis=1) + NORM_EPSILON)
    normed_input = (gathered_float * inverse[:, None] * norm_gain[None, :]).astype(jnp.bfloat16)
    query_raw = jnp.dot(normed_input, w_query, preferred_element_type=jnp.float32)
    key_raw = jnp.dot(normed_input, key_weight, preferred_element_type=jnp.float32)
    value_raw = jnp.dot(normed_input, value_weight, preferred_element_type=jnp.float32)
    doc_ids, positions = doc_tables(doc_lengths[0], token_row_count)
    token_index = jnp.arange(token_row_count, dtype=jnp.int32)
    allowed = (doc_ids[:, None] == doc_ids[None, :]) & (
        token_index[None, :] <= token_index[:, None]
    )
    cosine, sine_table = rope_tables(positions, HEAD_SIZE)
    query_rows = rotate(
        query_raw.reshape(token_row_count, heads_local, HEAD_SIZE), cosine, sine_table
    ).astype(jnp.bfloat16)
    keys = rotate(
        key_raw.reshape(token_row_count, kv_local, HEAD_SIZE), cosine, sine_table
    ).astype(jnp.bfloat16)
    value_rows = value_raw.astype(jnp.bfloat16).reshape(token_row_count, kv_local, HEAD_SIZE)
    grouped_query = query_rows.reshape(token_row_count, kv_local, query_group_width, HEAD_SIZE)
    scores = (
        jnp.einsum("qkgd,skd->kgqs", grouped_query, keys, preferred_element_type=jnp.float32)
        * scale_factor
    )
    weights = jnp.where(allowed[None, None], jnp.exp(scores), 0.0)
    probs = weights / jnp.sum(weights, axis=-1, keepdims=True)
    probs_low = probs.astype(jnp.bfloat16)
    attended = jnp.einsum(
        "kgqs,skd->qkgd", probs_low, value_rows, preferred_element_type=jnp.float32
    ).astype(jnp.bfloat16)
    attended_flat = attended.reshape(token_row_count, query_width)
    mixed_partial = jnp.dot(attended_flat, w_out, preferred_element_type=jnp.float32)
    mixed, _ = scatter_features(mixed_partial, "tensor", tensor_size, tensor_index)
    output_home = (x_float + mixed).astype(jnp.bfloat16)
    grad_full = lax.all_gather(grad_home, "tensor", axis=1, tiled=True)
    attended_gradient = lax.dot_general(
        grad_full,
        w_out,
        (((1,), (1,)), ((), ())),
        preferred_element_type=jnp.float32,
    ).astype(jnp.bfloat16)
    grouped_gradient = attended_gradient.reshape(
        token_row_count, kv_local, query_group_width, HEAD_SIZE
    )
    delta = jnp.sum(grouped_gradient.astype(jnp.float32) * attended.astype(jnp.float32), axis=-1)
    grad_probs = jnp.einsum(
        "qkgd,skd->kgqs", grouped_gradient, value_rows, preferred_element_type=jnp.float32
    )
    grad_scores = (probs * (grad_probs - jnp.transpose(delta, (1, 2, 0))[..., None])).astype(
        jnp.bfloat16
    )
    grad_query_rot = (
        jnp.einsum("kgqs,skd->qkgd", grad_scores, keys, preferred_element_type=jnp.float32)
        * scale_factor
    )
    grad_keys_rot = (
        jnp.einsum("kgqs,qkgd->skd", grad_scores, grouped_query, preferred_element_type=jnp.float32)
        * scale_factor
    )
    value_gradient = jnp.einsum(
        "kgqs,qkgd->skd", probs_low, grouped_gradient, preferred_element_type=jnp.float32
    )
    grad_query = unrotate(
        grad_query_rot.reshape(token_row_count, heads_local, HEAD_SIZE), cosine, sine_table
    ).astype(jnp.bfloat16)
    key_gradient = unrotate(grad_keys_rot, cosine, sine_table).astype(jnp.bfloat16)
    output_home, grad_query, key_gradient, value_gradient = lax.optimization_barrier(
        (output_home, grad_query, key_gradient, value_gradient)
    )
    home_blocks = output_home.reshape(block_count, home_rows, width_part)
    outgoing = jnp.dot(
        send_table, home_blocks.reshape(block_count, -1), preferred_element_type=jnp.float32
    ).astype(jnp.bfloat16)
    relaid = lax.all_to_all(outgoing, "dp", split_axis=0, concat_axis=0, tiled=True).reshape(
        token_row_count, width_part
    )

    contract_out = (((1,), (1,)), ((), ()))
    normed_partial = (
        lax.dot_general(
            grad_query.reshape(token_row_count, query_width),
            w_query,
            contract_out,
            preferred_element_type=jnp.float32,
        )
        + lax.dot_general(
            key_gradient.reshape(token_row_count, key_width),
            key_weight,
            contract_out,
            preferred_element_type=jnp.float32,
        )
        + lax.dot_general(
            value_gradient.astype(jnp.bfloat16).reshape(token_row_count, key_width),
            value_weight,
            contract_out,
            preferred_element_type=jnp.float32,
        )
    )
    stat_partial = jnp.sum(normed_partial * norm_gain[None, :] * gathered_float, axis=1)
    normed_gradient, stat_sum = scatter_features(
        normed_partial, "tensor", tensor_size, tensor_index, extra=stat_partial
    )
    stat = stat_sum / full_width
    cubed = inverse * inverse * inverse
    grad_x = (
        grad_home.astype(jnp.float32)
        + inverse[:, None] * gain_part[None, :] * normed_gradient
        - x_float * cubed[:, None] * stat[:, None]
    )
    return (relaid, grad_x.astype(jnp.bfloat16))


def solution(mesh):
    placed = (
        P("dp", "tensor"),
        P(),
        P(None, "tensor"),
        P(None, "tensor"),
        P(None, "tensor"),
        P("tensor", None),
        P("dp", "tensor"),
        P("dp", None),
        P(),
    )
    return jax.shard_map(
        per_device,
        mesh=mesh,
        in_specs=placed,
        out_specs=(P("dp", "tensor"), P("dp", "tensor")),
        check_vma=False,
    )
```

```python
import math

import jax
import jax.numpy as jnp
from jax import lax
from jax.sharding import PartitionSpec as P

HEAD_SIZE = 128


ROPE_BASE = 500000.0
NORM_EPSILON = 1e-05


def doc_tables(lengths_row, token_row_count):
    ends = jnp.cumsum(lengths_row)
    token_index = jnp.arange(token_row_count, dtype=jnp.int32)
    passed = (token_index[:, None] >= ends[None, :]).astype(jnp.int32)
    doc_ids = jnp.sum(passed, axis=1)
    starts = jnp.max(jnp.where(passed > 0, ends[None, :], 0), axis=1)
    return (doc_ids, token_index - starts)


def rope_tables(positions, head_size):
    half_dim = head_size // 2
    steps = jnp.arange(half_dim, dtype=jnp.float32)
    inverse_freq = jnp.power(ROPE_BASE, -2.0 * steps / head_size)
    angles = positions.astype(jnp.float32)[:, None] * inverse_freq[None, :]
    return (jnp.cos(angles), jnp.sin(angles))


def rotate(vectors, cosine, sine_table):
    half_dim = vectors.shape[-1] // 2
    former = vectors[..., :half_dim]
    latter = vectors[..., half_dim:]
    cos_part = cosine[:, None, :]
    sin_part = sine_table[:, None, :]
    return jnp.concatenate(
        [former * cos_part - latter * sin_part, latter * cos_part + former * sin_part], axis=-1
    )


def unrotate(vectors, cosine, sine_table):
    half_dim = vectors.shape[-1] // 2
    former = vectors[..., :half_dim]
    latter = vectors[..., half_dim:]
    cos_part = cosine[:, None, :]
    sin_part = sine_table[:, None, :]
    return jnp.concatenate(
        [former * cos_part + latter * sin_part, latter * cos_part - former * sin_part], axis=-1
    )


def _is_pow2(n):
    return n > 1 and (n & (n - 1)) == 0


def _xor_pairs(size, bit):
    return [(i, i ^ bit) for i in range(size)]


def gather_features(shard, axis_name, size, position):
    if not _is_pow2(size):
        return lax.all_gather(shard, axis_name, axis=1, tiled=True)
    held = shard[None]
    masks = [0]
    bit = size >> 1
    while bit:
        incoming = lax.ppermute(held, axis_name, _xor_pairs(size, bit))
        held = jnp.concatenate([held, incoming], axis=0)
        masks = masks + [m ^ bit for m in masks]
        bit >>= 1
    table = jnp.asarray([masks.index(m) for m in range(size)], jnp.int32)
    blocks = [
        lax.dynamic_index_in_dim(held, table[s ^ position], axis=0, keepdims=False)
        for s in range(size)
    ]
    return jnp.concatenate(blocks, axis=1)


def scatter_features(partial, axis_name, size, position, extra=None):
    width = partial.shape[1] // size
    if not _is_pow2(size):
        summed = lax.psum_scatter(
            partial.astype(jnp.bfloat16), axis_name, scatter_dimension=1, tiled=True
        )
        if extra is not None:
            extra = lax.psum(extra, axis_name)
        return summed.astype(jnp.float32), extra
    held = [
        lax.dynamic_slice_in_dim(partial, (position ^ m) * width, width, axis=1)
        for m in range(size)
    ]
    masks = list(range(size))
    bit = 1
    while bit < size:
        keep = [i for i, m in enumerate(masks) if not m & bit]
        send = [i for i, m in enumerate(masks) if m & bit]
        outgoing = jnp.stack([held[i] for i in send]).astype(jnp.bfloat16)
        if extra is None:
            incoming = lax.ppermute(outgoing, axis_name, _xor_pairs(size, bit))
        else:
            incoming, extra_in = lax.ppermute((outgoing, extra), axis_name, _xor_pairs(size, bit))
            extra = extra + extra_in
        sent_masks = [masks[i] ^ bit for i in send]
        held = [
            held[i] + incoming[sent_masks.index(masks[i])].astype(jnp.float32) for i in keep
        ]
        masks = [masks[i] for i in keep]
        bit <<= 1
    return held[0], extra


def per_device(
    tokens,
    norm_gain,
    w_query,
    key_weight,
    value_weight,
    w_out,
    grad_output,
    doc_lengths,
    block_owner,
):
    token_row_count, width_part = tokens.shape
    full_width = norm_gain.shape[0]
    sources = lax.axis_size("dp")
    tensor_size = lax.axis_size("tensor")
    data_index = lax.axis_index("dp")
    tensor_index = lax.axis_index("tensor")
    query_width = w_query.shape[1]
    key_width = key_weight.shape[1]
    heads_local = query_width // HEAD_SIZE
    kv_local = key_width // HEAD_SIZE
    query_group_width = heads_local // kv_local
    scale_factor = 1.0 / math.sqrt(HEAD_SIZE)
    gain_part = lax.dynamic_slice_in_dim(norm_gain, tensor_index * width_part, width_part)
    x_float = tokens.astype(jnp.float32)

    block_count = block_owner.shape[1]
    owner_row = lax.dynamic_slice_in_dim(block_owner, data_index, 1, 0)[0]
    slot_index = jnp.arange(sources, dtype=jnp.int32)
    send_table = (owner_row[None, :] == slot_index[:, None]).astype(jnp.bfloat16)

    home_rows = token_row_count // block_count
    owned_blocks = grad_output.reshape(block_count, home_rows, width_part)
    if sources <= 16:
        returned = [lax.dynamic_index_in_dim(owned_blocks, data_index, 0, keepdims=False)]
        for shift in range(1, sources):
            pairs = [(a, (a + shift) % sources) for a in range(sources)]
            piece = lax.dynamic_index_in_dim(
                owned_blocks, (data_index + shift) % sources, 0, keepdims=False
            )
            returned.append(lax.ppermute(piece, "dp", pairs))
        returned = jnp.stack(returned)
        came_over = (
            ((data_index - owner_row) % sources)[:, None] == slot_index[None, :]
        ).astype(jnp.bfloat16)
        grad_home = (
            jnp.einsum("js,srw->jrw", came_over, returned, preferred_element_type=jnp.float32)
            .astype(jnp.bfloat16)
            .reshape(token_row_count, width_part)
        )
    else:
        arrived = lax.all_to_all(
            owned_blocks.reshape(block_count, -1), "dp", split_axis=0, concat_axis=0, tiled=True
        )
        grad_home = (
            lax.dot_general(
                send_table, arrived, (((0,), (0,)), ((), ())), preferred_element_type=jnp.float32
            )
            .astype(jnp.bfloat16)
            .reshape(token_row_count, width_part)
        )

    gathered = lax.all_gather(tokens, "tensor", axis=1, tiled=True)
    gathered_float = gathered.astype(jnp.float32)
    inverse = lax.rsqrt(jnp.mean(gathered_float * gathered_float, axis=1) + NORM_EPSILON)
    normed_input = (gathered_float * inverse[:, None] * norm_gain[None, :]).astype(jnp.bfloat16)
    query_raw = jnp.dot(normed_input, w_query, preferred_element_type=jnp.float32)
    key_raw = jnp.dot(normed_input, key_weight, preferred_element_type=jnp.float32)
    value_raw = jnp.dot(normed_input, value_weight, preferred_element_type=jnp.float32)
    doc_ids, positions = doc_tables(doc_lengths[0], token_row_count)
    token_index = jnp.arange(token_row_count, dtype=jnp.int32)
    allowed = (doc_ids[:, None] == doc_ids[None, :]) & (
        token_index[None, :] <= token_index[:, None]
    )
    cosine, sine_table = rope_tables(positions, HEAD_SIZE)
    query_rows = rotate(
        query_raw.reshape(token_row_count, heads_local, HEAD_SIZE), cosine, sine_table
    ).astype(jnp.bfloat16)
    keys = rotate(
        key_raw.reshape(token_row_count, kv_local, HEAD_SIZE), cosine, sine_table
    ).astype(jnp.bfloat16)
    value_rows = value_raw.astype(jnp.bfloat16).reshape(token_row_count, kv_local, HEAD_SIZE)
    grouped_query = query_rows.reshape(token_row_count, kv_local, query_group_width, HEAD_SIZE)
    scores = (
        jnp.einsum("qkgd,skd->kgqs", grouped_query, keys, preferred_element_type=jnp.float32)
        * scale_factor
    )
    weights = jnp.where(allowed[None, None], jnp.exp(scores), 0.0)
    probs = weights / jnp.sum(weights, axis=-1, keepdims=True)
    probs_low = probs.astype(jnp.bfloat16)
    attended = jnp.einsum(
        "kgqs,skd->qkgd", probs_low, value_rows, preferred_element_type=jnp.float32
    ).astype(jnp.bfloat16)
    attended_flat = attended.reshape(token_row_count, query_width)
    mixed_partial = jnp.dot(attended_flat, w_out, preferred_element_type=jnp.float32)
    mixed, _ = scatter_features(mixed_partial, "tensor", tensor_size, tensor_index)
    output_home = (x_float + mixed).astype(jnp.bfloat16)
    grad_full = lax.all_gather(grad_home, "tensor", axis=1, tiled=True)
    attended_gradient = lax.dot_general(
        grad_full,
        w_out,
        (((1,), (1,)), ((), ())),
        preferred_element_type=jnp.float32,
    ).astype(jnp.bfloat16)
    grouped_gradient = attended_gradient.reshape(
        token_row_count, kv_local, query_group_width, HEAD_SIZE
    )
    delta = jnp.sum(grouped_gradient.astype(jnp.float32) * attended.astype(jnp.float32), axis=-1)
    grad_probs = jnp.einsum(
        "qkgd,skd->kgqs", grouped_gradient, value_rows, preferred_element_type=jnp.float32
    )
    grad_scores = (probs * (grad_probs - jnp.transpose(delta, (1, 2, 0))[..., None])).astype(
        jnp.bfloat16
    )
    grad_query_rot = (
        jnp.einsum("kgqs,skd->qkgd", grad_scores, keys, preferred_element_type=jnp.float32)
        * scale_factor
    )
    grad_keys_rot = (
        jnp.einsum("kgqs,qkgd->skd", grad_scores, grouped_query, preferred_element_type=jnp.float32)
        * scale_factor
    )
    value_gradient = jnp.einsum(
        "kgqs,qkgd->skd", probs_low, grouped_gradient, preferred_element_type=jnp.float32
    )
    grad_query = unrotate(
        grad_query_rot.reshape(token_row_count, heads_local, HEAD_SIZE), cosine, sine_table
    ).astype(jnp.bfloat16)
    key_gradient = unrotate(grad_keys_rot, cosine, sine_table).astype(jnp.bfloat16)
    output_home, grad_query, key_gradient, value_gradient = lax.optimization_barrier(
        (output_home, grad_query, key_gradient, value_gradient)
    )
    home_blocks = output_home.reshape(block_count, home_rows, width_part)
    outgoing = jnp.einsum(
        "dj,jrw->drw", send_table, home_blocks, preferred_element_type=jnp.float32
    ).astype(jnp.bfloat16)
    relaid = lax.all_to_all(outgoing, "dp", split_axis=0, concat_axis=0, tiled=True).reshape(
        token_row_count, width_part
    )

    contract_out = (((1,), (1,)), ((), ()))
    normed_partial = (
        lax.dot_general(
            grad_query.reshape(token_row_count, query_width),
            w_query,
            contract_out,
            preferred_element_type=jnp.float32,
        )
        + lax.dot_general(
            key_gradient.reshape(token_row_count, key_width),
            key_weight,
            contract_out,
            preferred_element_type=jnp.float32,
        )
        + lax.dot_general(
            value_gradient.astype(jnp.bfloat16).reshape(token_row_count, key_width),
            value_weight,
            contract_out,
            preferred_element_type=jnp.float32,
        )
    )
    stat_partial = jnp.sum(normed_partial * norm_gain[None, :] * gathered_float, axis=1)
    normed_gradient, stat_sum = scatter_features(
        normed_partial, "tensor", tensor_size, tensor_index, extra=stat_partial
    )
    stat = stat_sum / full_width
    cubed = inverse * inverse * inverse
    grad_x = (
        grad_home.astype(jnp.float32)
        + inverse[:, None] * gain_part[None, :] * normed_gradient
        - x_float * cubed[:, None] * stat[:, None]
    )
    return (relaid, grad_x.astype(jnp.bfloat16))


def solution(mesh):
    placed = (
        P("dp", "tensor"),
        P(),
        P(None, "tensor"),
        P(None, "tensor"),
        P(None, "tensor"),
        P("tensor", None),
        P("dp", "tensor"),
        P("dp", None),
        P(),
    )
    return jax.shard_map(
        per_device,
        mesh=mesh,
        in_specs=placed,
        out_specs=(P("dp", "tensor"), P("dp", "tensor")),
        check_vma=False,
    )
```

```python
import math

import jax
import jax.numpy as jnp
from jax import lax
from jax.sharding import PartitionSpec as P

HEAD_SIZE = 128


ROPE_BASE = 500000.0
NORM_EPSILON = 1e-05


def doc_tables(lengths_row, token_row_count):
    ends = jnp.cumsum(lengths_row)
    token_index = jnp.arange(token_row_count, dtype=jnp.int32)
    passed = (token_index[:, None] >= ends[None, :]).astype(jnp.int32)
    doc_ids = jnp.sum(passed, axis=1)
    starts = jnp.max(jnp.where(passed > 0, ends[None, :], 0), axis=1)
    return (doc_ids, token_index - starts)


def rope_tables(positions, head_size):
    half_dim = head_size // 2
    steps = jnp.arange(half_dim, dtype=jnp.float32)
    inverse_freq = jnp.power(ROPE_BASE, -2.0 * steps / head_size)
    angles = positions.astype(jnp.float32)[:, None] * inverse_freq[None, :]
    return (jnp.cos(angles), jnp.sin(angles))


def rotate(vectors, cosine, sine_table):
    half_dim = vectors.shape[-1] // 2
    former = vectors[..., :half_dim]
    latter = vectors[..., half_dim:]
    cos_part = cosine[:, None, :]
    sin_part = sine_table[:, None, :]
    return jnp.concatenate(
        [former * cos_part - latter * sin_part, latter * cos_part + former * sin_part], axis=-1
    )


def unrotate(vectors, cosine, sine_table):
    half_dim = vectors.shape[-1] // 2
    former = vectors[..., :half_dim]
    latter = vectors[..., half_dim:]
    cos_part = cosine[:, None, :]
    sin_part = sine_table[:, None, :]
    return jnp.concatenate(
        [former * cos_part + latter * sin_part, latter * cos_part - former * sin_part], axis=-1
    )


def _is_pow2(n):
    return n > 1 and (n & (n - 1)) == 0


def _xor_pairs(size, bit):
    return [(i, i ^ bit) for i in range(size)]


def gather_features(shard, axis_name, size, position):
    if not _is_pow2(size):
        return lax.all_gather(shard, axis_name, axis=1, tiled=True)
    held = shard[None]
    masks = [0]
    bit = size >> 1
    while bit:
        incoming = lax.ppermute(held, axis_name, _xor_pairs(size, bit))
        held = jnp.concatenate([held, incoming], axis=0)
        masks = masks + [m ^ bit for m in masks]
        bit >>= 1
    table = jnp.asarray([masks.index(m) for m in range(size)], jnp.int32)
    blocks = [
        lax.dynamic_index_in_dim(held, table[s ^ position], axis=0, keepdims=False)
        for s in range(size)
    ]
    return jnp.concatenate(blocks, axis=1)


def scatter_features(partial, axis_name, size, position, extra=None):
    width = partial.shape[1] // size
    if not _is_pow2(size):
        summed = lax.psum_scatter(
            partial.astype(jnp.bfloat16), axis_name, scatter_dimension=1, tiled=True
        )
        if extra is not None:
            extra = lax.psum(extra, axis_name)
        return summed.astype(jnp.float32), extra
    held = [
        lax.dynamic_slice_in_dim(partial, (position ^ m) * width, width, axis=1)
        for m in range(size)
    ]
    masks = list(range(size))
    bit = 1
    while bit < size:
        keep = [i for i, m in enumerate(masks) if not m & bit]
        send = [i for i, m in enumerate(masks) if m & bit]
        outgoing = jnp.stack([held[i] for i in send]).astype(jnp.bfloat16)
        if extra is None:
            incoming = lax.ppermute(outgoing, axis_name, _xor_pairs(size, bit))
        else:
            incoming, extra_in = lax.ppermute((outgoing, extra), axis_name, _xor_pairs(size, bit))
            extra = extra + extra_in
        sent_masks = [masks[i] ^ bit for i in send]
        held = [
            held[i] + incoming[sent_masks.index(masks[i])].astype(jnp.float32) for i in keep
        ]
        masks = [masks[i] for i in keep]
        bit <<= 1
    return held[0], extra


def per_device(
    tokens,
    norm_gain,
    w_query,
    key_weight,
    value_weight,
    w_out,
    grad_output,
    doc_lengths,
    block_owner,
):
    token_row_count, width_part = tokens.shape
    full_width = norm_gain.shape[0]
    sources = lax.axis_size("dp")
    tensor_size = lax.axis_size("tensor")
    data_index = lax.axis_index("dp")
    tensor_index = lax.axis_index("tensor")
    query_width = w_query.shape[1]
    key_width = key_weight.shape[1]
    heads_local = query_width // HEAD_SIZE
    kv_local = key_width // HEAD_SIZE
    query_group_width = heads_local // kv_local
    scale_factor = 1.0 / math.sqrt(HEAD_SIZE)
    gain_part = lax.dynamic_slice_in_dim(norm_gain, tensor_index * width_part, width_part)
    x_float = tokens.astype(jnp.float32)

    block_count = block_owner.shape[1]
    owner_row = lax.dynamic_slice_in_dim(block_owner, data_index, 1, 0)[0]
    slot_index = jnp.arange(sources, dtype=jnp.int32)
    send_table = (owner_row[None, :] == slot_index[:, None]).astype(jnp.bfloat16)

    home_rows = token_row_count // block_count
    owned_blocks = grad_output.reshape(block_count, home_rows, width_part)
    if sources <= 16:
        returned = [lax.dynamic_index_in_dim(owned_blocks, data_index, 0, keepdims=False)]
        for shift in range(1, sources):
            pairs = [(a, (a + shift) % sources) for a in range(sources)]
            piece = lax.dynamic_index_in_dim(
                owned_blocks, (data_index + shift) % sources, 0, keepdims=False
            )
            returned.append(lax.ppermute(piece, "dp", pairs))
        returned = jnp.stack(returned)
        came_over = (
            ((data_index - owner_row) % sources)[:, None] == slot_index[None, :]
        ).astype(jnp.bfloat16)
        grad_home = (
            jnp.einsum("js,srw->jrw", came_over, returned, preferred_element_type=jnp.float32)
            .astype(jnp.bfloat16)
            .reshape(token_row_count, width_part)
        )
    else:
        arrived = lax.all_to_all(
            owned_blocks.reshape(block_count, -1), "dp", split_axis=0, concat_axis=0, tiled=True
        )
        grad_home = (
            lax.dot_general(
                send_table, arrived, (((0,), (0,)), ((), ())), preferred_element_type=jnp.float32
            )
            .astype(jnp.bfloat16)
            .reshape(token_row_count, width_part)
        )

    gathered = lax.all_gather(tokens, "tensor", axis=1, tiled=True)
    gathered_float = gathered.astype(jnp.float32)
    inverse = lax.rsqrt(jnp.mean(gathered_float * gathered_float, axis=1) + NORM_EPSILON)
    normed_input = (gathered_float * inverse[:, None] * norm_gain[None, :]).astype(jnp.bfloat16)
    query_raw = jnp.dot(normed_input, w_query, preferred_element_type=jnp.float32)
    key_raw = jnp.dot(normed_input, key_weight, preferred_element_type=jnp.float32)
    value_raw = jnp.dot(normed_input, value_weight, preferred_element_type=jnp.float32)
    doc_ids, positions = doc_tables(doc_lengths[0], token_row_count)
    token_index = jnp.arange(token_row_count, dtype=jnp.int32)
    allowed = (doc_ids[:, None] == doc_ids[None, :]) & (
        token_index[None, :] <= token_index[:, None]
    )
    cosine, sine_table = rope_tables(positions, HEAD_SIZE)
    query_rows = rotate(
        query_raw.reshape(token_row_count, heads_local, HEAD_SIZE), cosine, sine_table
    ).astype(jnp.bfloat16)
    keys = rotate(
        key_raw.reshape(token_row_count, kv_local, HEAD_SIZE), cosine, sine_table
    ).astype(jnp.bfloat16)
    value_rows = value_raw.astype(jnp.bfloat16).reshape(token_row_count, kv_local, HEAD_SIZE)
    grouped_query = query_rows.reshape(token_row_count, kv_local, query_group_width, HEAD_SIZE)
    scores = (
        jnp.einsum("qkgd,skd->kgqs", grouped_query, keys, preferred_element_type=jnp.float32)
        * scale_factor
    )
    weights = jnp.where(allowed[None, None], jnp.exp(scores), 0.0)
    probs = weights / jnp.sum(weights, axis=-1, keepdims=True)
    probs_low = probs.astype(jnp.bfloat16)
    attended = jnp.einsum(
        "kgqs,skd->qkgd", probs_low, value_rows, preferred_element_type=jnp.float32
    ).astype(jnp.bfloat16)
    attended_flat = attended.reshape(token_row_count, query_width)
    mixed_partial = jnp.dot(attended_flat, w_out, preferred_element_type=jnp.float32)
    mixed, _ = scatter_features(mixed_partial, "tensor", tensor_size, tensor_index)
    output_home = (x_float + mixed).astype(jnp.bfloat16)
    grad_full = lax.all_gather(grad_home, "tensor", axis=1, tiled=True)
    attended_gradient = lax.dot_general(
        grad_full,
        w_out,
        (((1,), (1,)), ((), ())),
        preferred_element_type=jnp.float32,
    ).astype(jnp.bfloat16)
    grouped_gradient = attended_gradient.reshape(
        token_row_count, kv_local, query_group_width, HEAD_SIZE
    )
    delta = jnp.sum(grouped_gradient.astype(jnp.float32) * attended.astype(jnp.float32), axis=-1)
    grad_probs = jnp.einsum(
        "qkgd,skd->kgqs", grouped_gradient, value_rows, preferred_element_type=jnp.float32
    )
    grad_scores = (probs * (grad_probs - jnp.transpose(delta, (1, 2, 0))[..., None])).astype(
        jnp.bfloat16
    )
    grad_query_rot = (
        jnp.einsum("kgqs,skd->qkgd", grad_scores, keys, preferred_element_type=jnp.float32)
        * scale_factor
    )
    grad_keys_rot = (
        jnp.einsum("kgqs,qkgd->skd", grad_scores, grouped_query, preferred_element_type=jnp.float32)
        * scale_factor
    )
    value_gradient = jnp.einsum(
        "kgqs,qkgd->skd", probs_low, grouped_gradient, preferred_element_type=jnp.float32
    )
    grad_query = unrotate(
        grad_query_rot.reshape(token_row_count, heads_local, HEAD_SIZE), cosine, sine_table
    ).astype(jnp.bfloat16)
    key_gradient = unrotate(grad_keys_rot, cosine, sine_table).astype(jnp.bfloat16)
    contract_out = (((1,), (1,)), ((), ()))
    normed_partial = (
        lax.dot_general(
            grad_query.reshape(token_row_count, query_width),
            w_query,
            contract_out,
            preferred_element_type=jnp.float32,
        )
        + lax.dot_general(
            key_gradient.reshape(token_row_count, key_width),
            key_weight,
            contract_out,
            preferred_element_type=jnp.float32,
        )
        + lax.dot_general(
            value_gradient.astype(jnp.bfloat16).reshape(token_row_count, key_width),
            value_weight,
            contract_out,
            preferred_element_type=jnp.float32,
        )
    )
    output_home, normed_partial = lax.optimization_barrier((output_home, normed_partial))
    stat_partial = jnp.sum(normed_partial * norm_gain[None, :] * gathered_float, axis=1)
    home_blocks = output_home.reshape(block_count, home_rows, width_part)
    outgoing = jnp.einsum(
        "dj,jrw->drw", send_table, home_blocks, preferred_element_type=jnp.float32
    ).astype(jnp.bfloat16)
    relaid = lax.all_to_all(outgoing, "dp", split_axis=0, concat_axis=0, tiled=True).reshape(
        token_row_count, width_part
    )

    normed_gradient, stat_sum = scatter_features(
        normed_partial, "tensor", tensor_size, tensor_index, extra=stat_partial
    )
    stat = stat_sum / full_width
    cubed = inverse * inverse * inverse
    grad_x = (
        grad_home.astype(jnp.float32)
        + inverse[:, None] * gain_part[None, :] * normed_gradient
        - x_float * cubed[:, None] * stat[:, None]
    )
    return (relaid, grad_x.astype(jnp.bfloat16))


def solution(mesh):
    placed = (
        P("dp", "tensor"),
        P(),
        P(None, "tensor"),
        P(None, "tensor"),
        P(None, "tensor"),
        P("tensor", None),
        P("dp", "tensor"),
        P("dp", None),
        P(),
    )
    return jax.shard_map(
        per_device,
        mesh=mesh,
        in_specs=placed,
        out_specs=(P("dp", "tensor"), P("dp", "tensor")),
        check_vma=False,
    )
```

```python
import math

import jax
import jax.numpy as jnp
from jax import lax
from jax.sharding import PartitionSpec as P

HEAD_SIZE = 128


ROPE_BASE = 500000.0
NORM_EPSILON = 1e-05


def doc_tables(lengths_row, token_row_count):
    ends = jnp.cumsum(lengths_row)
    token_index = jnp.arange(token_row_count, dtype=jnp.int32)
    passed = (token_index[:, None] >= ends[None, :]).astype(jnp.int32)
    doc_ids = jnp.sum(passed, axis=1)
    starts = jnp.max(jnp.where(passed > 0, ends[None, :], 0), axis=1)
    return (doc_ids, token_index - starts)


def rope_tables(positions, head_size):
    half_dim = head_size // 2
    steps = jnp.arange(half_dim, dtype=jnp.float32)
    inverse_freq = jnp.power(ROPE_BASE, -2.0 * steps / head_size)
    angles = positions.astype(jnp.float32)[:, None] * inverse_freq[None, :]
    return (jnp.cos(angles), jnp.sin(angles))


def rotate(vectors, cosine, sine_table):
    half_dim = vectors.shape[-1] // 2
    former = vectors[..., :half_dim]
    latter = vectors[..., half_dim:]
    cos_part = cosine[:, None, :]
    sin_part = sine_table[:, None, :]
    return jnp.concatenate(
        [former * cos_part - latter * sin_part, latter * cos_part + former * sin_part], axis=-1
    )


def unrotate(vectors, cosine, sine_table):
    half_dim = vectors.shape[-1] // 2
    former = vectors[..., :half_dim]
    latter = vectors[..., half_dim:]
    cos_part = cosine[:, None, :]
    sin_part = sine_table[:, None, :]
    return jnp.concatenate(
        [former * cos_part + latter * sin_part, latter * cos_part - former * sin_part], axis=-1
    )


def _is_pow2(n):
    return n > 1 and (n & (n - 1)) == 0


def _xor_pairs(size, bit):
    return [(i, i ^ bit) for i in range(size)]


def gather_features(shard, axis_name, size, position):
    if not _is_pow2(size):
        return lax.all_gather(shard, axis_name, axis=1, tiled=True)
    held = shard[None]
    masks = [0]
    bit = size >> 1
    while bit:
        incoming = lax.ppermute(held, axis_name, _xor_pairs(size, bit))
        held = jnp.concatenate([held, incoming], axis=0)
        masks = masks + [m ^ bit for m in masks]
        bit >>= 1
    table = jnp.asarray([masks.index(m) for m in range(size)], jnp.int32)
    blocks = [
        lax.dynamic_index_in_dim(held, table[s ^ position], axis=0, keepdims=False)
        for s in range(size)
    ]
    return jnp.concatenate(blocks, axis=1)


def scatter_features(partial, axis_name, size, position, extra=None):
    width = partial.shape[1] // size
    if not _is_pow2(size):
        summed = lax.psum_scatter(
            partial.astype(jnp.bfloat16), axis_name, scatter_dimension=1, tiled=True
        )
        if extra is not None:
            extra = lax.psum(extra, axis_name)
        return summed.astype(jnp.float32), extra
    held = [
        lax.dynamic_slice_in_dim(partial, (position ^ m) * width, width, axis=1)
        for m in range(size)
    ]
    masks = list(range(size))
    bit = 1
    while bit < size:
        keep = [i for i, m in enumerate(masks) if not m & bit]
        send = [i for i, m in enumerate(masks) if m & bit]
        outgoing = jnp.stack([held[i] for i in send]).astype(jnp.bfloat16)
        if extra is None:
            incoming = lax.ppermute(outgoing, axis_name, _xor_pairs(size, bit))
        else:
            incoming, extra_in = lax.ppermute((outgoing, extra), axis_name, _xor_pairs(size, bit))
            extra = extra + extra_in
        sent_masks = [masks[i] ^ bit for i in send]
        held = [
            held[i] + incoming[sent_masks.index(masks[i])].astype(jnp.float32) for i in keep
        ]
        masks = [masks[i] for i in keep]
        bit <<= 1
    return held[0], extra


def per_device(
    tokens,
    norm_gain,
    w_query,
    key_weight,
    value_weight,
    w_out,
    grad_output,
    doc_lengths,
    block_owner,
):
    token_row_count, width_part = tokens.shape
    full_width = norm_gain.shape[0]
    sources = lax.axis_size("dp")
    tensor_size = lax.axis_size("tensor")
    data_index = lax.axis_index("dp")
    tensor_index = lax.axis_index("tensor")
    query_width = w_query.shape[1]
    key_width = key_weight.shape[1]
    heads_local = query_width // HEAD_SIZE
    kv_local = key_width // HEAD_SIZE
    query_group_width = heads_local // kv_local
    scale_factor = 1.0 / math.sqrt(HEAD_SIZE)
    gain_part = lax.dynamic_slice_in_dim(norm_gain, tensor_index * width_part, width_part)
    x_float = tokens.astype(jnp.float32)

    block_count = block_owner.shape[1]
    owner_row = lax.dynamic_slice_in_dim(block_owner, data_index, 1, 0)[0]
    slot_index = jnp.arange(sources, dtype=jnp.int32)
    send_table = (owner_row[None, :] == slot_index[:, None]).astype(jnp.bfloat16)

    home_rows = token_row_count // block_count
    owned_blocks = grad_output.reshape(block_count, home_rows, width_part)
    if sources <= 16:
        returned = [lax.dynamic_index_in_dim(owned_blocks, data_index, 0, keepdims=False)]
        for shift in range(1, sources):
            pairs = [(a, (a + shift) % sources) for a in range(sources)]
            piece = lax.dynamic_index_in_dim(
                owned_blocks, (data_index + shift) % sources, 0, keepdims=False
            )
            returned.append(lax.ppermute(piece, "dp", pairs))
        returned = jnp.stack(returned)
        came_over = (
            ((data_index - owner_row) % sources)[:, None] == slot_index[None, :]
        ).astype(jnp.bfloat16)
        grad_home = (
            jnp.einsum("js,srw->jrw", came_over, returned, preferred_element_type=jnp.float32)
            .astype(jnp.bfloat16)
            .reshape(token_row_count, width_part)
        )
    else:
        arrived = lax.all_to_all(
            owned_blocks.reshape(block_count, -1), "dp", split_axis=0, concat_axis=0, tiled=True
        )
        grad_home = (
            lax.dot_general(
                send_table, arrived, (((0,), (0,)), ((), ())), preferred_element_type=jnp.float32
            )
            .astype(jnp.bfloat16)
            .reshape(token_row_count, width_part)
        )

    gathered = lax.all_gather(tokens, "tensor", axis=1, tiled=True)
    gathered_float = gathered.astype(jnp.float32)
    inverse = lax.rsqrt(jnp.mean(gathered_float * gathered_float, axis=1) + NORM_EPSILON)
    normed_input = (gathered_float * inverse[:, None] * norm_gain[None, :]).astype(jnp.bfloat16)
    query_raw = jnp.dot(normed_input, w_query, preferred_element_type=jnp.float32)
    key_raw = jnp.dot(normed_input, key_weight, preferred_element_type=jnp.float32)
    value_raw = jnp.dot(normed_input, value_weight, preferred_element_type=jnp.float32)
    doc_ids, positions = doc_tables(doc_lengths[0], token_row_count)
    token_index = jnp.arange(token_row_count, dtype=jnp.int32)
    allowed = (doc_ids[:, None] == doc_ids[None, :]) & (
        token_index[None, :] <= token_index[:, None]
    )
    cosine, sine_table = rope_tables(positions, HEAD_SIZE)
    query_rows = rotate(
        query_raw.reshape(token_row_count, heads_local, HEAD_SIZE), cosine, sine_table
    ).astype(jnp.bfloat16)
    keys = rotate(
        key_raw.reshape(token_row_count, kv_local, HEAD_SIZE), cosine, sine_table
    ).astype(jnp.bfloat16)
    value_rows = value_raw.astype(jnp.bfloat16).reshape(token_row_count, kv_local, HEAD_SIZE)
    grouped_query = query_rows.reshape(token_row_count, kv_local, query_group_width, HEAD_SIZE)
    scores = (
        jnp.einsum("qkgd,skd->kgqs", grouped_query, keys, preferred_element_type=jnp.float32)
        * scale_factor
    )
    weights = jnp.where(allowed[None, None], jnp.exp(scores), 0.0)
    probs = weights / jnp.sum(weights, axis=-1, keepdims=True)
    probs_low = probs.astype(jnp.bfloat16)
    attended = jnp.einsum(
        "kgqs,skd->qkgd", probs_low, value_rows, preferred_element_type=jnp.float32
    ).astype(jnp.bfloat16)
    attended_flat = attended.reshape(token_row_count, query_width)
    mixed_partial = jnp.dot(attended_flat, w_out, preferred_element_type=jnp.float32)
    grad_full = lax.all_gather(grad_home, "tensor", axis=1, tiled=True)
    mixed_partial, grad_full = lax.optimization_barrier((mixed_partial, grad_full))
    mixed, _ = scatter_features(mixed_partial, "tensor", tensor_size, tensor_index)
    output_home = (x_float + mixed).astype(jnp.bfloat16)
    attended_gradient = lax.dot_general(
        grad_full,
        w_out,
        (((1,), (1,)), ((), ())),
        preferred_element_type=jnp.float32,
    ).astype(jnp.bfloat16)
    grouped_gradient = attended_gradient.reshape(
        token_row_count, kv_local, query_group_width, HEAD_SIZE
    )
    delta = jnp.sum(grouped_gradient.astype(jnp.float32) * attended.astype(jnp.float32), axis=-1)
    grad_probs = jnp.einsum(
        "qkgd,skd->kgqs", grouped_gradient, value_rows, preferred_element_type=jnp.float32
    )
    grad_scores = (probs * (grad_probs - jnp.transpose(delta, (1, 2, 0))[..., None])).astype(
        jnp.bfloat16
    )
    grad_query_rot = (
        jnp.einsum("kgqs,skd->qkgd", grad_scores, keys, preferred_element_type=jnp.float32)
        * scale_factor
    )
    grad_keys_rot = (
        jnp.einsum("kgqs,qkgd->skd", grad_scores, grouped_query, preferred_element_type=jnp.float32)
        * scale_factor
    )
    value_gradient = jnp.einsum(
        "kgqs,qkgd->skd", probs_low, grouped_gradient, preferred_element_type=jnp.float32
    )
    grad_query = unrotate(
        grad_query_rot.reshape(token_row_count, heads_local, HEAD_SIZE), cosine, sine_table
    ).astype(jnp.bfloat16)
    key_gradient = unrotate(grad_keys_rot, cosine, sine_table).astype(jnp.bfloat16)
    contract_out = (((1,), (1,)), ((), ()))
    normed_partial = (
        lax.dot_general(
            grad_query.reshape(token_row_count, query_width),
            w_query,
            contract_out,
            preferred_element_type=jnp.float32,
        )
        + lax.dot_general(
            key_gradient.reshape(token_row_count, key_width),
            key_weight,
            contract_out,
            preferred_element_type=jnp.float32,
        )
        + lax.dot_general(
            value_gradient.astype(jnp.bfloat16).reshape(token_row_count, key_width),
            value_weight,
            contract_out,
            preferred_element_type=jnp.float32,
        )
    )
    output_home, normed_partial = lax.optimization_barrier((output_home, normed_partial))
    stat_partial = jnp.sum(normed_partial * norm_gain[None, :] * gathered_float, axis=1)
    home_blocks = output_home.reshape(block_count, home_rows, width_part)
    outgoing = jnp.einsum(
        "dj,jrw->drw", send_table, home_blocks, preferred_element_type=jnp.float32
    ).astype(jnp.bfloat16)
    relaid = lax.all_to_all(outgoing, "dp", split_axis=0, concat_axis=0, tiled=True).reshape(
        token_row_count, width_part
    )

    normed_gradient, stat_sum = scatter_features(
        normed_partial, "tensor", tensor_size, tensor_index, extra=stat_partial
    )
    stat = stat_sum / full_width
    cubed = inverse * inverse * inverse
    grad_x = (
        grad_home.astype(jnp.float32)
        + inverse[:, None] * gain_part[None, :] * normed_gradient
        - x_float * cubed[:, None] * stat[:, None]
    )
    return (relaid, grad_x.astype(jnp.bfloat16))


def solution(mesh):
    placed = (
        P("dp", "tensor"),
        P(),
        P(None, "tensor"),
        P(None, "tensor"),
        P(None, "tensor"),
        P("tensor", None),
        P("dp", "tensor"),
        P("dp", None),
        P(),
    )
    return jax.shard_map(
        per_device,
        mesh=mesh,
        in_specs=placed,
        out_specs=(P("dp", "tensor"), P("dp", "tensor")),
        check_vma=False,
    )
```

```python
import math

import jax
import jax.numpy as jnp
from jax import lax
from jax.sharding import PartitionSpec as P

HEAD_SIZE = 128


ROPE_BASE = 500000.0
NORM_EPSILON = 1e-05


def doc_tables(lengths_row, token_row_count):
    ends = jnp.cumsum(lengths_row)
    token_index = jnp.arange(token_row_count, dtype=jnp.int32)
    passed = (token_index[:, None] >= ends[None, :]).astype(jnp.int32)
    doc_ids = jnp.sum(passed, axis=1)
    starts = jnp.max(jnp.where(passed > 0, ends[None, :], 0), axis=1)
    return (doc_ids, token_index - starts)


def rope_tables(positions, head_size):
    half_dim = head_size // 2
    steps = jnp.arange(half_dim, dtype=jnp.float32)
    inverse_freq = jnp.power(ROPE_BASE, -2.0 * steps / head_size)
    angles = positions.astype(jnp.float32)[:, None] * inverse_freq[None, :]
    return (jnp.cos(angles), jnp.sin(angles))


def rotate(vectors, cosine, sine_table):
    half_dim = vectors.shape[-1] // 2
    former = vectors[..., :half_dim]
    latter = vectors[..., half_dim:]
    cos_part = cosine[:, None, :]
    sin_part = sine_table[:, None, :]
    return jnp.concatenate(
        [former * cos_part - latter * sin_part, latter * cos_part + former * sin_part], axis=-1
    )


def unrotate(vectors, cosine, sine_table):
    half_dim = vectors.shape[-1] // 2
    former = vectors[..., :half_dim]
    latter = vectors[..., half_dim:]
    cos_part = cosine[:, None, :]
    sin_part = sine_table[:, None, :]
    return jnp.concatenate(
        [former * cos_part + latter * sin_part, latter * cos_part - former * sin_part], axis=-1
    )


def _is_pow2(n):
    return n > 1 and (n & (n - 1)) == 0


def _xor_pairs(size, bit):
    return [(i, i ^ bit) for i in range(size)]


def gather_features(shard, axis_name, size, position):
    if not _is_pow2(size):
        return lax.all_gather(shard, axis_name, axis=1, tiled=True)
    held = shard[None]
    masks = [0]
    bit = size >> 1
    while bit:
        incoming = lax.ppermute(held, axis_name, _xor_pairs(size, bit))
        held = jnp.concatenate([held, incoming], axis=0)
        masks = masks + [m ^ bit for m in masks]
        bit >>= 1
    table = jnp.asarray([masks.index(m) for m in range(size)], jnp.int32)
    blocks = [
        lax.dynamic_index_in_dim(held, table[s ^ position], axis=0, keepdims=False)
        for s in range(size)
    ]
    return jnp.concatenate(blocks, axis=1)


def scatter_features(partial, axis_name, size, position, extra=None, ties=()):
    width = partial.shape[1] // size
    if not _is_pow2(size):
        summed = lax.psum_scatter(
            partial.astype(jnp.bfloat16), axis_name, scatter_dimension=1, tiled=True
        )
        if extra is not None:
            extra = lax.psum(extra, axis_name)
        return summed.astype(jnp.float32), extra, ties
    held = [
        lax.dynamic_slice_in_dim(partial, (position ^ m) * width, width, axis=1)
        for m in range(size)
    ]
    masks = list(range(size))
    done_ties = []
    bit = 1
    while bit < size:
        keep = [i for i, m in enumerate(masks) if not m & bit]
        send = [i for i, m in enumerate(masks) if m & bit]
        outgoing = jnp.stack([held[i] for i in send]).astype(jnp.bfloat16)
        if extra is None:
            incoming = lax.ppermute(outgoing, axis_name, _xor_pairs(size, bit))
        else:
            incoming, extra_in = lax.ppermute((outgoing, extra), axis_name, _xor_pairs(size, bit))
            extra = extra + extra_in
        if ties:
            incoming, first = lax.optimization_barrier((incoming, ties[0]))
            ties = ties[1:]
            done_ties.append(first)
        sent_masks = [masks[i] ^ bit for i in send]
        held = [
            held[i] + incoming[sent_masks.index(masks[i])].astype(jnp.float32) for i in keep
        ]
        masks = [masks[i] for i in keep]
        bit <<= 1
    return held[0], extra, tuple(done_ties) + tuple(ties)


def per_device(
    tokens,
    norm_gain,
    w_query,
    key_weight,
    value_weight,
    w_out,
    grad_output,
    doc_lengths,
    block_owner,
):
    token_row_count, width_part = tokens.shape
    full_width = norm_gain.shape[0]
    sources = lax.axis_size("dp")
    tensor_size = lax.axis_size("tensor")
    data_index = lax.axis_index("dp")
    tensor_index = lax.axis_index("tensor")
    query_width = w_query.shape[1]
    key_width = key_weight.shape[1]
    heads_local = query_width // HEAD_SIZE
    kv_local = key_width // HEAD_SIZE
    query_group_width = heads_local // kv_local
    scale_factor = 1.0 / math.sqrt(HEAD_SIZE)
    gain_part = lax.dynamic_slice_in_dim(norm_gain, tensor_index * width_part, width_part)
    x_float = tokens.astype(jnp.float32)

    block_count = block_owner.shape[1]
    owner_row = lax.dynamic_slice_in_dim(block_owner, data_index, 1, 0)[0]
    slot_index = jnp.arange(sources, dtype=jnp.int32)
    send_table = (owner_row[None, :] == slot_index[:, None]).astype(jnp.bfloat16)

    home_rows = token_row_count // block_count
    owned_blocks = grad_output.reshape(block_count, home_rows, width_part)
    if sources <= 16:
        returned = [lax.dynamic_index_in_dim(owned_blocks, data_index, 0, keepdims=False)]
        for shift in range(1, sources):
            pairs = [(a, (a + shift) % sources) for a in range(sources)]
            piece = lax.dynamic_index_in_dim(
                owned_blocks, (data_index + shift) % sources, 0, keepdims=False
            )
            returned.append(lax.ppermute(piece, "dp", pairs))
        returned = jnp.stack(returned)
        came_over = (
            ((data_index - owner_row) % sources)[:, None] == slot_index[None, :]
        ).astype(jnp.bfloat16)
        grad_home = (
            jnp.einsum("js,srw->jrw", came_over, returned, preferred_element_type=jnp.float32)
            .astype(jnp.bfloat16)
            .reshape(token_row_count, width_part)
        )
    else:
        arrived = lax.all_to_all(
            owned_blocks.reshape(block_count, -1), "dp", split_axis=0, concat_axis=0, tiled=True
        )
        grad_home = (
            lax.dot_general(
                send_table, arrived, (((0,), (0,)), ((), ())), preferred_element_type=jnp.float32
            )
            .astype(jnp.bfloat16)
            .reshape(token_row_count, width_part)
        )

    gathered = lax.all_gather(tokens, "tensor", axis=1, tiled=True)
    gathered_float = gathered.astype(jnp.float32)
    inverse = lax.rsqrt(jnp.mean(gathered_float * gathered_float, axis=1) + NORM_EPSILON)
    normed_input = (gathered_float * inverse[:, None] * norm_gain[None, :]).astype(jnp.bfloat16)
    query_raw = jnp.dot(normed_input, w_query, preferred_element_type=jnp.float32)
    key_raw = jnp.dot(normed_input, key_weight, preferred_element_type=jnp.float32)
    value_raw = jnp.dot(normed_input, value_weight, preferred_element_type=jnp.float32)
    doc_ids, positions = doc_tables(doc_lengths[0], token_row_count)
    token_index = jnp.arange(token_row_count, dtype=jnp.int32)
    allowed = (doc_ids[:, None] == doc_ids[None, :]) & (
        token_index[None, :] <= token_index[:, None]
    )
    cosine, sine_table = rope_tables(positions, HEAD_SIZE)
    query_rows = rotate(
        query_raw.reshape(token_row_count, heads_local, HEAD_SIZE), cosine, sine_table
    ).astype(jnp.bfloat16)
    keys = rotate(
        key_raw.reshape(token_row_count, kv_local, HEAD_SIZE), cosine, sine_table
    ).astype(jnp.bfloat16)
    value_rows = value_raw.astype(jnp.bfloat16).reshape(token_row_count, kv_local, HEAD_SIZE)
    grouped_query = query_rows.reshape(token_row_count, kv_local, query_group_width, HEAD_SIZE)
    scores = (
        jnp.einsum("qkgd,skd->kgqs", grouped_query, keys, preferred_element_type=jnp.float32)
        * scale_factor
    )
    weights = jnp.where(allowed[None, None], jnp.exp(scores), 0.0)
    probs = weights / jnp.sum(weights, axis=-1, keepdims=True)
    probs_low = probs.astype(jnp.bfloat16)
    attended = jnp.einsum(
        "kgqs,skd->qkgd", probs_low, value_rows, preferred_element_type=jnp.float32
    ).astype(jnp.bfloat16)
    attended_flat = attended.reshape(token_row_count, query_width)
    mixed_partial = jnp.dot(attended_flat, w_out, preferred_element_type=jnp.float32)
    grad_full = lax.all_gather(grad_home, "tensor", axis=1, tiled=True)
    mixed_partial, grad_full = lax.optimization_barrier((mixed_partial, grad_full))
    attended_gradient = lax.dot_general(
        grad_full,
        w_out,
        (((1,), (1,)), ((), ())),
        preferred_element_type=jnp.float32,
    ).astype(jnp.bfloat16)
    mixed, _, (attended_gradient,) = scatter_features(
        mixed_partial, "tensor", tensor_size, tensor_index, ties=(attended_gradient,)
    )
    output_home = (x_float + mixed).astype(jnp.bfloat16)
    grouped_gradient = attended_gradient.reshape(
        token_row_count, kv_local, query_group_width, HEAD_SIZE
    )
    delta = jnp.sum(grouped_gradient.astype(jnp.float32) * attended.astype(jnp.float32), axis=-1)
    grad_probs = jnp.einsum(
        "qkgd,skd->kgqs", grouped_gradient, value_rows, preferred_element_type=jnp.float32
    )
    grad_scores = (probs * (grad_probs - jnp.transpose(delta, (1, 2, 0))[..., None])).astype(
        jnp.bfloat16
    )
    grad_query_rot = (
        jnp.einsum("kgqs,skd->qkgd", grad_scores, keys, preferred_element_type=jnp.float32)
        * scale_factor
    )
    grad_keys_rot = (
        jnp.einsum("kgqs,qkgd->skd", grad_scores, grouped_query, preferred_element_type=jnp.float32)
        * scale_factor
    )
    value_gradient = jnp.einsum(
        "kgqs,qkgd->skd", probs_low, grouped_gradient, preferred_element_type=jnp.float32
    )
    grad_query = unrotate(
        grad_query_rot.reshape(token_row_count, heads_local, HEAD_SIZE), cosine, sine_table
    ).astype(jnp.bfloat16)
    key_gradient = unrotate(grad_keys_rot, cosine, sine_table).astype(jnp.bfloat16)
    contract_out = (((1,), (1,)), ((), ()))
    normed_partial = (
        lax.dot_general(
            grad_query.reshape(token_row_count, query_width),
            w_query,
            contract_out,
            preferred_element_type=jnp.float32,
        )
        + lax.dot_general(
            key_gradient.reshape(token_row_count, key_width),
            key_weight,
            contract_out,
            preferred_element_type=jnp.float32,
        )
        + lax.dot_general(
            value_gradient.astype(jnp.bfloat16).reshape(token_row_count, key_width),
            value_weight,
            contract_out,
            preferred_element_type=jnp.float32,
        )
    )
    output_home, normed_partial = lax.optimization_barrier((output_home, normed_partial))
    stat_partial = jnp.sum(normed_partial * norm_gain[None, :] * gathered_float, axis=1)
    home_blocks = output_home.reshape(block_count, home_rows, width_part)
    outgoing = jnp.einsum(
        "dj,jrw->drw", send_table, home_blocks, preferred_element_type=jnp.float32
    ).astype(jnp.bfloat16)
    relaid = lax.all_to_all(outgoing, "dp", split_axis=0, concat_axis=0, tiled=True).reshape(
        token_row_count, width_part
    )

    normed_gradient, stat_sum, _ = scatter_features(
        normed_partial, "tensor", tensor_size, tensor_index, extra=stat_partial
    )
    stat = stat_sum / full_width
    cubed = inverse * inverse * inverse
    grad_x = (
        grad_home.astype(jnp.float32)
        + inverse[:, None] * gain_part[None, :] * normed_gradient
        - x_float * cubed[:, None] * stat[:, None]
    )
    return (relaid, grad_x.astype(jnp.bfloat16))


def solution(mesh):
    placed = (
        P("dp", "tensor"),
        P(),
        P(None, "tensor"),
        P(None, "tensor"),
        P(None, "tensor"),
        P("tensor", None),
        P("dp", "tensor"),
        P("dp", None),
        P(),
    )
    return jax.shard_map(
        per_device,
        mesh=mesh,
        in_specs=placed,
        out_specs=(P("dp", "tensor"), P("dp", "tensor")),
        check_vma=False,
    )
```

```python
import math

import jax
import jax.numpy as jnp
from jax import lax
from jax.sharding import PartitionSpec as P

HEAD_SIZE = 128


ROPE_BASE = 500000.0
NORM_EPSILON = 1e-05


def doc_tables(lengths_row, token_row_count):
    ends = jnp.cumsum(lengths_row)
    token_index = jnp.arange(token_row_count, dtype=jnp.int32)
    passed = (token_index[:, None] >= ends[None, :]).astype(jnp.int32)
    doc_ids = jnp.sum(passed, axis=1)
    starts = jnp.max(jnp.where(passed > 0, ends[None, :], 0), axis=1)
    return (doc_ids, token_index - starts)


def rope_tables(positions, head_size):
    half_dim = head_size // 2
    steps = jnp.arange(half_dim, dtype=jnp.float32)
    inverse_freq = jnp.power(ROPE_BASE, -2.0 * steps / head_size)
    angles = positions.astype(jnp.float32)[:, None] * inverse_freq[None, :]
    return (jnp.cos(angles), jnp.sin(angles))


def rotate(vectors, cosine, sine_table):
    half_dim = vectors.shape[-1] // 2
    former = vectors[..., :half_dim]
    latter = vectors[..., half_dim:]
    cos_part = cosine[:, None, :]
    sin_part = sine_table[:, None, :]
    return jnp.concatenate(
        [former * cos_part - latter * sin_part, latter * cos_part + former * sin_part], axis=-1
    )


def unrotate(vectors, cosine, sine_table):
    half_dim = vectors.shape[-1] // 2
    former = vectors[..., :half_dim]
    latter = vectors[..., half_dim:]
    cos_part = cosine[:, None, :]
    sin_part = sine_table[:, None, :]
    return jnp.concatenate(
        [former * cos_part + latter * sin_part, latter * cos_part - former * sin_part], axis=-1
    )


def _is_pow2(n):
    return n > 1 and (n & (n - 1)) == 0


def _xor_pairs(size, bit):
    return [(i, i ^ bit) for i in range(size)]


def gather_features(shard, axis_name, size, position):
    if not _is_pow2(size):
        return lax.all_gather(shard, axis_name, axis=1, tiled=True)
    held = shard[None]
    masks = [0]
    bit = size >> 1
    while bit:
        incoming = lax.ppermute(held, axis_name, _xor_pairs(size, bit))
        held = jnp.concatenate([held, incoming], axis=0)
        masks = masks + [m ^ bit for m in masks]
        bit >>= 1
    table = jnp.asarray([masks.index(m) for m in range(size)], jnp.int32)
    blocks = [
        lax.dynamic_index_in_dim(held, table[s ^ position], axis=0, keepdims=False)
        for s in range(size)
    ]
    return jnp.concatenate(blocks, axis=1)


def scatter_features(partial, axis_name, size, position, extra=None, ties=()):
    width = partial.shape[1] // size
    if not _is_pow2(size):
        summed = lax.psum_scatter(
            partial.astype(jnp.bfloat16), axis_name, scatter_dimension=1, tiled=True
        )
        if extra is not None:
            extra = lax.psum(extra, axis_name)
        return summed.astype(jnp.float32), extra, ties
    held = [
        lax.dynamic_slice_in_dim(partial, (position ^ m) * width, width, axis=1)
        for m in range(size)
    ]
    masks = list(range(size))
    done_ties = []
    bit = 1
    while bit < size:
        keep = [i for i, m in enumerate(masks) if not m & bit]
        send = [i for i, m in enumerate(masks) if m & bit]
        outgoing = jnp.stack([held[i] for i in send]).astype(jnp.bfloat16)
        if extra is None:
            incoming = lax.ppermute(outgoing, axis_name, _xor_pairs(size, bit))
        else:
            incoming, extra_in = lax.ppermute((outgoing, extra), axis_name, _xor_pairs(size, bit))
            extra = extra + extra_in
        if ties:
            incoming, first = lax.optimization_barrier((incoming, ties[0]))
            ties = ties[1:]
            done_ties.append(first)
        sent_masks = [masks[i] ^ bit for i in send]
        held = [
            held[i] + incoming[sent_masks.index(masks[i])].astype(jnp.float32) for i in keep
        ]
        masks = [masks[i] for i in keep]
        bit <<= 1
    return held[0], extra, tuple(done_ties) + tuple(ties)


def per_device(
    tokens,
    norm_gain,
    w_query,
    key_weight,
    value_weight,
    w_out,
    grad_output,
    doc_lengths,
    block_owner,
):
    token_row_count, width_part = tokens.shape
    full_width = norm_gain.shape[0]
    sources = lax.axis_size("dp")
    tensor_size = lax.axis_size("tensor")
    data_index = lax.axis_index("dp")
    tensor_index = lax.axis_index("tensor")
    query_width = w_query.shape[1]
    key_width = key_weight.shape[1]
    heads_local = query_width // HEAD_SIZE
    kv_local = key_width // HEAD_SIZE
    query_group_width = heads_local // kv_local
    scale_factor = 1.0 / math.sqrt(HEAD_SIZE)
    gain_part = lax.dynamic_slice_in_dim(norm_gain, tensor_index * width_part, width_part)
    x_float = tokens.astype(jnp.float32)

    block_count = block_owner.shape[1]
    owner_row = lax.dynamic_slice_in_dim(block_owner, data_index, 1, 0)[0]
    slot_index = jnp.arange(sources, dtype=jnp.int32)
    send_table = (owner_row[None, :] == slot_index[:, None]).astype(jnp.bfloat16)

    home_rows = token_row_count // block_count
    owned_blocks = grad_output.reshape(block_count, home_rows, width_part)
    if sources <= 16:
        returned = [lax.dynamic_index_in_dim(owned_blocks, data_index, 0, keepdims=False)]
        for shift in range(1, sources):
            pairs = [(a, (a + shift) % sources) for a in range(sources)]
            piece = lax.dynamic_index_in_dim(
                owned_blocks, (data_index + shift) % sources, 0, keepdims=False
            )
            returned.append(lax.ppermute(piece, "dp", pairs))
        returned = jnp.stack(returned)
        came_over = (
            ((data_index - owner_row) % sources)[:, None] == slot_index[None, :]
        ).astype(jnp.bfloat16)
        grad_home = (
            jnp.einsum("js,srw->jrw", came_over, returned, preferred_element_type=jnp.float32)
            .astype(jnp.bfloat16)
            .reshape(token_row_count, width_part)
        )
    else:
        arrived = lax.all_to_all(
            owned_blocks.reshape(block_count, -1), "dp", split_axis=0, concat_axis=0, tiled=True
        )
        grad_home = (
            lax.dot_general(
                send_table, arrived, (((0,), (0,)), ((), ())), preferred_element_type=jnp.float32
            )
            .astype(jnp.bfloat16)
            .reshape(token_row_count, width_part)
        )

    gathered = lax.all_gather(tokens, "tensor", axis=1, tiled=True)
    gathered_float = gathered.astype(jnp.float32)
    inverse = lax.rsqrt(jnp.mean(gathered_float * gathered_float, axis=1) + NORM_EPSILON)
    normed_input = (gathered_float * inverse[:, None] * norm_gain[None, :]).astype(jnp.bfloat16)
    query_raw = jnp.dot(normed_input, w_query, preferred_element_type=jnp.float32)
    key_raw = jnp.dot(normed_input, key_weight, preferred_element_type=jnp.float32)
    value_raw = jnp.dot(normed_input, value_weight, preferred_element_type=jnp.float32)
    doc_ids, positions = doc_tables(doc_lengths[0], token_row_count)
    token_index = jnp.arange(token_row_count, dtype=jnp.int32)
    allowed = (doc_ids[:, None] == doc_ids[None, :]) & (
        token_index[None, :] <= token_index[:, None]
    )
    cosine, sine_table = rope_tables(positions, HEAD_SIZE)
    query_rows = rotate(
        query_raw.reshape(token_row_count, heads_local, HEAD_SIZE), cosine, sine_table
    ).astype(jnp.bfloat16)
    keys = rotate(
        key_raw.reshape(token_row_count, kv_local, HEAD_SIZE), cosine, sine_table
    ).astype(jnp.bfloat16)
    value_rows = value_raw.astype(jnp.bfloat16).reshape(token_row_count, kv_local, HEAD_SIZE)
    grouped_query = query_rows.reshape(token_row_count, kv_local, query_group_width, HEAD_SIZE)
    scores = (
        jnp.einsum("qkgd,skd->kgqs", grouped_query, keys, preferred_element_type=jnp.float32)
        * scale_factor
    )
    weights = jnp.where(allowed[None, None], jnp.exp(scores), 0.0)
    probs = weights / jnp.sum(weights, axis=-1, keepdims=True)
    probs_low = probs.astype(jnp.bfloat16)
    attended = jnp.einsum(
        "kgqs,skd->qkgd", probs_low, value_rows, preferred_element_type=jnp.float32
    ).astype(jnp.bfloat16)
    attended_flat = attended.reshape(token_row_count, query_width)
    mixed_partial = jnp.dot(attended_flat, w_out, preferred_element_type=jnp.float32)
    grad_full = lax.all_gather(grad_home, "tensor", axis=1, tiled=True)
    mixed_partial, grad_full = lax.optimization_barrier((mixed_partial, grad_full))
    attended_gradient = lax.dot_general(
        grad_full,
        w_out,
        (((1,), (1,)), ((), ())),
        preferred_element_type=jnp.float32,
    ).astype(jnp.bfloat16)
    mixed, _, (attended_gradient,) = scatter_features(
        mixed_partial, "tensor", tensor_size, tensor_index, ties=(attended_gradient,)
    )
    output_home = (x_float + mixed).astype(jnp.bfloat16)
    grouped_gradient = attended_gradient.reshape(
        token_row_count, kv_local, query_group_width, HEAD_SIZE
    )
    delta = jnp.sum(grouped_gradient.astype(jnp.float32) * attended.astype(jnp.float32), axis=-1)
    grad_probs = jnp.einsum(
        "qkgd,skd->kgqs", grouped_gradient, value_rows, preferred_element_type=jnp.float32
    )
    grad_scores = (probs * (grad_probs - jnp.transpose(delta, (1, 2, 0))[..., None])).astype(
        jnp.bfloat16
    )
    grad_query_rot = (
        jnp.einsum("kgqs,skd->qkgd", grad_scores, keys, preferred_element_type=jnp.float32)
        * scale_factor
    )
    grad_keys_rot = (
        jnp.einsum("kgqs,qkgd->skd", grad_scores, grouped_query, preferred_element_type=jnp.float32)
        * scale_factor
    )
    value_gradient = jnp.einsum(
        "kgqs,qkgd->skd", probs_low, grouped_gradient, preferred_element_type=jnp.float32
    )
    grad_query = unrotate(
        grad_query_rot.reshape(token_row_count, heads_local, HEAD_SIZE), cosine, sine_table
    ).astype(jnp.bfloat16)
    key_gradient = unrotate(grad_keys_rot, cosine, sine_table).astype(jnp.bfloat16)
    contract_out = (((1,), (1,)), ((), ()))
    normed_partial = (
        lax.dot_general(
            grad_query.reshape(token_row_count, query_width),
            w_query,
            contract_out,
            preferred_element_type=jnp.float32,
        )
        + lax.dot_general(
            key_gradient.reshape(token_row_count, key_width),
            key_weight,
            contract_out,
            preferred_element_type=jnp.float32,
        )
        + lax.dot_general(
            value_gradient.astype(jnp.bfloat16).reshape(token_row_count, key_width),
            value_weight,
            contract_out,
            preferred_element_type=jnp.float32,
        )
    )
    output_home, normed_partial = lax.optimization_barrier((output_home, normed_partial))
    stat_partial = jnp.sum(normed_partial * norm_gain[None, :] * gathered_float, axis=1)
    home_blocks = output_home.reshape(block_count, home_rows, width_part)
    outgoing = jnp.einsum(
        "dj,jrw->drw", send_table, home_blocks, preferred_element_type=jnp.float32
    ).astype(jnp.bfloat16)
    normed_gradient, stat_sum, (outgoing,) = scatter_features(
        normed_partial, "tensor", tensor_size, tensor_index, extra=stat_partial, ties=(outgoing,)
    )
    relaid = lax.all_to_all(outgoing, "dp", split_axis=0, concat_axis=0, tiled=True).reshape(
        token_row_count, width_part
    )
    stat = stat_sum / full_width
    cubed = inverse * inverse * inverse
    grad_x = (
        grad_home.astype(jnp.float32)
        + inverse[:, None] * gain_part[None, :] * normed_gradient
        - x_float * cubed[:, None] * stat[:, None]
    )
    return (relaid, grad_x.astype(jnp.bfloat16))


def solution(mesh):
    placed = (
        P("dp", "tensor"),
        P(),
        P(None, "tensor"),
        P(None, "tensor"),
        P(None, "tensor"),
        P("tensor", None),
        P("dp", "tensor"),
        P("dp", None),
        P(),
    )
    return jax.shard_map(
        per_device,
        mesh=mesh,
        in_specs=placed,
        out_specs=(P("dp", "tensor"), P("dp", "tensor")),
        check_vma=False,
    )
```

```python
import math

import jax
import jax.numpy as jnp
from jax import lax
from jax.sharding import PartitionSpec as P

HEAD_SIZE = 128


ROPE_BASE = 500000.0
NORM_EPSILON = 1e-05


def doc_tables(lengths_row, token_row_count):
    ends = jnp.cumsum(lengths_row)
    token_index = jnp.arange(token_row_count, dtype=jnp.int32)
    passed = (token_index[:, None] >= ends[None, :]).astype(jnp.int32)
    doc_ids = jnp.sum(passed, axis=1)
    starts = jnp.max(jnp.where(passed > 0, ends[None, :], 0), axis=1)
    return (doc_ids, token_index - starts)


def rope_tables(positions, head_size):
    half_dim = head_size // 2
    steps = jnp.arange(half_dim, dtype=jnp.float32)
    inverse_freq = jnp.power(ROPE_BASE, -2.0 * steps / head_size)
    angles = positions.astype(jnp.float32)[:, None] * inverse_freq[None, :]
    return (jnp.cos(angles), jnp.sin(angles))


def rotate(vectors, cosine, sine_table):
    half_dim = vectors.shape[-1] // 2
    former = vectors[..., :half_dim]
    latter = vectors[..., half_dim:]
    cos_part = cosine[:, None, :]
    sin_part = sine_table[:, None, :]
    return jnp.concatenate(
        [former * cos_part - latter * sin_part, latter * cos_part + former * sin_part], axis=-1
    )


def unrotate(vectors, cosine, sine_table):
    half_dim = vectors.shape[-1] // 2
    former = vectors[..., :half_dim]
    latter = vectors[..., half_dim:]
    cos_part = cosine[:, None, :]
    sin_part = sine_table[:, None, :]
    return jnp.concatenate(
        [former * cos_part + latter * sin_part, latter * cos_part - former * sin_part], axis=-1
    )


def _is_pow2(n):
    return n > 1 and (n & (n - 1)) == 0


def _xor_pairs(size, bit):
    return [(i, i ^ bit) for i in range(size)]


def gather_features(shard, axis_name, size, position):
    if not _is_pow2(size):
        return lax.all_gather(shard, axis_name, axis=1, tiled=True)
    held = shard[None]
    masks = [0]
    bit = size >> 1
    while bit:
        incoming = lax.ppermute(held, axis_name, _xor_pairs(size, bit))
        held = jnp.concatenate([held, incoming], axis=0)
        masks = masks + [m ^ bit for m in masks]
        bit >>= 1
    table = jnp.asarray([masks.index(m) for m in range(size)], jnp.int32)
    blocks = [
        lax.dynamic_index_in_dim(held, table[s ^ position], axis=0, keepdims=False)
        for s in range(size)
    ]
    return jnp.concatenate(blocks, axis=1)


def scatter_features(partial, axis_name, size, position, extra=None, ties=(), pieces=1):
    width = partial.shape[1] // size
    if not _is_pow2(size):
        summed = lax.psum_scatter(
            partial.astype(jnp.bfloat16), axis_name, scatter_dimension=1, tiled=True
        )
        if extra is not None:
            extra = lax.psum(extra, axis_name)
        return summed.astype(jnp.float32), extra, ties
    held = [
        lax.dynamic_slice_in_dim(partial, (position ^ m) * width, width, axis=1)
        for m in range(size)
    ]
    masks = list(range(size))
    done_ties = []
    bit = 1
    while bit < size:
        keep = [i for i, m in enumerate(masks) if not m & bit]
        send = [i for i, m in enumerate(masks) if m & bit]
        outgoing = jnp.stack([held[i] for i in send]).astype(jnp.bfloat16)
        if pieces > 1 and bit == size >> 1:
            step = outgoing.shape[1] // pieces
            incoming = jnp.concatenate(
                [
                    lax.ppermute(
                        outgoing[:, k * step : (k + 1) * step], axis_name, _xor_pairs(size, bit)
                    )
                    for k in range(pieces)
                ],
                axis=1,
            )
        else:
            incoming = lax.ppermute(outgoing, axis_name, _xor_pairs(size, bit))
        if extra is not None:
            extra = extra + lax.ppermute(extra, axis_name, _xor_pairs(size, bit))
        if ties:
            incoming, first = lax.optimization_barrier((incoming, ties[0]))
            ties = ties[1:]
            done_ties.append(first)
        sent_masks = [masks[i] ^ bit for i in send]
        held = [
            held[i] + incoming[sent_masks.index(masks[i])].astype(jnp.float32) for i in keep
        ]
        masks = [masks[i] for i in keep]
        bit <<= 1
    return held[0], extra, tuple(done_ties) + tuple(ties)


def per_device(
    tokens,
    norm_gain,
    w_query,
    key_weight,
    value_weight,
    w_out,
    grad_output,
    doc_lengths,
    block_owner,
):
    token_row_count, width_part = tokens.shape
    full_width = norm_gain.shape[0]
    sources = lax.axis_size("dp")
    tensor_size = lax.axis_size("tensor")
    data_index = lax.axis_index("dp")
    tensor_index = lax.axis_index("tensor")
    query_width = w_query.shape[1]
    key_width = key_weight.shape[1]
    heads_local = query_width // HEAD_SIZE
    kv_local = key_width // HEAD_SIZE
    query_group_width = heads_local // kv_local
    scale_factor = 1.0 / math.sqrt(HEAD_SIZE)
    gain_part = lax.dynamic_slice_in_dim(norm_gain, tensor_index * width_part, width_part)
    x_float = tokens.astype(jnp.float32)

    block_count = block_owner.shape[1]
    owner_row = lax.dynamic_slice_in_dim(block_owner, data_index, 1, 0)[0]
    slot_index = jnp.arange(sources, dtype=jnp.int32)
    send_table = (owner_row[None, :] == slot_index[:, None]).astype(jnp.bfloat16)

    home_rows = token_row_count // block_count
    owned_blocks = grad_output.reshape(block_count, home_rows, width_part)
    if sources <= 16:
        returned = [lax.dynamic_index_in_dim(owned_blocks, data_index, 0, keepdims=False)]
        for shift in range(1, sources):
            pairs = [(a, (a + shift) % sources) for a in range(sources)]
            piece = lax.dynamic_index_in_dim(
                owned_blocks, (data_index + shift) % sources, 0, keepdims=False
            )
            returned.append(lax.ppermute(piece, "dp", pairs))
        returned = jnp.stack(returned)
        came_over = (
            ((data_index - owner_row) % sources)[:, None] == slot_index[None, :]
        ).astype(jnp.bfloat16)
        grad_home = (
            jnp.einsum("js,srw->jrw", came_over, returned, preferred_element_type=jnp.float32)
            .astype(jnp.bfloat16)
            .reshape(token_row_count, width_part)
        )
    else:
        arrived = lax.all_to_all(
            owned_blocks.reshape(block_count, -1), "dp", split_axis=0, concat_axis=0, tiled=True
        )
        grad_home = (
            lax.dot_general(
                send_table, arrived, (((0,), (0,)), ((), ())), preferred_element_type=jnp.float32
            )
            .astype(jnp.bfloat16)
            .reshape(token_row_count, width_part)
        )

    gathered = lax.all_gather(tokens, "tensor", axis=1, tiled=True)
    gathered_float = gathered.astype(jnp.float32)
    inverse = lax.rsqrt(jnp.mean(gathered_float * gathered_float, axis=1) + NORM_EPSILON)
    normed_input = (gathered_float * inverse[:, None] * norm_gain[None, :]).astype(jnp.bfloat16)
    query_raw = jnp.dot(normed_input, w_query, preferred_element_type=jnp.float32)
    key_raw = jnp.dot(normed_input, key_weight, preferred_element_type=jnp.float32)
    value_raw = jnp.dot(normed_input, value_weight, preferred_element_type=jnp.float32)
    doc_ids, positions = doc_tables(doc_lengths[0], token_row_count)
    token_index = jnp.arange(token_row_count, dtype=jnp.int32)
    allowed = (doc_ids[:, None] == doc_ids[None, :]) & (
        token_index[None, :] <= token_index[:, None]
    )
    cosine, sine_table = rope_tables(positions, HEAD_SIZE)
    query_rows = rotate(
        query_raw.reshape(token_row_count, heads_local, HEAD_SIZE), cosine, sine_table
    ).astype(jnp.bfloat16)
    keys = rotate(
        key_raw.reshape(token_row_count, kv_local, HEAD_SIZE), cosine, sine_table
    ).astype(jnp.bfloat16)
    value_rows = value_raw.astype(jnp.bfloat16).reshape(token_row_count, kv_local, HEAD_SIZE)
    grouped_query = query_rows.reshape(token_row_count, kv_local, query_group_width, HEAD_SIZE)
    scores = (
        jnp.einsum("qkgd,skd->kgqs", grouped_query, keys, preferred_element_type=jnp.float32)
        * scale_factor
    )
    weights = jnp.where(allowed[None, None], jnp.exp(scores), 0.0)
    probs = weights / jnp.sum(weights, axis=-1, keepdims=True)
    probs_low = probs.astype(jnp.bfloat16)
    attended = jnp.einsum(
        "kgqs,skd->qkgd", probs_low, value_rows, preferred_element_type=jnp.float32
    ).astype(jnp.bfloat16)
    attended_flat = attended.reshape(token_row_count, query_width)
    mixed_partial = jnp.dot(attended_flat, w_out, preferred_element_type=jnp.float32)
    grad_full = lax.all_gather(grad_home, "tensor", axis=1, tiled=True)
    mixed_partial, grad_full = lax.optimization_barrier((mixed_partial, grad_full))
    attended_gradient = lax.dot_general(
        grad_full,
        w_out,
        (((1,), (1,)), ((), ())),
        preferred_element_type=jnp.float32,
    ).astype(jnp.bfloat16)
    mixed, _, (attended_gradient,) = scatter_features(
        mixed_partial, "tensor", tensor_size, tensor_index, ties=(attended_gradient,)
    )
    output_home = (x_float + mixed).astype(jnp.bfloat16)
    grouped_gradient = attended_gradient.reshape(
        token_row_count, kv_local, query_group_width, HEAD_SIZE
    )
    delta = jnp.sum(grouped_gradient.astype(jnp.float32) * attended.astype(jnp.float32), axis=-1)
    grad_probs = jnp.einsum(
        "qkgd,skd->kgqs", grouped_gradient, value_rows, preferred_element_type=jnp.float32
    )
    grad_scores = (probs * (grad_probs - jnp.transpose(delta, (1, 2, 0))[..., None])).astype(
        jnp.bfloat16
    )
    grad_query_rot = (
        jnp.einsum("kgqs,skd->qkgd", grad_scores, keys, preferred_element_type=jnp.float32)
        * scale_factor
    )
    grad_keys_rot = (
        jnp.einsum("kgqs,qkgd->skd", grad_scores, grouped_query, preferred_element_type=jnp.float32)
        * scale_factor
    )
    value_gradient = jnp.einsum(
        "kgqs,qkgd->skd", probs_low, grouped_gradient, preferred_element_type=jnp.float32
    )
    grad_query = unrotate(
        grad_query_rot.reshape(token_row_count, heads_local, HEAD_SIZE), cosine, sine_table
    ).astype(jnp.bfloat16)
    key_gradient = unrotate(grad_keys_rot, cosine, sine_table).astype(jnp.bfloat16)
    contract_out = (((1,), (1,)), ((), ()))
    normed_partial = (
        lax.dot_general(
            grad_query.reshape(token_row_count, query_width),
            w_query,
            contract_out,
            preferred_element_type=jnp.float32,
        )
        + lax.dot_general(
            key_gradient.reshape(token_row_count, key_width),
            key_weight,
            contract_out,
            preferred_element_type=jnp.float32,
        )
        + lax.dot_general(
            value_gradient.astype(jnp.bfloat16).reshape(token_row_count, key_width),
            value_weight,
            contract_out,
            preferred_element_type=jnp.float32,
        )
    )
    output_home, normed_partial = lax.optimization_barrier((output_home, normed_partial))
    stat_partial = jnp.sum(normed_partial * norm_gain[None, :] * gathered_float, axis=1)
    home_blocks = output_home.reshape(block_count, home_rows, width_part)
    outgoing = jnp.einsum(
        "dj,jrw->drw", send_table, home_blocks, preferred_element_type=jnp.float32
    ).astype(jnp.bfloat16)
    normed_gradient, stat_sum, (outgoing,) = scatter_features(
        normed_partial,
        "tensor",
        tensor_size,
        tensor_index,
        extra=stat_partial,
        ties=(outgoing,),
        pieces=2,
    )
    relaid = lax.all_to_all(outgoing, "dp", split_axis=0, concat_axis=0, tiled=True).reshape(
        token_row_count, width_part
    )
    stat = stat_sum / full_width
    cubed = inverse * inverse * inverse
    grad_x = (
        grad_home.astype(jnp.float32)
        + inverse[:, None] * gain_part[None, :] * normed_gradient
        - x_float * cubed[:, None] * stat[:, None]
    )
    return (relaid, grad_x.astype(jnp.bfloat16))


def solution(mesh):
    placed = (
        P("dp", "tensor"),
        P(),
        P(None, "tensor"),
        P(None, "tensor"),
        P(None, "tensor"),
        P("tensor", None),
        P("dp", "tensor"),
        P("dp", None),
        P(),
    )
    return jax.shard_map(
        per_device,
        mesh=mesh,
        in_specs=placed,
        out_specs=(P("dp", "tensor"), P("dp", "tensor")),
        check_vma=False,
    )
```

```python
import math

import jax
import jax.numpy as jnp
from jax import lax
from jax.sharding import PartitionSpec as P

HEAD_SIZE = 128


ROPE_BASE = 500000.0
NORM_EPSILON = 1e-05


def doc_tables(lengths_row, token_row_count):
    ends = jnp.cumsum(lengths_row)
    token_index = jnp.arange(token_row_count, dtype=jnp.int32)
    passed = (token_index[:, None] >= ends[None, :]).astype(jnp.int32)
    doc_ids = jnp.sum(passed, axis=1)
    starts = jnp.max(jnp.where(passed > 0, ends[None, :], 0), axis=1)
    return (doc_ids, token_index - starts)


def rope_tables(positions, head_size):
    half_dim = head_size // 2
    steps = jnp.arange(half_dim, dtype=jnp.float32)
    inverse_freq = jnp.power(ROPE_BASE, -2.0 * steps / head_size)
    angles = positions.astype(jnp.float32)[:, None] * inverse_freq[None, :]
    return (jnp.cos(angles), jnp.sin(angles))


def rotate(vectors, cosine, sine_table):
    half_dim = vectors.shape[-1] // 2
    former = vectors[..., :half_dim]
    latter = vectors[..., half_dim:]
    cos_part = cosine[:, None, :]
    sin_part = sine_table[:, None, :]
    return jnp.concatenate(
        [former * cos_part - latter * sin_part, latter * cos_part + former * sin_part], axis=-1
    )


def unrotate(vectors, cosine, sine_table):
    half_dim = vectors.shape[-1] // 2
    former = vectors[..., :half_dim]
    latter = vectors[..., half_dim:]
    cos_part = cosine[:, None, :]
    sin_part = sine_table[:, None, :]
    return jnp.concatenate(
        [former * cos_part + latter * sin_part, latter * cos_part - former * sin_part], axis=-1
    )


def _is_pow2(n):
    return n > 1 and (n & (n - 1)) == 0


def _xor_pairs(size, bit):
    return [(i, i ^ bit) for i in range(size)]


def gather_features(shard, axis_name, size, position):
    if not _is_pow2(size):
        return lax.all_gather(shard, axis_name, axis=1, tiled=True)
    held = shard[None]
    masks = [0]
    bit = size >> 1
    while bit:
        incoming = lax.ppermute(held, axis_name, _xor_pairs(size, bit))
        held = jnp.concatenate([held, incoming], axis=0)
        masks = masks + [m ^ bit for m in masks]
        bit >>= 1
    table = jnp.asarray([masks.index(m) for m in range(size)], jnp.int32)
    blocks = [
        lax.dynamic_index_in_dim(held, table[s ^ position], axis=0, keepdims=False)
        for s in range(size)
    ]
    return jnp.concatenate(blocks, axis=1)


def scatter_features(partial, axis_name, size, position, extra=None, ties=()):
    width = partial.shape[1] // size
    if not _is_pow2(size):
        summed = lax.psum_scatter(
            partial.astype(jnp.bfloat16), axis_name, scatter_dimension=1, tiled=True
        )
        if extra is not None:
            extra = lax.psum(extra, axis_name)
        return summed.astype(jnp.float32), extra, ties
    held = [
        lax.dynamic_slice_in_dim(partial, (position ^ m) * width, width, axis=1)
        for m in range(size)
    ]
    masks = list(range(size))
    done_ties = []
    bit = 1
    while bit < size:
        keep = [i for i, m in enumerate(masks) if not m & bit]
        send = [i for i, m in enumerate(masks) if m & bit]
        outgoing = jnp.stack([held[i] for i in send]).astype(jnp.bfloat16)
        if extra is None:
            incoming = lax.ppermute(outgoing, axis_name, _xor_pairs(size, bit))
        else:
            incoming, extra_in = lax.ppermute((outgoing, extra), axis_name, _xor_pairs(size, bit))
            extra = extra + extra_in
        if ties:
            incoming, first = lax.optimization_barrier((incoming, ties[0]))
            ties = ties[1:]
            done_ties.append(first)
        sent_masks = [masks[i] ^ bit for i in send]
        held = [
            held[i] + incoming[sent_masks.index(masks[i])].astype(jnp.float32) for i in keep
        ]
        masks = [masks[i] for i in keep]
        bit <<= 1
    return held[0], extra, tuple(done_ties) + tuple(ties)


def per_device(
    tokens,
    norm_gain,
    w_query,
    key_weight,
    value_weight,
    w_out,
    grad_output,
    doc_lengths,
    block_owner,
):
    token_row_count, width_part = tokens.shape
    full_width = norm_gain.shape[0]
    sources = lax.axis_size("dp")
    tensor_size = lax.axis_size("tensor")
    data_index = lax.axis_index("dp")
    tensor_index = lax.axis_index("tensor")
    query_width = w_query.shape[1]
    key_width = key_weight.shape[1]
    heads_local = query_width // HEAD_SIZE
    kv_local = key_width // HEAD_SIZE
    query_group_width = heads_local // kv_local
    scale_factor = 1.0 / math.sqrt(HEAD_SIZE)
    gain_part = lax.dynamic_slice_in_dim(norm_gain, tensor_index * width_part, width_part)
    x_float = tokens.astype(jnp.float32)

    block_count = block_owner.shape[1]
    owner_row = lax.dynamic_slice_in_dim(block_owner, data_index, 1, 0)[0]
    slot_index = jnp.arange(sources, dtype=jnp.int32)
    send_table = (owner_row[None, :] == slot_index[:, None]).astype(jnp.bfloat16)

    home_rows = token_row_count // block_count
    owned_blocks = grad_output.reshape(block_count, home_rows, width_part)
    arrived = lax.all_to_all(owned_blocks, "dp", split_axis=0, concat_axis=0, tiled=True)
    grad_home = (
        jnp.einsum("dj,drw->jrw", send_table, arrived, preferred_element_type=jnp.float32)
        .astype(jnp.bfloat16)
        .reshape(token_row_count, width_part)
    )

    gathered = gather_features(tokens, "tensor", tensor_size, tensor_index)
    gathered_float = gathered.astype(jnp.float32)
    inverse = lax.rsqrt(jnp.mean(gathered_float * gathered_float, axis=1) + NORM_EPSILON)
    normed_input = (gathered_float * inverse[:, None] * norm_gain[None, :]).astype(jnp.bfloat16)
    query_raw = jnp.dot(normed_input, w_query, preferred_element_type=jnp.float32)
    key_raw = jnp.dot(normed_input, key_weight, preferred_element_type=jnp.float32)
    value_raw = jnp.dot(normed_input, value_weight, preferred_element_type=jnp.float32)
    doc_ids, positions = doc_tables(doc_lengths[0], token_row_count)
    token_index = jnp.arange(token_row_count, dtype=jnp.int32)
    allowed = (doc_ids[:, None] == doc_ids[None, :]) & (
        token_index[None, :] <= token_index[:, None]
    )
    cosine, sine_table = rope_tables(positions, HEAD_SIZE)
    query_rows = rotate(
        query_raw.reshape(token_row_count, heads_local, HEAD_SIZE), cosine, sine_table
    ).astype(jnp.bfloat16)
    keys = rotate(
        key_raw.reshape(token_row_count, kv_local, HEAD_SIZE), cosine, sine_table
    ).astype(jnp.bfloat16)
    value_rows = value_raw.astype(jnp.bfloat16).reshape(token_row_count, kv_local, HEAD_SIZE)
    grouped_query = query_rows.reshape(token_row_count, kv_local, query_group_width, HEAD_SIZE)
    scores = (
        jnp.einsum("qkgd,skd->kgqs", grouped_query, keys, preferred_element_type=jnp.float32)
        * scale_factor
    )
    weights = jnp.where(allowed[None, None], jnp.exp(scores), 0.0)
    probs = weights / jnp.sum(weights, axis=-1, keepdims=True)
    probs_low = probs.astype(jnp.bfloat16)
    attended = jnp.einsum(
        "kgqs,skd->qkgd", probs_low, value_rows, preferred_element_type=jnp.float32
    ).astype(jnp.bfloat16)
    attended_flat = attended.reshape(token_row_count, query_width)
    mixed_partial = jnp.dot(attended_flat, w_out, preferred_element_type=jnp.float32)
    grad_full = lax.all_gather(grad_home, "tensor", axis=1, tiled=True)
    mixed_partial, grad_full = lax.optimization_barrier((mixed_partial, grad_full))
    attended_gradient = lax.dot_general(
        grad_full,
        w_out,
        (((1,), (1,)), ((), ())),
        preferred_element_type=jnp.float32,
    ).astype(jnp.bfloat16)
    mixed, _, (attended_gradient,) = scatter_features(
        mixed_partial, "tensor", tensor_size, tensor_index, ties=(attended_gradient,)
    )
    output_home = (x_float + mixed).astype(jnp.bfloat16)
    grouped_gradient = attended_gradient.reshape(
        token_row_count, kv_local, query_group_width, HEAD_SIZE
    )
    delta = jnp.sum(grouped_gradient.astype(jnp.float32) * attended.astype(jnp.float32), axis=-1)
    grad_probs = jnp.einsum(
        "qkgd,skd->kgqs", grouped_gradient, value_rows, preferred_element_type=jnp.float32
    )
    grad_scores = (probs * (grad_probs - jnp.transpose(delta, (1, 2, 0))[..., None])).astype(
        jnp.bfloat16
    )
    grad_query_rot = (
        jnp.einsum("kgqs,skd->qkgd", grad_scores, keys, preferred_element_type=jnp.float32)
        * scale_factor
    )
    grad_keys_rot = (
        jnp.einsum("kgqs,qkgd->skd", grad_scores, grouped_query, preferred_element_type=jnp.float32)
        * scale_factor
    )
    value_gradient = jnp.einsum(
        "kgqs,qkgd->skd", probs_low, grouped_gradient, preferred_element_type=jnp.float32
    )
    grad_query = unrotate(
        grad_query_rot.reshape(token_row_count, heads_local, HEAD_SIZE), cosine, sine_table
    ).astype(jnp.bfloat16)
    key_gradient = unrotate(grad_keys_rot, cosine, sine_table).astype(jnp.bfloat16)
    contract_out = (((1,), (1,)), ((), ()))
    normed_partial = (
        lax.dot_general(
            grad_query.reshape(token_row_count, query_width),
            w_query,
            contract_out,
            preferred_element_type=jnp.float32,
        )
        + lax.dot_general(
            key_gradient.reshape(token_row_count, key_width),
            key_weight,
            contract_out,
            preferred_element_type=jnp.float32,
        )
        + lax.dot_general(
            value_gradient.astype(jnp.bfloat16).reshape(token_row_count, key_width),
            value_weight,
            contract_out,
            preferred_element_type=jnp.float32,
        )
    )
    output_home, normed_partial = lax.optimization_barrier((output_home, normed_partial))
    stat_partial = jnp.sum(normed_partial * norm_gain[None, :] * gathered_float, axis=1)
    home_blocks = output_home.reshape(block_count, home_rows, width_part)
    outgoing = jnp.einsum(
        "dj,jrw->drw", send_table, home_blocks, preferred_element_type=jnp.float32
    ).astype(jnp.bfloat16)
    normed_gradient, stat_sum, (outgoing,) = scatter_features(
        normed_partial, "tensor", tensor_size, tensor_index, extra=stat_partial, ties=(outgoing,)
    )
    relaid = lax.all_to_all(outgoing, "dp", split_axis=0, concat_axis=0, tiled=True).reshape(
        token_row_count, width_part
    )
    stat = stat_sum / full_width
    cubed = inverse * inverse * inverse
    grad_x = (
        grad_home.astype(jnp.float32)
        + inverse[:, None] * gain_part[None, :] * normed_gradient
        - x_float * cubed[:, None] * stat[:, None]
    )
    return (relaid, grad_x.astype(jnp.bfloat16))


def solution(mesh):
    placed = (
        P("dp", "tensor"),
        P(),
        P(None, "tensor"),
        P(None, "tensor"),
        P(None, "tensor"),
        P("tensor", None),
        P("dp", "tensor"),
        P("dp", None),
        P(),
    )
    return jax.shard_map(
        per_device,
        mesh=mesh,
        in_specs=placed,
        out_specs=(P("dp", "tensor"), P("dp", "tensor")),
        check_vma=False,
    )
```

```python
import math

import jax
import jax.numpy as jnp
from jax import lax
from jax.sharding import PartitionSpec as P

HEAD_SIZE = 128


ROPE_BASE = 500000.0
NORM_EPSILON = 1e-05


def doc_tables(lengths_row, token_row_count):
    ends = jnp.cumsum(lengths_row)
    token_index = jnp.arange(token_row_count, dtype=jnp.int32)
    passed = (token_index[:, None] >= ends[None, :]).astype(jnp.int32)
    doc_ids = jnp.sum(passed, axis=1)
    starts = jnp.max(jnp.where(passed > 0, ends[None, :], 0), axis=1)
    return (doc_ids, token_index - starts)


def rope_tables(positions, head_size):
    half_dim = head_size // 2
    steps = jnp.arange(half_dim, dtype=jnp.float32)
    inverse_freq = jnp.power(ROPE_BASE, -2.0 * steps / head_size)
    angles = positions.astype(jnp.float32)[:, None] * inverse_freq[None, :]
    return (jnp.cos(angles), jnp.sin(angles))


def rotate(vectors, cosine, sine_table):
    half_dim = vectors.shape[-1] // 2
    former = vectors[..., :half_dim]
    latter = vectors[..., half_dim:]
    cos_part = cosine[:, None, :]
    sin_part = sine_table[:, None, :]
    return jnp.concatenate(
        [former * cos_part - latter * sin_part, latter * cos_part + former * sin_part], axis=-1
    )


def unrotate(vectors, cosine, sine_table):
    half_dim = vectors.shape[-1] // 2
    former = vectors[..., :half_dim]
    latter = vectors[..., half_dim:]
    cos_part = cosine[:, None, :]
    sin_part = sine_table[:, None, :]
    return jnp.concatenate(
        [former * cos_part + latter * sin_part, latter * cos_part - former * sin_part], axis=-1
    )


def _is_pow2(n):
    return n > 1 and (n & (n - 1)) == 0


def _xor_pairs(size, bit):
    return [(i, i ^ bit) for i in range(size)]


def gather_features(shard, axis_name, size, position):
    if not _is_pow2(size):
        return lax.all_gather(shard, axis_name, axis=1, tiled=True)
    held = shard[None]
    masks = [0]
    bit = size >> 1
    while bit:
        incoming = lax.ppermute(held, axis_name, _xor_pairs(size, bit))
        held = jnp.concatenate([held, incoming], axis=0)
        masks = masks + [m ^ bit for m in masks]
        bit >>= 1
    table = jnp.asarray([masks.index(m) for m in range(size)], jnp.int32)
    blocks = [
        lax.dynamic_index_in_dim(held, table[s ^ position], axis=0, keepdims=False)
        for s in range(size)
    ]
    return jnp.concatenate(blocks, axis=1)


def scatter_features(partial, axis_name, size, position, extra=None, ties=()):
    width = partial.shape[1] // size
    if not _is_pow2(size):
        summed = lax.psum_scatter(
            partial.astype(jnp.bfloat16), axis_name, scatter_dimension=1, tiled=True
        )
        if extra is not None:
            extra = lax.psum(extra, axis_name)
        return summed.astype(jnp.float32), extra, ties
    held = [
        lax.dynamic_slice_in_dim(partial, (position ^ m) * width, width, axis=1)
        for m in range(size)
    ]
    masks = list(range(size))
    done_ties = []
    bit = 1
    while bit < size:
        keep = [i for i, m in enumerate(masks) if not m & bit]
        send = [i for i, m in enumerate(masks) if m & bit]
        outgoing = jnp.stack([held[i] for i in send]).astype(jnp.bfloat16)
        if extra is None:
            incoming = lax.ppermute(outgoing, axis_name, _xor_pairs(size, bit))
        else:
            incoming, extra_in = lax.ppermute((outgoing, extra), axis_name, _xor_pairs(size, bit))
            extra = extra + extra_in
        if ties:
            incoming, first = lax.optimization_barrier((incoming, ties[0]))
            ties = ties[1:]
            done_ties.append(first)
        sent_masks = [masks[i] ^ bit for i in send]
        held = [
            held[i] + incoming[sent_masks.index(masks[i])].astype(jnp.float32) for i in keep
        ]
        masks = [masks[i] for i in keep]
        bit <<= 1
    return held[0], extra, tuple(done_ties) + tuple(ties)


def per_device(
    tokens,
    norm_gain,
    w_query,
    key_weight,
    value_weight,
    w_out,
    grad_output,
    doc_lengths,
    block_owner,
):
    token_row_count, width_part = tokens.shape
    full_width = norm_gain.shape[0]
    sources = lax.axis_size("dp")
    tensor_size = lax.axis_size("tensor")
    data_index = lax.axis_index("dp")
    tensor_index = lax.axis_index("tensor")
    query_width = w_query.shape[1]
    key_width = key_weight.shape[1]
    heads_local = query_width // HEAD_SIZE
    kv_local = key_width // HEAD_SIZE
    query_group_width = heads_local // kv_local
    scale_factor = 1.0 / math.sqrt(HEAD_SIZE)
    gain_part = lax.dynamic_slice_in_dim(norm_gain, tensor_index * width_part, width_part)
    x_float = tokens.astype(jnp.float32)

    block_count = block_owner.shape[1]
    owner_row = lax.dynamic_slice_in_dim(block_owner, data_index, 1, 0)[0]
    slot_index = jnp.arange(sources, dtype=jnp.int32)
    send_table = (owner_row[None, :] == slot_index[:, None]).astype(jnp.bfloat16)

    home_rows = token_row_count // block_count
    gathered = gather_features(tokens, "tensor", tensor_size, tensor_index)
    gathered, grad_output = lax.optimization_barrier((gathered, grad_output))
    owned_blocks = grad_output.reshape(block_count, home_rows, width_part)
    arrived = lax.all_to_all(owned_blocks, "dp", split_axis=0, concat_axis=0, tiled=True)
    grad_home = (
        jnp.einsum("dj,drw->jrw", send_table, arrived, preferred_element_type=jnp.float32)
        .astype(jnp.bfloat16)
        .reshape(token_row_count, width_part)
    )

    gathered_float = gathered.astype(jnp.float32)
    inverse = lax.rsqrt(jnp.mean(gathered_float * gathered_float, axis=1) + NORM_EPSILON)
    normed_input = (gathered_float * inverse[:, None] * norm_gain[None, :]).astype(jnp.bfloat16)
    query_raw = jnp.dot(normed_input, w_query, preferred_element_type=jnp.float32)
    key_raw = jnp.dot(normed_input, key_weight, preferred_element_type=jnp.float32)
    value_raw = jnp.dot(normed_input, value_weight, preferred_element_type=jnp.float32)
    doc_ids, positions = doc_tables(doc_lengths[0], token_row_count)
    token_index = jnp.arange(token_row_count, dtype=jnp.int32)
    allowed = (doc_ids[:, None] == doc_ids[None, :]) & (
        token_index[None, :] <= token_index[:, None]
    )
    cosine, sine_table = rope_tables(positions, HEAD_SIZE)
    query_rows = rotate(
        query_raw.reshape(token_row_count, heads_local, HEAD_SIZE), cosine, sine_table
    ).astype(jnp.bfloat16)
    keys = rotate(
        key_raw.reshape(token_row_count, kv_local, HEAD_SIZE), cosine, sine_table
    ).astype(jnp.bfloat16)
    value_rows = value_raw.astype(jnp.bfloat16).reshape(token_row_count, kv_local, HEAD_SIZE)
    grouped_query = query_rows.reshape(token_row_count, kv_local, query_group_width, HEAD_SIZE)
    scores = (
        jnp.einsum("qkgd,skd->kgqs", grouped_query, keys, preferred_element_type=jnp.float32)
        * scale_factor
    )
    weights = jnp.where(allowed[None, None], jnp.exp(scores), 0.0)
    probs = weights / jnp.sum(weights, axis=-1, keepdims=True)
    probs_low = probs.astype(jnp.bfloat16)
    attended = jnp.einsum(
        "kgqs,skd->qkgd", probs_low, value_rows, preferred_element_type=jnp.float32
    ).astype(jnp.bfloat16)
    attended_flat = attended.reshape(token_row_count, query_width)
    mixed_partial = jnp.dot(attended_flat, w_out, preferred_element_type=jnp.float32)
    grad_full = lax.all_gather(grad_home, "tensor", axis=1, tiled=True)
    mixed_partial, grad_full = lax.optimization_barrier((mixed_partial, grad_full))
    attended_gradient = lax.dot_general(
        grad_full,
        w_out,
        (((1,), (1,)), ((), ())),
        preferred_element_type=jnp.float32,
    ).astype(jnp.bfloat16)
    mixed, _, (attended_gradient,) = scatter_features(
        mixed_partial, "tensor", tensor_size, tensor_index, ties=(attended_gradient,)
    )
    output_home = (x_float + mixed).astype(jnp.bfloat16)
    grouped_gradient = attended_gradient.reshape(
        token_row_count, kv_local, query_group_width, HEAD_SIZE
    )
    delta = jnp.sum(grouped_gradient.astype(jnp.float32) * attended.astype(jnp.float32), axis=-1)
    grad_probs = jnp.einsum(
        "qkgd,skd->kgqs", grouped_gradient, value_rows, preferred_element_type=jnp.float32
    )
    grad_scores = (probs * (grad_probs - jnp.transpose(delta, (1, 2, 0))[..., None])).astype(
        jnp.bfloat16
    )
    grad_query_rot = (
        jnp.einsum("kgqs,skd->qkgd", grad_scores, keys, preferred_element_type=jnp.float32)
        * scale_factor
    )
    grad_keys_rot = (
        jnp.einsum("kgqs,qkgd->skd", grad_scores, grouped_query, preferred_element_type=jnp.float32)
        * scale_factor
    )
    value_gradient = jnp.einsum(
        "kgqs,qkgd->skd", probs_low, grouped_gradient, preferred_element_type=jnp.float32
    )
    grad_query = unrotate(
        grad_query_rot.reshape(token_row_count, heads_local, HEAD_SIZE), cosine, sine_table
    ).astype(jnp.bfloat16)
    key_gradient = unrotate(grad_keys_rot, cosine, sine_table).astype(jnp.bfloat16)
    contract_out = (((1,), (1,)), ((), ()))
    normed_partial = (
        lax.dot_general(
            grad_query.reshape(token_row_count, query_width),
            w_query,
            contract_out,
            preferred_element_type=jnp.float32,
        )
        + lax.dot_general(
            key_gradient.reshape(token_row_count, key_width),
            key_weight,
            contract_out,
            preferred_element_type=jnp.float32,
        )
        + lax.dot_general(
            value_gradient.astype(jnp.bfloat16).reshape(token_row_count, key_width),
            value_weight,
            contract_out,
            preferred_element_type=jnp.float32,
        )
    )
    output_home, normed_partial = lax.optimization_barrier((output_home, normed_partial))
    stat_partial = jnp.sum(normed_partial * norm_gain[None, :] * gathered_float, axis=1)
    home_blocks = output_home.reshape(block_count, home_rows, width_part)
    outgoing = jnp.einsum(
        "dj,jrw->drw", send_table, home_blocks, preferred_element_type=jnp.float32
    ).astype(jnp.bfloat16)
    normed_gradient, stat_sum, (outgoing,) = scatter_features(
        normed_partial, "tensor", tensor_size, tensor_index, extra=stat_partial, ties=(outgoing,)
    )
    relaid = lax.all_to_all(outgoing, "dp", split_axis=0, concat_axis=0, tiled=True).reshape(
        token_row_count, width_part
    )
    stat = stat_sum / full_width
    cubed = inverse * inverse * inverse
    grad_x = (
        grad_home.astype(jnp.float32)
        + inverse[:, None] * gain_part[None, :] * normed_gradient
        - x_float * cubed[:, None] * stat[:, None]
    )
    return (relaid, grad_x.astype(jnp.bfloat16))


def solution(mesh):
    placed = (
        P("dp", "tensor"),
        P(),
        P(None, "tensor"),
        P(None, "tensor"),
        P(None, "tensor"),
        P("tensor", None),
        P("dp", "tensor"),
        P("dp", None),
        P(),
    )
    return jax.shard_map(
        per_device,
        mesh=mesh,
        in_specs=placed,
        out_specs=(P("dp", "tensor"), P("dp", "tensor")),
        check_vma=False,
    )
```

```python
import math

import jax
import jax.numpy as jnp
from jax import lax
from jax.sharding import PartitionSpec as P

HEAD_SIZE = 128


ROPE_BASE = 500000.0
NORM_EPSILON = 1e-05


def doc_tables(lengths_row, token_row_count):
    ends = jnp.cumsum(lengths_row)
    token_index = jnp.arange(token_row_count, dtype=jnp.int32)
    passed = (token_index[:, None] >= ends[None, :]).astype(jnp.int32)
    doc_ids = jnp.sum(passed, axis=1)
    starts = jnp.max(jnp.where(passed > 0, ends[None, :], 0), axis=1)
    return (doc_ids, token_index - starts)


def rope_tables(positions, head_size):
    half_dim = head_size // 2
    steps = jnp.arange(half_dim, dtype=jnp.float32)
    inverse_freq = jnp.power(ROPE_BASE, -2.0 * steps / head_size)
    angles = positions.astype(jnp.float32)[:, None] * inverse_freq[None, :]
    return (jnp.cos(angles), jnp.sin(angles))


def rotate(vectors, cosine, sine_table):
    half_dim = vectors.shape[-1] // 2
    former = vectors[..., :half_dim]
    latter = vectors[..., half_dim:]
    cos_part = cosine[:, None, :]
    sin_part = sine_table[:, None, :]
    return jnp.concatenate(
        [former * cos_part - latter * sin_part, latter * cos_part + former * sin_part], axis=-1
    )


def unrotate(vectors, cosine, sine_table):
    half_dim = vectors.shape[-1] // 2
    former = vectors[..., :half_dim]
    latter = vectors[..., half_dim:]
    cos_part = cosine[:, None, :]
    sin_part = sine_table[:, None, :]
    return jnp.concatenate(
        [former * cos_part + latter * sin_part, latter * cos_part - former * sin_part], axis=-1
    )


def _is_pow2(n):
    return n > 1 and (n & (n - 1)) == 0


def _xor_pairs(size, bit):
    return [(i, i ^ bit) for i in range(size)]


def gather_features(shard, axis_name, size, position):
    if not _is_pow2(size):
        return lax.all_gather(shard, axis_name, axis=1, tiled=True)
    held = shard[None]
    masks = [0]
    bit = size >> 1
    while bit:
        incoming = lax.ppermute(held, axis_name, _xor_pairs(size, bit))
        held = jnp.concatenate([held, incoming], axis=0)
        masks = masks + [m ^ bit for m in masks]
        bit >>= 1
    table = jnp.asarray([masks.index(m) for m in range(size)], jnp.int32)
    blocks = [
        lax.dynamic_index_in_dim(held, table[s ^ position], axis=0, keepdims=False)
        for s in range(size)
    ]
    return jnp.concatenate(blocks, axis=1)


def scatter_features(partial, axis_name, size, position, extra=None, ties=()):
    width = partial.shape[1] // size
    if not _is_pow2(size):
        summed = lax.psum_scatter(
            partial.astype(jnp.bfloat16), axis_name, scatter_dimension=1, tiled=True
        )
        if extra is not None:
            extra = lax.psum(extra, axis_name)
        return summed.astype(jnp.float32), extra, ties
    held = [
        lax.dynamic_slice_in_dim(partial, (position ^ m) * width, width, axis=1)
        for m in range(size)
    ]
    masks = list(range(size))
    done_ties = []
    bit = 1
    while bit < size:
        keep = [i for i, m in enumerate(masks) if not m & bit]
        send = [i for i, m in enumerate(masks) if m & bit]
        outgoing = jnp.stack([held[i] for i in send]).astype(jnp.bfloat16)
        incoming = lax.ppermute(outgoing, axis_name, _xor_pairs(size, bit))
        if ties:
            incoming, first = lax.optimization_barrier((incoming, ties[0]))
            ties = ties[1:]
            done_ties.append(first)
        if extra is not None and bit == 1:
            incoming, extra = lax.optimization_barrier((incoming, extra))
            extra = extra + sum(
                lax.ppermute(extra, axis_name, _xor_pairs(size, other))
                for other in range(1, size)
            )
        sent_masks = [masks[i] ^ bit for i in send]
        held = [
            held[i] + incoming[sent_masks.index(masks[i])].astype(jnp.float32) for i in keep
        ]
        masks = [masks[i] for i in keep]
        bit <<= 1
    return held[0], extra, tuple(done_ties) + tuple(ties)


def per_device(
    tokens,
    norm_gain,
    w_query,
    key_weight,
    value_weight,
    w_out,
    grad_output,
    doc_lengths,
    block_owner,
):
    token_row_count, width_part = tokens.shape
    full_width = norm_gain.shape[0]
    sources = lax.axis_size("dp")
    tensor_size = lax.axis_size("tensor")
    data_index = lax.axis_index("dp")
    tensor_index = lax.axis_index("tensor")
    query_width = w_query.shape[1]
    key_width = key_weight.shape[1]
    heads_local = query_width // HEAD_SIZE
    kv_local = key_width // HEAD_SIZE
    query_group_width = heads_local // kv_local
    scale_factor = 1.0 / math.sqrt(HEAD_SIZE)
    gain_part = lax.dynamic_slice_in_dim(norm_gain, tensor_index * width_part, width_part)
    x_float = tokens.astype(jnp.float32)

    block_count = block_owner.shape[1]
    owner_row = lax.dynamic_slice_in_dim(block_owner, data_index, 1, 0)[0]
    slot_index = jnp.arange(sources, dtype=jnp.int32)
    send_table = (owner_row[None, :] == slot_index[:, None]).astype(jnp.bfloat16)

    home_rows = token_row_count // block_count
    owned_blocks = grad_output.reshape(block_count, home_rows, width_part)
    if sources <= 16:
        returned = [lax.dynamic_index_in_dim(owned_blocks, data_index, 0, keepdims=False)]
        for shift in range(1, sources):
            pairs = [(a, (a + shift) % sources) for a in range(sources)]
            piece = lax.dynamic_index_in_dim(
                owned_blocks, (data_index + shift) % sources, 0, keepdims=False
            )
            returned.append(lax.ppermute(piece, "dp", pairs))
        returned = jnp.stack(returned)
        came_over = (
            ((data_index - owner_row) % sources)[:, None] == slot_index[None, :]
        ).astype(jnp.bfloat16)
        grad_home = (
            jnp.einsum("js,srw->jrw", came_over, returned, preferred_element_type=jnp.float32)
            .astype(jnp.bfloat16)
            .reshape(token_row_count, width_part)
        )
    else:
        arrived = lax.all_to_all(
            owned_blocks.reshape(block_count, -1), "dp", split_axis=0, concat_axis=0, tiled=True
        )
        grad_home = (
            lax.dot_general(
                send_table, arrived, (((0,), (0,)), ((), ())), preferred_element_type=jnp.float32
            )
            .astype(jnp.bfloat16)
            .reshape(token_row_count, width_part)
        )

    gathered = lax.all_gather(tokens, "tensor", axis=1, tiled=True)
    gathered_float = gathered.astype(jnp.float32)
    inverse = lax.rsqrt(jnp.mean(gathered_float * gathered_float, axis=1) + NORM_EPSILON)
    normed_input = (gathered_float * inverse[:, None] * norm_gain[None, :]).astype(jnp.bfloat16)
    query_raw = jnp.dot(normed_input, w_query, preferred_element_type=jnp.float32)
    key_raw = jnp.dot(normed_input, key_weight, preferred_element_type=jnp.float32)
    value_raw = jnp.dot(normed_input, value_weight, preferred_element_type=jnp.float32)
    doc_ids, positions = doc_tables(doc_lengths[0], token_row_count)
    token_index = jnp.arange(token_row_count, dtype=jnp.int32)
    allowed = (doc_ids[:, None] == doc_ids[None, :]) & (
        token_index[None, :] <= token_index[:, None]
    )
    cosine, sine_table = rope_tables(positions, HEAD_SIZE)
    query_rows = rotate(
        query_raw.reshape(token_row_count, heads_local, HEAD_SIZE), cosine, sine_table
    ).astype(jnp.bfloat16)
    keys = rotate(
        key_raw.reshape(token_row_count, kv_local, HEAD_SIZE), cosine, sine_table
    ).astype(jnp.bfloat16)
    value_rows = value_raw.astype(jnp.bfloat16).reshape(token_row_count, kv_local, HEAD_SIZE)
    grouped_query = query_rows.reshape(token_row_count, kv_local, query_group_width, HEAD_SIZE)
    scores = (
        jnp.einsum("qkgd,skd->kgqs", grouped_query, keys, preferred_element_type=jnp.float32)
        * scale_factor
    )
    weights = jnp.where(allowed[None, None], jnp.exp(scores), 0.0)
    probs = weights / jnp.sum(weights, axis=-1, keepdims=True)
    probs_low = probs.astype(jnp.bfloat16)
    attended = jnp.einsum(
        "kgqs,skd->qkgd", probs_low, value_rows, preferred_element_type=jnp.float32
    ).astype(jnp.bfloat16)
    attended_flat = attended.reshape(token_row_count, query_width)
    mixed_partial = jnp.dot(attended_flat, w_out, preferred_element_type=jnp.float32)
    grad_full = lax.all_gather(grad_home, "tensor", axis=1, tiled=True)
    mixed_partial, grad_full = lax.optimization_barrier((mixed_partial, grad_full))
    attended_gradient = lax.dot_general(
        grad_full,
        w_out,
        (((1,), (1,)), ((), ())),
        preferred_element_type=jnp.float32,
    ).astype(jnp.bfloat16)
    mixed, _, (attended_gradient,) = scatter_features(
        mixed_partial, "tensor", tensor_size, tensor_index, ties=(attended_gradient,)
    )
    output_home = (x_float + mixed).astype(jnp.bfloat16)
    grouped_gradient = attended_gradient.reshape(
        token_row_count, kv_local, query_group_width, HEAD_SIZE
    )
    delta = jnp.sum(grouped_gradient.astype(jnp.float32) * attended.astype(jnp.float32), axis=-1)
    grad_probs = jnp.einsum(
        "qkgd,skd->kgqs", grouped_gradient, value_rows, preferred_element_type=jnp.float32
    )
    grad_scores = (probs * (grad_probs - jnp.transpose(delta, (1, 2, 0))[..., None])).astype(
        jnp.bfloat16
    )
    grad_query_rot = (
        jnp.einsum("kgqs,skd->qkgd", grad_scores, keys, preferred_element_type=jnp.float32)
        * scale_factor
    )
    grad_keys_rot = (
        jnp.einsum("kgqs,qkgd->skd", grad_scores, grouped_query, preferred_element_type=jnp.float32)
        * scale_factor
    )
    value_gradient = jnp.einsum(
        "kgqs,qkgd->skd", probs_low, grouped_gradient, preferred_element_type=jnp.float32
    )
    grad_query = unrotate(
        grad_query_rot.reshape(token_row_count, heads_local, HEAD_SIZE), cosine, sine_table
    ).astype(jnp.bfloat16)
    key_gradient = unrotate(grad_keys_rot, cosine, sine_table).astype(jnp.bfloat16)
    contract_out = (((1,), (1,)), ((), ()))
    normed_partial = (
        lax.dot_general(
            grad_query.reshape(token_row_count, query_width),
            w_query,
            contract_out,
            preferred_element_type=jnp.float32,
        )
        + lax.dot_general(
            key_gradient.reshape(token_row_count, key_width),
            key_weight,
            contract_out,
            preferred_element_type=jnp.float32,
        )
        + lax.dot_general(
            value_gradient.astype(jnp.bfloat16).reshape(token_row_count, key_width),
            value_weight,
            contract_out,
            preferred_element_type=jnp.float32,
        )
    )
    output_home, normed_partial = lax.optimization_barrier((output_home, normed_partial))
    stat_partial = jnp.sum(normed_partial * norm_gain[None, :] * gathered_float, axis=1)
    home_blocks = output_home.reshape(block_count, home_rows, width_part)
    outgoing = jnp.einsum(
        "dj,jrw->drw", send_table, home_blocks, preferred_element_type=jnp.float32
    ).astype(jnp.bfloat16)
    normed_gradient, stat_sum, (outgoing,) = scatter_features(
        normed_partial, "tensor", tensor_size, tensor_index, extra=stat_partial, ties=(outgoing,)
    )
    relaid = lax.all_to_all(outgoing, "dp", split_axis=0, concat_axis=0, tiled=True).reshape(
        token_row_count, width_part
    )
    stat = stat_sum / full_width
    cubed = inverse * inverse * inverse
    grad_x = (
        grad_home.astype(jnp.float32)
        + inverse[:, None] * gain_part[None, :] * normed_gradient
        - x_float * cubed[:, None] * stat[:, None]
    )
    return (relaid, grad_x.astype(jnp.bfloat16))


def solution(mesh):
    placed = (
        P("dp", "tensor"),
        P(),
        P(None, "tensor"),
        P(None, "tensor"),
        P(None, "tensor"),
        P("tensor", None),
        P("dp", "tensor"),
        P("dp", None),
        P(),
    )
    return jax.shard_map(
        per_device,
        mesh=mesh,
        in_specs=placed,
        out_specs=(P("dp", "tensor"), P("dp", "tensor")),
        check_vma=False,
    )
```

```python
import math

import jax
import jax.numpy as jnp
from jax import lax
from jax.sharding import PartitionSpec as P

HEAD_SIZE = 128


ROPE_BASE = 500000.0
NORM_EPSILON = 1e-05


def doc_tables(lengths_row, token_row_count):
    ends = jnp.cumsum(lengths_row)
    token_index = jnp.arange(token_row_count, dtype=jnp.int32)
    passed = (token_index[:, None] >= ends[None, :]).astype(jnp.int32)
    doc_ids = jnp.sum(passed, axis=1)
    starts = jnp.max(jnp.where(passed > 0, ends[None, :], 0), axis=1)
    return (doc_ids, token_index - starts)


def rope_tables(positions, head_size):
    half_dim = head_size // 2
    steps = jnp.arange(half_dim, dtype=jnp.float32)
    inverse_freq = jnp.power(ROPE_BASE, -2.0 * steps / head_size)
    angles = positions.astype(jnp.float32)[:, None] * inverse_freq[None, :]
    return (jnp.cos(angles), jnp.sin(angles))


def rotate(vectors, cosine, sine_table):
    half_dim = vectors.shape[-1] // 2
    former = vectors[..., :half_dim]
    latter = vectors[..., half_dim:]
    cos_part = cosine[:, None, :]
    sin_part = sine_table[:, None, :]
    return jnp.concatenate(
        [former * cos_part - latter * sin_part, latter * cos_part + former * sin_part], axis=-1
    )


def unrotate(vectors, cosine, sine_table):
    half_dim = vectors.shape[-1] // 2
    former = vectors[..., :half_dim]
    latter = vectors[..., half_dim:]
    cos_part = cosine[:, None, :]
    sin_part = sine_table[:, None, :]
    return jnp.concatenate(
        [former * cos_part + latter * sin_part, latter * cos_part - former * sin_part], axis=-1
    )


def _is_pow2(n):
    return n > 1 and (n & (n - 1)) == 0


def _xor_pairs(size, bit):
    return [(i, i ^ bit) for i in range(size)]


def gather_features(shard, axis_name, size, position):
    if not _is_pow2(size):
        return lax.all_gather(shard, axis_name, axis=1, tiled=True)
    held = shard[None]
    masks = [0]
    bit = size >> 1
    while bit:
        incoming = lax.ppermute(held, axis_name, _xor_pairs(size, bit))
        held = jnp.concatenate([held, incoming], axis=0)
        masks = masks + [m ^ bit for m in masks]
        bit >>= 1
    table = jnp.asarray([masks.index(m) for m in range(size)], jnp.int32)
    blocks = [
        lax.dynamic_index_in_dim(held, table[s ^ position], axis=0, keepdims=False)
        for s in range(size)
    ]
    return jnp.concatenate(blocks, axis=1)


def scatter_features(partial, axis_name, size, position, extra=None, ties=()):
    width = partial.shape[1] // size
    if not _is_pow2(size):
        summed = lax.psum_scatter(
            partial.astype(jnp.bfloat16), axis_name, scatter_dimension=1, tiled=True
        )
        if extra is not None:
            extra = lax.psum(extra, axis_name)
        return summed.astype(jnp.float32), extra, ties
    held = [
        lax.dynamic_slice_in_dim(partial, (position ^ m) * width, width, axis=1)
        for m in range(size)
    ]
    masks = list(range(size))
    done_ties = []
    bit = 1
    while bit < size:
        keep = [i for i, m in enumerate(masks) if not m & bit]
        send = [i for i, m in enumerate(masks) if m & bit]
        outgoing = jnp.stack([held[i] for i in send]).astype(jnp.bfloat16)
        if extra is None:
            incoming = lax.ppermute(outgoing, axis_name, _xor_pairs(size, bit))
        else:
            incoming, extra_in = lax.ppermute((outgoing, extra), axis_name, _xor_pairs(size, bit))
            extra = extra + extra_in
        if ties:
            incoming, first = lax.optimization_barrier((incoming, ties[0]))
            ties = ties[1:]
            done_ties.append(first)
        sent_masks = [masks[i] ^ bit for i in send]
        held = [
            held[i] + incoming[sent_masks.index(masks[i])].astype(jnp.float32) for i in keep
        ]
        masks = [masks[i] for i in keep]
        bit <<= 1
    return held[0], extra, tuple(done_ties) + tuple(ties)


def per_device(
    tokens,
    norm_gain,
    w_query,
    key_weight,
    value_weight,
    w_out,
    grad_output,
    doc_lengths,
    block_owner,
):
    token_row_count, width_part = tokens.shape
    full_width = norm_gain.shape[0]
    sources = lax.axis_size("dp")
    tensor_size = lax.axis_size("tensor")
    data_index = lax.axis_index("dp")
    tensor_index = lax.axis_index("tensor")
    query_width = w_query.shape[1]
    key_width = key_weight.shape[1]
    heads_local = query_width // HEAD_SIZE
    kv_local = key_width // HEAD_SIZE
    query_group_width = heads_local // kv_local
    scale_factor = 1.0 / math.sqrt(HEAD_SIZE)
    gain_part = lax.dynamic_slice_in_dim(norm_gain, tensor_index * width_part, width_part)
    x_float = tokens.astype(jnp.float32)

    block_count = block_owner.shape[1]
    owner_row = lax.dynamic_slice_in_dim(block_owner, data_index, 1, 0)[0]
    slot_index = jnp.arange(sources, dtype=jnp.int32)
    send_table = (owner_row[None, :] == slot_index[:, None]).astype(jnp.bfloat16)

    home_rows = token_row_count // block_count
    owned_blocks = grad_output.reshape(block_count, home_rows, width_part)
    if sources <= 16:
        returned = [lax.dynamic_index_in_dim(owned_blocks, data_index, 0, keepdims=False)]
        for shift in range(1, sources):
            pairs = [(a, (a + shift) % sources) for a in range(sources)]
            piece = lax.dynamic_index_in_dim(
                owned_blocks, (data_index + shift) % sources, 0, keepdims=False
            )
            returned.append(lax.ppermute(piece, "dp", pairs))
        returned = jnp.stack(returned)
        came_over = (
            ((data_index - owner_row) % sources)[:, None] == slot_index[None, :]
        ).astype(jnp.bfloat16)
        grad_home = (
            jnp.einsum("js,srw->jrw", came_over, returned, preferred_element_type=jnp.float32)
            .astype(jnp.bfloat16)
            .reshape(token_row_count, width_part)
        )
    else:
        arrived = lax.all_to_all(
            owned_blocks.reshape(block_count, -1), "dp", split_axis=0, concat_axis=0, tiled=True
        )
        grad_home = (
            lax.dot_general(
                send_table, arrived, (((0,), (0,)), ((), ())), preferred_element_type=jnp.float32
            )
            .astype(jnp.bfloat16)
            .reshape(token_row_count, width_part)
        )

    gathered = lax.all_gather(tokens, "tensor", axis=1, tiled=True)
    gathered_float = gathered.astype(jnp.float32)
    inverse = lax.rsqrt(jnp.mean(gathered_float * gathered_float, axis=1) + NORM_EPSILON)
    normed_input = (gathered_float * inverse[:, None] * norm_gain[None, :]).astype(jnp.bfloat16)
    query_raw = jnp.dot(normed_input, w_query, preferred_element_type=jnp.float32)
    key_raw = jnp.dot(normed_input, key_weight, preferred_element_type=jnp.float32)
    value_raw = jnp.dot(normed_input, value_weight, preferred_element_type=jnp.float32)
    doc_ids, positions = doc_tables(doc_lengths[0], token_row_count)
    token_index = jnp.arange(token_row_count, dtype=jnp.int32)
    allowed = (doc_ids[:, None] == doc_ids[None, :]) & (
        token_index[None, :] <= token_index[:, None]
    )
    cosine, sine_table = rope_tables(positions, HEAD_SIZE)
    query_rows = rotate(
        query_raw.reshape(token_row_count, heads_local, HEAD_SIZE), cosine, sine_table
    ).astype(jnp.bfloat16)
    keys = rotate(
        key_raw.reshape(token_row_count, kv_local, HEAD_SIZE), cosine, sine_table
    ).astype(jnp.bfloat16)
    value_rows = value_raw.astype(jnp.bfloat16).reshape(token_row_count, kv_local, HEAD_SIZE)
    grouped_query = query_rows.reshape(token_row_count, kv_local, query_group_width, HEAD_SIZE)
    scores = (
        jnp.einsum("qkgd,skd->kgqs", grouped_query, keys, preferred_element_type=jnp.float32)
        * scale_factor
    )
    weights = jnp.where(allowed[None, None], jnp.exp(scores), 0.0)
    probs = weights / jnp.sum(weights, axis=-1, keepdims=True)
    probs_low = probs.astype(jnp.bfloat16)
    attended = jnp.einsum(
        "kgqs,skd->qkgd", probs_low, value_rows, preferred_element_type=jnp.float32
    ).astype(jnp.bfloat16)
    attended_flat = attended.reshape(token_row_count, query_width)
    mixed_partial = jnp.dot(attended_flat, w_out, preferred_element_type=jnp.float32)
    grad_full = lax.all_gather(grad_home, "tensor", axis=1, tiled=True)
    mixed_partial, grad_full = lax.optimization_barrier((mixed_partial, grad_full))
    attended_gradient = lax.dot_general(
        grad_full,
        w_out,
        (((1,), (1,)), ((), ())),
        preferred_element_type=jnp.float32,
    ).astype(jnp.bfloat16)
    mixed, _, (attended_gradient,) = scatter_features(
        mixed_partial, "tensor", tensor_size, tensor_index, ties=(attended_gradient,)
    )
    output_home = (x_float + mixed).astype(jnp.bfloat16)
    grouped_gradient = attended_gradient.reshape(
        token_row_count, kv_local, query_group_width, HEAD_SIZE
    )
    delta = jnp.sum(grouped_gradient.astype(jnp.float32) * attended.astype(jnp.float32), axis=-1)
    grad_probs = jnp.einsum(
        "qkgd,skd->kgqs", grouped_gradient, value_rows, preferred_element_type=jnp.float32
    )
    grad_scores = (probs * (grad_probs - jnp.transpose(delta, (1, 2, 0))[..., None])).astype(
        jnp.bfloat16
    )
    grad_query_rot = (
        jnp.einsum("kgqs,skd->qkgd", grad_scores, keys, preferred_element_type=jnp.float32)
        * scale_factor
    )
    grad_keys_rot = (
        jnp.einsum("kgqs,qkgd->skd", grad_scores, grouped_query, preferred_element_type=jnp.float32)
        * scale_factor
    )
    value_gradient = jnp.einsum(
        "kgqs,qkgd->skd", probs_low, grouped_gradient, preferred_element_type=jnp.float32
    )
    grad_query = unrotate(
        grad_query_rot.reshape(token_row_count, heads_local, HEAD_SIZE), cosine, sine_table
    ).astype(jnp.bfloat16)
    key_gradient = unrotate(grad_keys_rot, cosine, sine_table).astype(jnp.bfloat16)
    contract_out = (((1,), (1,)), ((), ()))
    normed_partial = (
        lax.dot_general(
            grad_query.reshape(token_row_count, query_width),
            w_query,
            contract_out,
            preferred_element_type=jnp.float32,
        )
        + lax.dot_general(
            key_gradient.reshape(token_row_count, key_width),
            key_weight,
            contract_out,
            preferred_element_type=jnp.float32,
        )
        + lax.dot_general(
            value_gradient.astype(jnp.bfloat16).reshape(token_row_count, key_width),
            value_weight,
            contract_out,
            preferred_element_type=jnp.float32,
        )
    )
    stat_partial = jnp.sum(normed_partial * norm_gain[None, :] * gathered_float, axis=1)
    home_blocks = output_home.reshape(block_count, home_rows, width_part)
    outgoing = jnp.einsum(
        "dj,jrw->drw", send_table, home_blocks, preferred_element_type=jnp.float32
    ).astype(jnp.bfloat16)
    normed_gradient, stat_sum, (outgoing,) = scatter_features(
        normed_partial, "tensor", tensor_size, tensor_index, extra=stat_partial, ties=(outgoing,)
    )
    relaid = lax.all_to_all(outgoing, "dp", split_axis=0, concat_axis=0, tiled=True).reshape(
        token_row_count, width_part
    )
    stat = stat_sum / full_width
    cubed = inverse * inverse * inverse
    grad_x = (
        grad_home.astype(jnp.float32)
        + inverse[:, None] * gain_part[None, :] * normed_gradient
        - x_float * cubed[:, None] * stat[:, None]
    )
    return (relaid, grad_x.astype(jnp.bfloat16))


def solution(mesh):
    placed = (
        P("dp", "tensor"),
        P(),
        P(None, "tensor"),
        P(None, "tensor"),
        P(None, "tensor"),
        P("tensor", None),
        P("dp", "tensor"),
        P("dp", None),
        P(),
    )
    return jax.shard_map(
        per_device,
        mesh=mesh,
        in_specs=placed,
        out_specs=(P("dp", "tensor"), P("dp", "tensor")),
        check_vma=False,
    )
```

```python
import math

import jax
import jax.numpy as jnp
from jax import lax
from jax.sharding import PartitionSpec as P

HEAD_SIZE = 128


ROPE_BASE = 500000.0
NORM_EPSILON = 1e-05


def doc_tables(lengths_row, token_row_count):
    ends = jnp.cumsum(lengths_row)
    token_index = jnp.arange(token_row_count, dtype=jnp.int32)
    passed = (token_index[:, None] >= ends[None, :]).astype(jnp.int32)
    doc_ids = jnp.sum(passed, axis=1)
    starts = jnp.max(jnp.where(passed > 0, ends[None, :], 0), axis=1)
    return (doc_ids, token_index - starts)


def rope_tables(positions, head_size):
    half_dim = head_size // 2
    steps = jnp.arange(half_dim, dtype=jnp.float32)
    inverse_freq = jnp.power(ROPE_BASE, -2.0 * steps / head_size)
    angles = positions.astype(jnp.float32)[:, None] * inverse_freq[None, :]
    return (jnp.cos(angles), jnp.sin(angles))


def rotate(vectors, cosine, sine_table):
    half_dim = vectors.shape[-1] // 2
    former = vectors[..., :half_dim]
    latter = vectors[..., half_dim:]
    cos_part = cosine[:, None, :]
    sin_part = sine_table[:, None, :]
    return jnp.concatenate(
        [former * cos_part - latter * sin_part, latter * cos_part + former * sin_part], axis=-1
    )


def unrotate(vectors, cosine, sine_table):
    half_dim = vectors.shape[-1] // 2
    former = vectors[..., :half_dim]
    latter = vectors[..., half_dim:]
    cos_part = cosine[:, None, :]
    sin_part = sine_table[:, None, :]
    return jnp.concatenate(
        [former * cos_part + latter * sin_part, latter * cos_part - former * sin_part], axis=-1
    )


def _is_pow2(n):
    return n > 1 and (n & (n - 1)) == 0


def _xor_pairs(size, bit):
    return [(i, i ^ bit) for i in range(size)]


def gather_features(shard, axis_name, size, position):
    if not _is_pow2(size):
        return lax.all_gather(shard, axis_name, axis=1, tiled=True)
    held = shard[None]
    masks = [0]
    bit = size >> 1
    while bit:
        incoming = lax.ppermute(held, axis_name, _xor_pairs(size, bit))
        held = jnp.concatenate([held, incoming], axis=0)
        masks = masks + [m ^ bit for m in masks]
        bit >>= 1
    table = jnp.asarray([masks.index(m) for m in range(size)], jnp.int32)
    blocks = [
        lax.dynamic_index_in_dim(held, table[s ^ position], axis=0, keepdims=False)
        for s in range(size)
    ]
    return jnp.concatenate(blocks, axis=1)


def scatter_features(partial, axis_name, size, position, extra=None, ties=()):
    width = partial.shape[1] // size
    if not _is_pow2(size):
        summed = lax.psum_scatter(
            partial.astype(jnp.bfloat16), axis_name, scatter_dimension=1, tiled=True
        )
        if extra is not None:
            extra = lax.psum(extra, axis_name)
        return summed.astype(jnp.float32), extra, ties
    held = [
        lax.dynamic_slice_in_dim(partial, (position ^ m) * width, width, axis=1)
        for m in range(size)
    ]
    masks = list(range(size))
    done_ties = []
    bit = 1
    while bit < size:
        keep = [i for i, m in enumerate(masks) if not m & bit]
        send = [i for i, m in enumerate(masks) if m & bit]
        outgoing = jnp.stack([held[i] for i in send]).astype(jnp.bfloat16)
        if extra is None:
            incoming = lax.ppermute(outgoing, axis_name, _xor_pairs(size, bit))
        else:
            incoming, extra_in = lax.ppermute((outgoing, extra), axis_name, _xor_pairs(size, bit))
            extra = extra + extra_in
        if ties:
            incoming, first = lax.optimization_barrier((incoming, ties[0]))
            ties = ties[1:]
            done_ties.append(first)
        sent_masks = [masks[i] ^ bit for i in send]
        held = [
            held[i] + incoming[sent_masks.index(masks[i])].astype(jnp.float32) for i in keep
        ]
        masks = [masks[i] for i in keep]
        bit <<= 1
    return held[0], extra, tuple(done_ties) + tuple(ties)


def per_device(
    tokens,
    norm_gain,
    w_query,
    key_weight,
    value_weight,
    w_out,
    grad_output,
    doc_lengths,
    block_owner,
):
    token_row_count, width_part = tokens.shape
    full_width = norm_gain.shape[0]
    sources = lax.axis_size("dp")
    tensor_size = lax.axis_size("tensor")
    data_index = lax.axis_index("dp")
    tensor_index = lax.axis_index("tensor")
    query_width = w_query.shape[1]
    key_width = key_weight.shape[1]
    heads_local = query_width // HEAD_SIZE
    kv_local = key_width // HEAD_SIZE
    query_group_width = heads_local // kv_local
    scale_factor = 1.0 / math.sqrt(HEAD_SIZE)
    gain_part = lax.dynamic_slice_in_dim(norm_gain, tensor_index * width_part, width_part)
    x_float = tokens.astype(jnp.float32)

    block_count = block_owner.shape[1]
    owner_row = lax.dynamic_slice_in_dim(block_owner, data_index, 1, 0)[0]
    slot_index = jnp.arange(sources, dtype=jnp.int32)
    send_table = (owner_row[None, :] == slot_index[:, None]).astype(jnp.bfloat16)

    home_rows = token_row_count // block_count
    owned_blocks = grad_output.reshape(block_count, home_rows, width_part)
    if sources <= 16:
        returned = [lax.dynamic_index_in_dim(owned_blocks, data_index, 0, keepdims=False)]
        for shift in range(1, sources):
            pairs = [(a, (a + shift) % sources) for a in range(sources)]
            piece = lax.dynamic_index_in_dim(
                owned_blocks, (data_index + shift) % sources, 0, keepdims=False
            )
            returned.append(lax.ppermute(piece, "dp", pairs))
        returned = jnp.stack(returned)
        came_over = (
            ((data_index - owner_row) % sources)[:, None] == slot_index[None, :]
        ).astype(jnp.bfloat16)
        grad_home = (
            jnp.einsum("js,srw->jrw", came_over, returned, preferred_element_type=jnp.float32)
            .astype(jnp.bfloat16)
            .reshape(token_row_count, width_part)
        )
    else:
        arrived = lax.all_to_all(
            owned_blocks.reshape(block_count, -1), "dp", split_axis=0, concat_axis=0, tiled=True
        )
        grad_home = (
            lax.dot_general(
                send_table, arrived, (((0,), (0,)), ((), ())), preferred_element_type=jnp.float32
            )
            .astype(jnp.bfloat16)
            .reshape(token_row_count, width_part)
        )

    gathered = lax.all_gather(tokens, "tensor", axis=1, tiled=True)
    gathered_float = gathered.astype(jnp.float32)
    inverse = lax.rsqrt(jnp.mean(gathered_float * gathered_float, axis=1) + NORM_EPSILON)
    normed_input = (gathered_float * inverse[:, None] * norm_gain[None, :]).astype(jnp.bfloat16)
    query_raw = jnp.dot(normed_input, w_query, preferred_element_type=jnp.float32)
    key_raw = jnp.dot(normed_input, key_weight, preferred_element_type=jnp.float32)
    value_raw = jnp.dot(normed_input, value_weight, preferred_element_type=jnp.float32)
    doc_ids, positions = doc_tables(doc_lengths[0], token_row_count)
    token_index = jnp.arange(token_row_count, dtype=jnp.int32)
    allowed = (doc_ids[:, None] == doc_ids[None, :]) & (
        token_index[None, :] <= token_index[:, None]
    )
    cosine, sine_table = rope_tables(positions, HEAD_SIZE)
    query_rows = rotate(
        query_raw.reshape(token_row_count, heads_local, HEAD_SIZE), cosine, sine_table
    ).astype(jnp.bfloat16)
    keys = rotate(
        key_raw.reshape(token_row_count, kv_local, HEAD_SIZE), cosine, sine_table
    ).astype(jnp.bfloat16)
    value_rows = value_raw.astype(jnp.bfloat16).reshape(token_row_count, kv_local, HEAD_SIZE)
    grouped_query = query_rows.reshape(token_row_count, kv_local, query_group_width, HEAD_SIZE)
    scores = (
        jnp.einsum("qkgd,skd->kgqs", grouped_query, keys, preferred_element_type=jnp.float32)
        * scale_factor
    )
    weights = jnp.where(allowed[None, None], jnp.exp(scores), 0.0)
    probs = weights / jnp.sum(weights, axis=-1, keepdims=True)
    probs_low = probs.astype(jnp.bfloat16)
    attended = jnp.einsum(
        "kgqs,skd->qkgd", probs_low, value_rows, preferred_element_type=jnp.float32
    ).astype(jnp.bfloat16)
    attended_flat = attended.reshape(token_row_count, query_width)
    mixed_partial = jnp.dot(attended_flat, w_out, preferred_element_type=jnp.float32)
    grad_full = lax.all_gather(grad_home, "tensor", axis=1, tiled=True)
    mixed_partial, grad_full = lax.optimization_barrier((mixed_partial, grad_full))
    attended_gradient = lax.dot_general(
        grad_full,
        w_out,
        (((1,), (1,)), ((), ())),
        preferred_element_type=jnp.float32,
    ).astype(jnp.bfloat16)
    mixed, _, (attended_gradient,) = scatter_features(
        mixed_partial, "tensor", tensor_size, tensor_index, ties=(attended_gradient,)
    )
    output_home = (x_float + mixed).astype(jnp.bfloat16)
    grouped_gradient = attended_gradient.reshape(
        token_row_count, kv_local, query_group_width, HEAD_SIZE
    )
    delta = jnp.sum(grouped_gradient.astype(jnp.float32) * attended.astype(jnp.float32), axis=-1)
    grad_probs = jnp.einsum(
        "qkgd,skd->kgqs", grouped_gradient, value_rows, preferred_element_type=jnp.float32
    )
    grad_scores = (probs * (grad_probs - jnp.transpose(delta, (1, 2, 0))[..., None])).astype(
        jnp.bfloat16
    )
    grad_query_rot = (
        jnp.einsum("kgqs,skd->qkgd", grad_scores, keys, preferred_element_type=jnp.float32)
        * scale_factor
    )
    grad_keys_rot = (
        jnp.einsum("kgqs,qkgd->skd", grad_scores, grouped_query, preferred_element_type=jnp.float32)
        * scale_factor
    )
    value_gradient = jnp.einsum(
        "kgqs,qkgd->skd", probs_low, grouped_gradient, preferred_element_type=jnp.float32
    )
    grad_query = unrotate(
        grad_query_rot.reshape(token_row_count, heads_local, HEAD_SIZE), cosine, sine_table
    ).astype(jnp.bfloat16)
    key_gradient = unrotate(grad_keys_rot, cosine, sine_table).astype(jnp.bfloat16)
    contract_out = (((1,), (1,)), ((), ()))
    normed_partial = (
        lax.dot_general(
            grad_query.reshape(token_row_count, query_width),
            w_query,
            contract_out,
            preferred_element_type=jnp.float32,
        )
        + lax.dot_general(
            key_gradient.reshape(token_row_count, key_width),
            key_weight,
            contract_out,
            preferred_element_type=jnp.float32,
        )
        + lax.dot_general(
            value_gradient.astype(jnp.bfloat16).reshape(token_row_count, key_width),
            value_weight,
            contract_out,
            preferred_element_type=jnp.float32,
        )
    )
    output_home, normed_partial = lax.optimization_barrier((output_home, normed_partial))
    stat_partial = jnp.sum(normed_partial * norm_gain[None, :] * gathered_float, axis=1)
    home_blocks = output_home.reshape(block_count, home_rows, width_part)
    outgoing = jnp.einsum(
        "dj,jrw->drw", send_table, home_blocks, preferred_element_type=jnp.float32
    ).astype(jnp.bfloat16)
    normed_gradient, stat_sum, (outgoing,) = scatter_features(
        normed_partial, "tensor", tensor_size, tensor_index, extra=stat_partial, ties=(outgoing,)
    )
    relaid = lax.all_to_all(outgoing, "dp", split_axis=0, concat_axis=0, tiled=True).reshape(
        token_row_count, width_part
    )
    relaid, stat_sum = lax.optimization_barrier((relaid, stat_sum))
    stat = stat_sum / full_width
    cubed = inverse * inverse * inverse
    grad_x = (
        grad_home.astype(jnp.float32)
        + inverse[:, None] * gain_part[None, :] * normed_gradient
        - x_float * cubed[:, None] * stat[:, None]
    )
    return (relaid, grad_x.astype(jnp.bfloat16))


def solution(mesh):
    placed = (
        P("dp", "tensor"),
        P(),
        P(None, "tensor"),
        P(None, "tensor"),
        P(None, "tensor"),
        P("tensor", None),
        P("dp", "tensor"),
        P("dp", None),
        P(),
    )
    return jax.shard_map(
        per_device,
        mesh=mesh,
        in_specs=placed,
        out_specs=(P("dp", "tensor"), P("dp", "tensor")),
        check_vma=False,
    )
```

```python
import math

import jax
import jax.numpy as jnp
from jax import lax
from jax.sharding import PartitionSpec as P

HEAD_SIZE = 128


ROPE_BASE = 500000.0
NORM_EPSILON = 1e-05


def doc_tables(lengths_row, token_row_count):
    ends = jnp.cumsum(lengths_row)
    token_index = jnp.arange(token_row_count, dtype=jnp.int32)
    passed = (token_index[:, None] >= ends[None, :]).astype(jnp.int32)
    doc_ids = jnp.sum(passed, axis=1)
    starts = jnp.max(jnp.where(passed > 0, ends[None, :], 0), axis=1)
    return (doc_ids, token_index - starts)


def rope_tables(positions, head_size):
    half_dim = head_size // 2
    steps = jnp.arange(half_dim, dtype=jnp.float32)
    inverse_freq = jnp.power(ROPE_BASE, -2.0 * steps / head_size)
    angles = positions.astype(jnp.float32)[:, None] * inverse_freq[None, :]
    return (jnp.cos(angles), jnp.sin(angles))


def rotate(vectors, cosine, sine_table):
    half_dim = vectors.shape[-1] // 2
    former = vectors[..., :half_dim]
    latter = vectors[..., half_dim:]
    cos_part = cosine[:, None, :]
    sin_part = sine_table[:, None, :]
    return jnp.concatenate(
        [former * cos_part - latter * sin_part, latter * cos_part + former * sin_part], axis=-1
    )


def unrotate(vectors, cosine, sine_table):
    half_dim = vectors.shape[-1] // 2
    former = vectors[..., :half_dim]
    latter = vectors[..., half_dim:]
    cos_part = cosine[:, None, :]
    sin_part = sine_table[:, None, :]
    return jnp.concatenate(
        [former * cos_part + latter * sin_part, latter * cos_part - former * sin_part], axis=-1
    )


def _is_pow2(n):
    return n > 1 and (n & (n - 1)) == 0


def _xor_pairs(size, bit):
    return [(i, i ^ bit) for i in range(size)]


def gather_features(shard, axis_name, size, position):
    if not _is_pow2(size):
        return lax.all_gather(shard, axis_name, axis=1, tiled=True)
    held = shard[None]
    masks = [0]
    bit = size >> 1
    while bit:
        incoming = lax.ppermute(held, axis_name, _xor_pairs(size, bit))
        held = jnp.concatenate([held, incoming], axis=0)
        masks = masks + [m ^ bit for m in masks]
        bit >>= 1
    table = jnp.asarray([masks.index(m) for m in range(size)], jnp.int32)
    blocks = [
        lax.dynamic_index_in_dim(held, table[s ^ position], axis=0, keepdims=False)
        for s in range(size)
    ]
    return jnp.concatenate(blocks, axis=1)


def scatter_features(partial, axis_name, size, position, extra=None, ties=()):
    if not _is_pow2(size) and isinstance(partial, list):
        partial = jnp.concatenate(partial, axis=1)
    width = None if isinstance(partial, list) else partial.shape[1] // size
    if not _is_pow2(size):
        summed = lax.psum_scatter(
            partial.astype(jnp.bfloat16), axis_name, scatter_dimension=1, tiled=True
        )
        if extra is not None:
            extra = lax.psum(extra, axis_name)
        return summed.astype(jnp.float32), extra, ties
    if isinstance(partial, list):
        held = list(partial)
    else:
        held = [
            lax.dynamic_slice_in_dim(partial, (position ^ m) * width, width, axis=1)
            for m in range(size)
        ]
    masks = list(range(size))
    done_ties = []
    bit = 1
    while bit < size:
        keep = [i for i, m in enumerate(masks) if not m & bit]
        send = [i for i, m in enumerate(masks) if m & bit]
        outgoing = jnp.stack([held[i] for i in send]).astype(jnp.bfloat16)
        if extra is None:
            incoming = lax.ppermute(outgoing, axis_name, _xor_pairs(size, bit))
        else:
            incoming, extra_in = lax.ppermute((outgoing, extra), axis_name, _xor_pairs(size, bit))
            extra = extra + extra_in
        if ties:
            incoming, first = lax.optimization_barrier((incoming, ties[0]))
            ties = ties[1:]
            done_ties.append(first)
        sent_masks = [masks[i] ^ bit for i in send]
        held = [
            held[i] + incoming[sent_masks.index(masks[i])].astype(jnp.float32) for i in keep
        ]
        masks = [masks[i] for i in keep]
        bit <<= 1
    return held[0], extra, tuple(done_ties) + tuple(ties)


def per_device(
    tokens,
    norm_gain,
    w_query,
    key_weight,
    value_weight,
    w_out,
    grad_output,
    doc_lengths,
    block_owner,
):
    token_row_count, width_part = tokens.shape
    full_width = norm_gain.shape[0]
    sources = lax.axis_size("dp")
    tensor_size = lax.axis_size("tensor")
    data_index = lax.axis_index("dp")
    tensor_index = lax.axis_index("tensor")
    query_width = w_query.shape[1]
    key_width = key_weight.shape[1]
    heads_local = query_width // HEAD_SIZE
    kv_local = key_width // HEAD_SIZE
    query_group_width = heads_local // kv_local
    scale_factor = 1.0 / math.sqrt(HEAD_SIZE)
    gain_part = lax.dynamic_slice_in_dim(norm_gain, tensor_index * width_part, width_part)
    x_float = tokens.astype(jnp.float32)

    block_count = block_owner.shape[1]
    owner_row = lax.dynamic_slice_in_dim(block_owner, data_index, 1, 0)[0]
    slot_index = jnp.arange(sources, dtype=jnp.int32)
    send_table = (owner_row[None, :] == slot_index[:, None]).astype(jnp.bfloat16)

    home_rows = token_row_count // block_count
    owned_blocks = grad_output.reshape(block_count, home_rows, width_part)
    if sources <= 16:
        returned = [lax.dynamic_index_in_dim(owned_blocks, data_index, 0, keepdims=False)]
        for shift in range(1, sources):
            pairs = [(a, (a + shift) % sources) for a in range(sources)]
            piece = lax.dynamic_index_in_dim(
                owned_blocks, (data_index + shift) % sources, 0, keepdims=False
            )
            returned.append(lax.ppermute(piece, "dp", pairs))
        returned = jnp.stack(returned)
        came_over = (
            ((data_index - owner_row) % sources)[:, None] == slot_index[None, :]
        ).astype(jnp.bfloat16)
        grad_home = (
            jnp.einsum("js,srw->jrw", came_over, returned, preferred_element_type=jnp.float32)
            .astype(jnp.bfloat16)
            .reshape(token_row_count, width_part)
        )
    else:
        arrived = lax.all_to_all(
            owned_blocks.reshape(block_count, -1), "dp", split_axis=0, concat_axis=0, tiled=True
        )
        grad_home = (
            lax.dot_general(
                send_table, arrived, (((0,), (0,)), ((), ())), preferred_element_type=jnp.float32
            )
            .astype(jnp.bfloat16)
            .reshape(token_row_count, width_part)
        )

    gathered = lax.all_gather(tokens, "tensor", axis=1, tiled=True)
    gathered_float = gathered.astype(jnp.float32)
    inverse = lax.rsqrt(jnp.mean(gathered_float * gathered_float, axis=1) + NORM_EPSILON)
    normed_input = (gathered_float * inverse[:, None] * norm_gain[None, :]).astype(jnp.bfloat16)
    query_raw = jnp.dot(normed_input, w_query, preferred_element_type=jnp.float32)
    key_raw = jnp.dot(normed_input, key_weight, preferred_element_type=jnp.float32)
    value_raw = jnp.dot(normed_input, value_weight, preferred_element_type=jnp.float32)
    doc_ids, positions = doc_tables(doc_lengths[0], token_row_count)
    token_index = jnp.arange(token_row_count, dtype=jnp.int32)
    allowed = (doc_ids[:, None] == doc_ids[None, :]) & (
        token_index[None, :] <= token_index[:, None]
    )
    cosine, sine_table = rope_tables(positions, HEAD_SIZE)
    query_rows = rotate(
        query_raw.reshape(token_row_count, heads_local, HEAD_SIZE), cosine, sine_table
    ).astype(jnp.bfloat16)
    keys = rotate(
        key_raw.reshape(token_row_count, kv_local, HEAD_SIZE), cosine, sine_table
    ).astype(jnp.bfloat16)
    value_rows = value_raw.astype(jnp.bfloat16).reshape(token_row_count, kv_local, HEAD_SIZE)
    grouped_query = query_rows.reshape(token_row_count, kv_local, query_group_width, HEAD_SIZE)
    scores = (
        jnp.einsum("qkgd,skd->kgqs", grouped_query, keys, preferred_element_type=jnp.float32)
        * scale_factor
    )
    weights = jnp.where(allowed[None, None], jnp.exp(scores), 0.0)
    probs = weights / jnp.sum(weights, axis=-1, keepdims=True)
    probs_low = probs.astype(jnp.bfloat16)
    attended = jnp.einsum(
        "kgqs,skd->qkgd", probs_low, value_rows, preferred_element_type=jnp.float32
    ).astype(jnp.bfloat16)
    attended_flat = attended.reshape(token_row_count, query_width)
    mixed_partial = jnp.dot(attended_flat, w_out, preferred_element_type=jnp.float32)
    grad_full = lax.all_gather(grad_home, "tensor", axis=1, tiled=True)
    mixed_partial, grad_full = lax.optimization_barrier((mixed_partial, grad_full))
    attended_gradient = lax.dot_general(
        grad_full,
        w_out,
        (((1,), (1,)), ((), ())),
        preferred_element_type=jnp.float32,
    ).astype(jnp.bfloat16)
    mixed, _, (attended_gradient,) = scatter_features(
        mixed_partial, "tensor", tensor_size, tensor_index, ties=(attended_gradient,)
    )
    output_home = (x_float + mixed).astype(jnp.bfloat16)
    grouped_gradient = attended_gradient.reshape(
        token_row_count, kv_local, query_group_width, HEAD_SIZE
    )
    delta = jnp.sum(grouped_gradient.astype(jnp.float32) * attended.astype(jnp.float32), axis=-1)
    grad_probs = jnp.einsum(
        "qkgd,skd->kgqs", grouped_gradient, value_rows, preferred_element_type=jnp.float32
    )
    grad_scores = (probs * (grad_probs - jnp.transpose(delta, (1, 2, 0))[..., None])).astype(
        jnp.bfloat16
    )
    grad_query_rot = (
        jnp.einsum("kgqs,skd->qkgd", grad_scores, keys, preferred_element_type=jnp.float32)
        * scale_factor
    )
    grad_keys_rot = (
        jnp.einsum("kgqs,qkgd->skd", grad_scores, grouped_query, preferred_element_type=jnp.float32)
        * scale_factor
    )
    value_gradient = jnp.einsum(
        "kgqs,qkgd->skd", probs_low, grouped_gradient, preferred_element_type=jnp.float32
    )
    grad_query = unrotate(
        grad_query_rot.reshape(token_row_count, heads_local, HEAD_SIZE), cosine, sine_table
    ).astype(jnp.bfloat16)
    key_gradient = unrotate(grad_keys_rot, cosine, sine_table).astype(jnp.bfloat16)
    contract_out = (((1,), (1,)), ((), ()))
    grad_query_flat = grad_query.reshape(token_row_count, query_width)
    grad_key_flat = key_gradient.reshape(token_row_count, key_width)
    grad_value_flat = value_gradient.astype(jnp.bfloat16).reshape(token_row_count, key_width)

    def normed_block(shard):
        start = shard * width_part
        return (
            lax.dot_general(
                grad_query_flat,
                lax.dynamic_slice_in_dim(w_query, start, width_part, axis=0),
                contract_out,
                preferred_element_type=jnp.float32,
            )
            + lax.dot_general(
                grad_key_flat,
                lax.dynamic_slice_in_dim(key_weight, start, width_part, axis=0),
                contract_out,
                preferred_element_type=jnp.float32,
            )
            + lax.dot_general(
                grad_value_flat,
                lax.dynamic_slice_in_dim(value_weight, start, width_part, axis=0),
                contract_out,
                preferred_element_type=jnp.float32,
            )
        )

    if _is_pow2(tensor_size):
        shard_of = [tensor_index ^ m for m in range(tensor_size)]
    else:
        shard_of = list(range(tensor_size))
    parts = [normed_block(s) for s in shard_of]
    stat_partial = sum(
        jnp.sum(
            part
            * lax.dynamic_slice_in_dim(norm_gain, s * width_part, width_part)[None, :]
            * lax.dynamic_slice_in_dim(gathered_float, s * width_part, width_part, axis=1),
            axis=1,
        )
        for s, part in zip(shard_of, parts)
    )
    home_blocks = output_home.reshape(block_count, home_rows, width_part)
    outgoing = jnp.einsum(
        "dj,jrw->drw", send_table, home_blocks, preferred_element_type=jnp.float32
    ).astype(jnp.bfloat16)
    normed_gradient, stat_sum, (outgoing,) = scatter_features(
        parts, "tensor", tensor_size, tensor_index, extra=stat_partial, ties=(outgoing,)
    )
    relaid = lax.all_to_all(outgoing, "dp", split_axis=0, concat_axis=0, tiled=True).reshape(
        token_row_count, width_part
    )
    stat = stat_sum / full_width
    cubed = inverse * inverse * inverse
    grad_x = (
        grad_home.astype(jnp.float32)
        + inverse[:, None] * gain_part[None, :] * normed_gradient
        - x_float * cubed[:, None] * stat[:, None]
    )
    return (relaid, grad_x.astype(jnp.bfloat16))


def solution(mesh):
    placed = (
        P("dp", "tensor"),
        P(),
        P(None, "tensor"),
        P(None, "tensor"),
        P(None, "tensor"),
        P("tensor", None),
        P("dp", "tensor"),
        P("dp", None),
        P(),
    )
    return jax.shard_map(
        per_device,
        mesh=mesh,
        in_specs=placed,
        out_specs=(P("dp", "tensor"), P("dp", "tensor")),
        check_vma=False,
    )
```

```python
import math

import jax
import jax.numpy as jnp
from jax import lax
from jax.sharding import PartitionSpec as P

HEAD_SIZE = 128


ROPE_BASE = 500000.0
NORM_EPSILON = 1e-05


def doc_tables(lengths_row, token_row_count):
    ends = jnp.cumsum(lengths_row)
    token_index = jnp.arange(token_row_count, dtype=jnp.int32)
    passed = (token_index[:, None] >= ends[None, :]).astype(jnp.int32)
    doc_ids = jnp.sum(passed, axis=1)
    starts = jnp.max(jnp.where(passed > 0, ends[None, :], 0), axis=1)
    return (doc_ids, token_index - starts)


def rope_tables(positions, head_size):
    half_dim = head_size // 2
    steps = jnp.arange(half_dim, dtype=jnp.float32)
    inverse_freq = jnp.power(ROPE_BASE, -2.0 * steps / head_size)
    angles = positions.astype(jnp.float32)[:, None] * inverse_freq[None, :]
    return (jnp.cos(angles), jnp.sin(angles))


def rotate(vectors, cosine, sine_table):
    half_dim = vectors.shape[-1] // 2
    former = vectors[..., :half_dim]
    latter = vectors[..., half_dim:]
    cos_part = cosine[:, None, :]
    sin_part = sine_table[:, None, :]
    return jnp.concatenate(
        [former * cos_part - latter * sin_part, latter * cos_part + former * sin_part], axis=-1
    )


def unrotate(vectors, cosine, sine_table):
    half_dim = vectors.shape[-1] // 2
    former = vectors[..., :half_dim]
    latter = vectors[..., half_dim:]
    cos_part = cosine[:, None, :]
    sin_part = sine_table[:, None, :]
    return jnp.concatenate(
        [former * cos_part + latter * sin_part, latter * cos_part - former * sin_part], axis=-1
    )


def _is_pow2(n):
    return n > 1 and (n & (n - 1)) == 0


def _xor_pairs(size, bit):
    return [(i, i ^ bit) for i in range(size)]


def gather_features(shard, axis_name, size, position, tied=None):
    if not _is_pow2(size):
        return lax.all_gather(shard, axis_name, axis=1, tiled=True), tied
    held = shard[None]
    masks = [0]
    tied_done = tied
    bit = size >> 1
    while bit:
        incoming = lax.ppermute(held, axis_name, _xor_pairs(size, bit))
        if tied is not None:
            incoming, tied = lax.optimization_barrier((incoming, tied))
            tied_done = tied
            tied = None
        held = jnp.concatenate([held, incoming], axis=0)
        masks = masks + [m ^ bit for m in masks]
        bit >>= 1
    table = jnp.asarray([masks.index(m) for m in range(size)], jnp.int32)
    blocks = [
        lax.dynamic_index_in_dim(held, table[s ^ position], axis=0, keepdims=False)
        for s in range(size)
    ]
    return jnp.concatenate(blocks, axis=1), tied_done


def scatter_features(partial, axis_name, size, position, extra=None, ties=()):
    width = partial.shape[1] // size
    if not _is_pow2(size):
        summed = lax.psum_scatter(
            partial.astype(jnp.bfloat16), axis_name, scatter_dimension=1, tiled=True
        )
        if extra is not None:
            extra = lax.psum(extra, axis_name)
        return summed.astype(jnp.float32), extra, ties
    held = [
        lax.dynamic_slice_in_dim(partial, (position ^ m) * width, width, axis=1)
        for m in range(size)
    ]
    masks = list(range(size))
    done_ties = []
    bit = 1
    while bit < size:
        keep = [i for i, m in enumerate(masks) if not m & bit]
        send = [i for i, m in enumerate(masks) if m & bit]
        outgoing = jnp.stack([held[i] for i in send]).astype(jnp.bfloat16)
        if extra is None:
            incoming = lax.ppermute(outgoing, axis_name, _xor_pairs(size, bit))
        else:
            incoming, extra_in = lax.ppermute((outgoing, extra), axis_name, _xor_pairs(size, bit))
            extra = extra + extra_in
        if ties:
            incoming, first = lax.optimization_barrier((incoming, ties[0]))
            ties = ties[1:]
            done_ties.append(first)
        sent_masks = [masks[i] ^ bit for i in send]
        held = [
            held[i] + incoming[sent_masks.index(masks[i])].astype(jnp.float32) for i in keep
        ]
        masks = [masks[i] for i in keep]
        bit <<= 1
    return held[0], extra, tuple(done_ties) + tuple(ties)


def per_device(
    tokens,
    norm_gain,
    w_query,
    key_weight,
    value_weight,
    w_out,
    grad_output,
    doc_lengths,
    block_owner,
):
    token_row_count, width_part = tokens.shape
    full_width = norm_gain.shape[0]
    sources = lax.axis_size("dp")
    tensor_size = lax.axis_size("tensor")
    data_index = lax.axis_index("dp")
    tensor_index = lax.axis_index("tensor")
    query_width = w_query.shape[1]
    key_width = key_weight.shape[1]
    heads_local = query_width // HEAD_SIZE
    kv_local = key_width // HEAD_SIZE
    query_group_width = heads_local // kv_local
    scale_factor = 1.0 / math.sqrt(HEAD_SIZE)
    gain_part = lax.dynamic_slice_in_dim(norm_gain, tensor_index * width_part, width_part)
    x_float = tokens.astype(jnp.float32)

    block_count = block_owner.shape[1]
    owner_row = lax.dynamic_slice_in_dim(block_owner, data_index, 1, 0)[0]
    slot_index = jnp.arange(sources, dtype=jnp.int32)
    send_table = (owner_row[None, :] == slot_index[:, None]).astype(jnp.bfloat16)

    home_rows = token_row_count // block_count
    gathered, grad_output = gather_features(
        tokens, "tensor", tensor_size, tensor_index, tied=grad_output
    )
    owned_blocks = grad_output.reshape(block_count, home_rows, width_part)
    if sources <= 16:
        returned = [lax.dynamic_index_in_dim(owned_blocks, data_index, 0, keepdims=False)]
        for shift in range(1, sources):
            pairs = [(a, (a + shift) % sources) for a in range(sources)]
            piece = lax.dynamic_index_in_dim(
                owned_blocks, (data_index + shift) % sources, 0, keepdims=False
            )
            returned.append(lax.ppermute(piece, "dp", pairs))
        returned = jnp.stack(returned)
        came_over = (
            ((data_index - owner_row) % sources)[:, None] == slot_index[None, :]
        ).astype(jnp.bfloat16)
        grad_home = (
            jnp.einsum("js,srw->jrw", came_over, returned, preferred_element_type=jnp.float32)
            .astype(jnp.bfloat16)
            .reshape(token_row_count, width_part)
        )
    else:
        arrived = lax.all_to_all(
            owned_blocks.reshape(block_count, -1), "dp", split_axis=0, concat_axis=0, tiled=True
        )
        grad_home = (
            lax.dot_general(
                send_table, arrived, (((0,), (0,)), ((), ())), preferred_element_type=jnp.float32
            )
            .astype(jnp.bfloat16)
            .reshape(token_row_count, width_part)
        )

    gathered_float = gathered.astype(jnp.float32)
    inverse = lax.rsqrt(jnp.mean(gathered_float * gathered_float, axis=1) + NORM_EPSILON)
    normed_input = (gathered_float * inverse[:, None] * norm_gain[None, :]).astype(jnp.bfloat16)
    query_raw = jnp.dot(normed_input, w_query, preferred_element_type=jnp.float32)
    key_raw = jnp.dot(normed_input, key_weight, preferred_element_type=jnp.float32)
    value_raw = jnp.dot(normed_input, value_weight, preferred_element_type=jnp.float32)
    doc_ids, positions = doc_tables(doc_lengths[0], token_row_count)
    token_index = jnp.arange(token_row_count, dtype=jnp.int32)
    allowed = (doc_ids[:, None] == doc_ids[None, :]) & (
        token_index[None, :] <= token_index[:, None]
    )
    cosine, sine_table = rope_tables(positions, HEAD_SIZE)
    query_rows = rotate(
        query_raw.reshape(token_row_count, heads_local, HEAD_SIZE), cosine, sine_table
    ).astype(jnp.bfloat16)
    keys = rotate(
        key_raw.reshape(token_row_count, kv_local, HEAD_SIZE), cosine, sine_table
    ).astype(jnp.bfloat16)
    value_rows = value_raw.astype(jnp.bfloat16).reshape(token_row_count, kv_local, HEAD_SIZE)
    grouped_query = query_rows.reshape(token_row_count, kv_local, query_group_width, HEAD_SIZE)
    scores = (
        jnp.einsum("qkgd,skd->kgqs", grouped_query, keys, preferred_element_type=jnp.float32)
        * scale_factor
    )
    weights = jnp.where(allowed[None, None], jnp.exp(scores), 0.0)
    probs = weights / jnp.sum(weights, axis=-1, keepdims=True)
    probs_low = probs.astype(jnp.bfloat16)
    attended = jnp.einsum(
        "kgqs,skd->qkgd", probs_low, value_rows, preferred_element_type=jnp.float32
    ).astype(jnp.bfloat16)
    attended_flat = attended.reshape(token_row_count, query_width)
    mixed_partial = jnp.dot(attended_flat, w_out, preferred_element_type=jnp.float32)
    grad_full, _ = gather_features(grad_home, "tensor", tensor_size, tensor_index)
    mixed_partial, grad_full = lax.optimization_barrier((mixed_partial, grad_full))
    attended_gradient = lax.dot_general(
        grad_full,
        w_out,
        (((1,), (1,)), ((), ())),
        preferred_element_type=jnp.float32,
    ).astype(jnp.bfloat16)
    mixed, _, (attended_gradient,) = scatter_features(
        mixed_partial, "tensor", tensor_size, tensor_index, ties=(attended_gradient,)
    )
    output_home = (x_float + mixed).astype(jnp.bfloat16)
    grouped_gradient = attended_gradient.reshape(
        token_row_count, kv_local, query_group_width, HEAD_SIZE
    )
    delta = jnp.sum(grouped_gradient.astype(jnp.float32) * attended.astype(jnp.float32), axis=-1)
    grad_probs = jnp.einsum(
        "qkgd,skd->kgqs", grouped_gradient, value_rows, preferred_element_type=jnp.float32
    )
    grad_scores = (probs * (grad_probs - jnp.transpose(delta, (1, 2, 0))[..., None])).astype(
        jnp.bfloat16
    )
    grad_query_rot = (
        jnp.einsum("kgqs,skd->qkgd", grad_scores, keys, preferred_element_type=jnp.float32)
        * scale_factor
    )
    grad_keys_rot = (
        jnp.einsum("kgqs,qkgd->skd", grad_scores, grouped_query, preferred_element_type=jnp.float32)
        * scale_factor
    )
    value_gradient = jnp.einsum(
        "kgqs,qkgd->skd", probs_low, grouped_gradient, preferred_element_type=jnp.float32
    )
    grad_query = unrotate(
        grad_query_rot.reshape(token_row_count, heads_local, HEAD_SIZE), cosine, sine_table
    ).astype(jnp.bfloat16)
    key_gradient = unrotate(grad_keys_rot, cosine, sine_table).astype(jnp.bfloat16)
    contract_out = (((1,), (1,)), ((), ()))
    normed_partial = (
        lax.dot_general(
            grad_query.reshape(token_row_count, query_width),
            w_query,
            contract_out,
            preferred_element_type=jnp.float32,
        )
        + lax.dot_general(
            key_gradient.reshape(token_row_count, key_width),
            key_weight,
            contract_out,
            preferred_element_type=jnp.float32,
        )
        + lax.dot_general(
            value_gradient.astype(jnp.bfloat16).reshape(token_row_count, key_width),
            value_weight,
            contract_out,
            preferred_element_type=jnp.float32,
        )
    )
    output_home, normed_partial = lax.optimization_barrier((output_home, normed_partial))
    stat_partial = jnp.sum(normed_partial * norm_gain[None, :] * gathered_float, axis=1)
    home_blocks = output_home.reshape(block_count, home_rows, width_part)
    outgoing = jnp.einsum(
        "dj,jrw->drw", send_table, home_blocks, preferred_element_type=jnp.float32
    ).astype(jnp.bfloat16)
    normed_gradient, stat_sum, (outgoing,) = scatter_features(
        normed_partial, "tensor", tensor_size, tensor_index, extra=stat_partial, ties=(outgoing,)
    )
    relaid = lax.all_to_all(outgoing, "dp", split_axis=0, concat_axis=0, tiled=True).reshape(
        token_row_count, width_part
    )
    stat = stat_sum / full_width
    cubed = inverse * inverse * inverse
    grad_x = (
        grad_home.astype(jnp.float32)
        + inverse[:, None] * gain_part[None, :] * normed_gradient
        - x_float * cubed[:, None] * stat[:, None]
    )
    return (relaid, grad_x.astype(jnp.bfloat16))


def solution(mesh):
    placed = (
        P("dp", "tensor"),
        P(),
        P(None, "tensor"),
        P(None, "tensor"),
        P(None, "tensor"),
        P("tensor", None),
        P("dp", "tensor"),
        P("dp", None),
        P(),
    )
    return jax.shard_map(
        per_device,
        mesh=mesh,
        in_specs=placed,
        out_specs=(P("dp", "tensor"), P("dp", "tensor")),
        check_vma=False,
    )
```

```python
import math

import jax
import jax.numpy as jnp
from jax import lax
from jax.sharding import PartitionSpec as P

HEAD_SIZE = 128


ROPE_BASE = 500000.0
NORM_EPSILON = 1e-05


def doc_tables(lengths_row, token_row_count):
    ends = jnp.cumsum(lengths_row)
    token_index = jnp.arange(token_row_count, dtype=jnp.int32)
    passed = (token_index[:, None] >= ends[None, :]).astype(jnp.int32)
    doc_ids = jnp.sum(passed, axis=1)
    starts = jnp.max(jnp.where(passed > 0, ends[None, :], 0), axis=1)
    return (doc_ids, token_index - starts)


def rope_tables(positions, head_size):
    half_dim = head_size // 2
    steps = jnp.arange(half_dim, dtype=jnp.float32)
    inverse_freq = jnp.power(ROPE_BASE, -2.0 * steps / head_size)
    angles = positions.astype(jnp.float32)[:, None] * inverse_freq[None, :]
    return (jnp.cos(angles), jnp.sin(angles))


def rotate(vectors, cosine, sine_table):
    half_dim = vectors.shape[-1] // 2
    former = vectors[..., :half_dim]
    latter = vectors[..., half_dim:]
    cos_part = cosine[:, None, :]
    sin_part = sine_table[:, None, :]
    return jnp.concatenate(
        [former * cos_part - latter * sin_part, latter * cos_part + former * sin_part], axis=-1
    )


def unrotate(vectors, cosine, sine_table):
    half_dim = vectors.shape[-1] // 2
    former = vectors[..., :half_dim]
    latter = vectors[..., half_dim:]
    cos_part = cosine[:, None, :]
    sin_part = sine_table[:, None, :]
    return jnp.concatenate(
        [former * cos_part + latter * sin_part, latter * cos_part - former * sin_part], axis=-1
    )


def _is_pow2(n):
    return n > 1 and (n & (n - 1)) == 0


def _xor_pairs(size, bit):
    return [(i, i ^ bit) for i in range(size)]


def gather_features(shard, axis_name, size, position):
    if not _is_pow2(size):
        return lax.all_gather(shard, axis_name, axis=1, tiled=True)
    held = shard[None]
    masks = [0]
    bit = size >> 1
    while bit:
        incoming = lax.ppermute(held, axis_name, _xor_pairs(size, bit))
        held = jnp.concatenate([held, incoming], axis=0)
        masks = masks + [m ^ bit for m in masks]
        bit >>= 1
    table = jnp.asarray([masks.index(m) for m in range(size)], jnp.int32)
    blocks = [
        lax.dynamic_index_in_dim(held, table[s ^ position], axis=0, keepdims=False)
        for s in range(size)
    ]
    return jnp.concatenate(blocks, axis=1)


def scatter_features(partial, axis_name, size, position, extra=None, ties=()):
    width = partial.shape[1] // size
    if not _is_pow2(size):
        summed = lax.psum_scatter(
            partial.astype(jnp.bfloat16), axis_name, scatter_dimension=1, tiled=True
        )
        if extra is not None:
            extra = lax.psum(extra, axis_name)
        return summed.astype(jnp.float32), extra, ties
    held = [
        lax.dynamic_slice_in_dim(partial, (position ^ m) * width, width, axis=1)
        for m in range(size)
    ]
    masks = list(range(size))
    done_ties = []
    bit = 1
    while bit < size:
        keep = [i for i, m in enumerate(masks) if not m & bit]
        send = [i for i, m in enumerate(masks) if m & bit]
        outgoing = jnp.stack([held[i] for i in send]).astype(jnp.bfloat16)
        if extra is None:
            incoming = lax.ppermute(outgoing, axis_name, _xor_pairs(size, bit))
        else:
            incoming, extra_in = lax.ppermute((outgoing, extra), axis_name, _xor_pairs(size, bit))
            extra = extra + extra_in
        if ties:
            incoming, first = lax.optimization_barrier((incoming, ties[0]))
            ties = ties[1:]
            done_ties.append(first)
        sent_masks = [masks[i] ^ bit for i in send]
        held = [
            held[i] + incoming[sent_masks.index(masks[i])].astype(jnp.float32) for i in keep
        ]
        masks = [masks[i] for i in keep]
        bit <<= 1
    return held[0], extra, tuple(done_ties) + tuple(ties)


def per_device(
    tokens,
    norm_gain,
    w_query,
    key_weight,
    value_weight,
    w_out,
    grad_output,
    doc_lengths,
    block_owner,
):
    token_row_count, width_part = tokens.shape
    full_width = norm_gain.shape[0]
    sources = lax.axis_size("dp")
    tensor_size = lax.axis_size("tensor")
    data_index = lax.axis_index("dp")
    tensor_index = lax.axis_index("tensor")
    query_width = w_query.shape[1]
    key_width = key_weight.shape[1]
    heads_local = query_width // HEAD_SIZE
    kv_local = key_width // HEAD_SIZE
    query_group_width = heads_local // kv_local
    scale_factor = 1.0 / math.sqrt(HEAD_SIZE)
    gain_part = lax.dynamic_slice_in_dim(norm_gain, tensor_index * width_part, width_part)
    x_float = tokens.astype(jnp.float32)

    block_count = block_owner.shape[1]
    owner_row = lax.dynamic_slice_in_dim(block_owner, data_index, 1, 0)[0]
    slot_index = jnp.arange(sources, dtype=jnp.int32)
    send_table = (owner_row[None, :] == slot_index[:, None]).astype(jnp.bfloat16)

    home_rows = token_row_count // block_count
    owned_blocks = grad_output.reshape(block_count, home_rows, width_part)
    if sources <= 16:
        returned = [lax.dynamic_index_in_dim(owned_blocks, data_index, 0, keepdims=False)]
        for shift in range(1, sources):
            pairs = [(a, (a + shift) % sources) for a in range(sources)]
            piece = lax.dynamic_index_in_dim(
                owned_blocks, (data_index + shift) % sources, 0, keepdims=False
            )
            returned.append(lax.ppermute(piece, "dp", pairs))
        returned = jnp.stack(returned)
        came_over = (
            ((data_index - owner_row) % sources)[:, None] == slot_index[None, :]
        ).astype(jnp.bfloat16)
        grad_home = (
            jnp.einsum("js,srw->jrw", came_over, returned, preferred_element_type=jnp.float32)
            .astype(jnp.bfloat16)
            .reshape(token_row_count, width_part)
        )
    else:
        arrived = lax.all_to_all(
            owned_blocks.reshape(block_count, -1), "dp", split_axis=0, concat_axis=0, tiled=True
        )
        grad_home = (
            lax.dot_general(
                send_table, arrived, (((0,), (0,)), ((), ())), preferred_element_type=jnp.float32
            )
            .astype(jnp.bfloat16)
            .reshape(token_row_count, width_part)
        )

    gathered = lax.all_gather(tokens, "tensor", axis=1, tiled=True)
    gathered_float = gathered.astype(jnp.float32)
    inverse = lax.rsqrt(jnp.mean(gathered_float * gathered_float, axis=1) + NORM_EPSILON)
    normed_input = (gathered_float * inverse[:, None] * norm_gain[None, :]).astype(jnp.bfloat16)
    query_raw = jnp.dot(normed_input, w_query, preferred_element_type=jnp.float32)
    key_raw = jnp.dot(normed_input, key_weight, preferred_element_type=jnp.float32)
    value_raw = jnp.dot(normed_input, value_weight, preferred_element_type=jnp.float32)
    doc_ids, positions = doc_tables(doc_lengths[0], token_row_count)
    token_index = jnp.arange(token_row_count, dtype=jnp.int32)
    allowed = (doc_ids[:, None] == doc_ids[None, :]) & (
        token_index[None, :] <= token_index[:, None]
    )
    cosine, sine_table = rope_tables(positions, HEAD_SIZE)
    query_rows = rotate(
        query_raw.reshape(token_row_count, heads_local, HEAD_SIZE), cosine, sine_table
    ).astype(jnp.bfloat16)
    keys = rotate(
        key_raw.reshape(token_row_count, kv_local, HEAD_SIZE), cosine, sine_table
    ).astype(jnp.bfloat16)
    value_rows = value_raw.astype(jnp.bfloat16).reshape(token_row_count, kv_local, HEAD_SIZE)
    grouped_query = query_rows.reshape(token_row_count, kv_local, query_group_width, HEAD_SIZE)
    scores = (
        jnp.einsum("qkgd,skd->kgqs", grouped_query, keys, preferred_element_type=jnp.float32)
        * scale_factor
    )
    weights = jnp.where(allowed[None, None], jnp.exp(scores), 0.0)
    probs = weights / jnp.sum(weights, axis=-1, keepdims=True)
    probs_low = probs.astype(jnp.bfloat16)
    attended = jnp.einsum(
        "kgqs,skd->qkgd", probs_low, value_rows, preferred_element_type=jnp.float32
    ).astype(jnp.bfloat16)
    attended_flat = attended.reshape(token_row_count, query_width)
    mixed_partial = jnp.dot(attended_flat, w_out, preferred_element_type=jnp.float32)
    grad_full = lax.all_gather(grad_home, "tensor", axis=1, tiled=True)
    mixed_partial, grad_full = lax.optimization_barrier((mixed_partial, grad_full))
    attended_gradient = lax.dot_general(
        grad_full,
        w_out,
        (((1,), (1,)), ((), ())),
        preferred_element_type=jnp.float32,
    ).astype(jnp.bfloat16)
    mixed, _, (attended_gradient,) = scatter_features(
        mixed_partial, "tensor", tensor_size, tensor_index, ties=(attended_gradient,)
    )
    output_home = (x_float + mixed).astype(jnp.bfloat16)
    grouped_gradient = attended_gradient.reshape(
        token_row_count, kv_local, query_group_width, HEAD_SIZE
    )
    delta = jnp.sum(grouped_gradient.astype(jnp.float32) * attended.astype(jnp.float32), axis=-1)
    grad_probs = jnp.einsum(
        "qkgd,skd->kgqs", grouped_gradient, value_rows, preferred_element_type=jnp.float32
    )
    grad_scores = (probs * (grad_probs - jnp.transpose(delta, (1, 2, 0))[..., None])).astype(
        jnp.bfloat16
    )
    grad_query_rot = (
        jnp.einsum("kgqs,skd->qkgd", grad_scores, keys, preferred_element_type=jnp.float32)
        * scale_factor
    )
    grad_keys_rot = (
        jnp.einsum("kgqs,qkgd->skd", grad_scores, grouped_query, preferred_element_type=jnp.float32)
        * scale_factor
    )
    value_gradient = jnp.einsum(
        "kgqs,qkgd->skd", probs_low, grouped_gradient, preferred_element_type=jnp.float32
    )
    grad_query = unrotate(
        grad_query_rot.reshape(token_row_count, heads_local, HEAD_SIZE), cosine, sine_table
    ).astype(jnp.bfloat16)
    key_gradient = unrotate(grad_keys_rot, cosine, sine_table).astype(jnp.bfloat16)
    contract_out = (((1,), (1,)), ((), ()))
    normed_partial = (
        lax.dot_general(
            grad_query.reshape(token_row_count, query_width),
            w_query,
            contract_out,
            preferred_element_type=jnp.float32,
        )
        + lax.dot_general(
            key_gradient.reshape(token_row_count, key_width),
            key_weight,
            contract_out,
            preferred_element_type=jnp.float32,
        )
        + lax.dot_general(
            value_gradient.astype(jnp.bfloat16).reshape(token_row_count, key_width),
            value_weight,
            contract_out,
            preferred_element_type=jnp.float32,
        )
    )
    output_home, normed_partial = lax.optimization_barrier((output_home, normed_partial))
    stat_partial = jnp.sum(normed_partial * norm_gain[None, :] * gathered_float, axis=1)
    home_blocks = output_home.reshape(block_count, home_rows, width_part)
    outgoing = jnp.einsum(
        "dj,jrw->drw", send_table, home_blocks, preferred_element_type=jnp.float32
    ).astype(jnp.bfloat16)
    normed_gradient, stat_sum, (_, outgoing) = scatter_features(
        normed_partial,
        "tensor",
        tensor_size,
        tensor_index,
        extra=stat_partial,
        ties=(stat_partial, outgoing),
    )
    relaid = lax.all_to_all(outgoing, "dp", split_axis=0, concat_axis=0, tiled=True).reshape(
        token_row_count, width_part
    )
    stat = stat_sum / full_width
    cubed = inverse * inverse * inverse
    grad_x = (
        grad_home.astype(jnp.float32)
        + inverse[:, None] * gain_part[None, :] * normed_gradient
        - x_float * cubed[:, None] * stat[:, None]
    )
    return (relaid, grad_x.astype(jnp.bfloat16))


def solution(mesh):
    placed = (
        P("dp", "tensor"),
        P(),
        P(None, "tensor"),
        P(None, "tensor"),
        P(None, "tensor"),
        P("tensor", None),
        P("dp", "tensor"),
        P("dp", None),
        P(),
    )
    return jax.shard_map(
        per_device,
        mesh=mesh,
        in_specs=placed,
        out_specs=(P("dp", "tensor"), P("dp", "tensor")),
        check_vma=False,
    )
```

```python
import math

import jax
import jax.numpy as jnp
from jax import lax
from jax.sharding import PartitionSpec as P

HEAD_SIZE = 128


ROPE_BASE = 500000.0
NORM_EPSILON = 1e-05


def doc_tables(lengths_row, token_row_count):
    ends = jnp.cumsum(lengths_row)
    token_index = jnp.arange(token_row_count, dtype=jnp.int32)
    passed = (token_index[:, None] >= ends[None, :]).astype(jnp.int32)
    doc_ids = jnp.sum(passed, axis=1)
    starts = jnp.max(jnp.where(passed > 0, ends[None, :], 0), axis=1)
    return (doc_ids, token_index - starts)


def rope_tables(positions, head_size):
    half_dim = head_size // 2
    steps = jnp.arange(half_dim, dtype=jnp.float32)
    inverse_freq = jnp.power(ROPE_BASE, -2.0 * steps / head_size)
    angles = positions.astype(jnp.float32)[:, None] * inverse_freq[None, :]
    return (jnp.cos(angles), jnp.sin(angles))


def rotate(vectors, cosine, sine_table):
    half_dim = vectors.shape[-1] // 2
    former = vectors[..., :half_dim]
    latter = vectors[..., half_dim:]
    cos_part = cosine[:, None, :]
    sin_part = sine_table[:, None, :]
    return jnp.concatenate(
        [former * cos_part - latter * sin_part, latter * cos_part + former * sin_part], axis=-1
    )


def unrotate(vectors, cosine, sine_table):
    half_dim = vectors.shape[-1] // 2
    former = vectors[..., :half_dim]
    latter = vectors[..., half_dim:]
    cos_part = cosine[:, None, :]
    sin_part = sine_table[:, None, :]
    return jnp.concatenate(
        [former * cos_part + latter * sin_part, latter * cos_part - former * sin_part], axis=-1
    )


def _is_pow2(n):
    return n > 1 and (n & (n - 1)) == 0


def _xor_pairs(size, bit):
    return [(i, i ^ bit) for i in range(size)]


def gather_features(shard, axis_name, size, position):
    if not _is_pow2(size):
        return lax.all_gather(shard, axis_name, axis=1, tiled=True)
    held = shard[None]
    masks = [0]
    bit = size >> 1
    while bit:
        incoming = lax.ppermute(held, axis_name, _xor_pairs(size, bit))
        held = jnp.concatenate([held, incoming], axis=0)
        masks = masks + [m ^ bit for m in masks]
        bit >>= 1
    table = jnp.asarray([masks.index(m) for m in range(size)], jnp.int32)
    blocks = [
        lax.dynamic_index_in_dim(held, table[s ^ position], axis=0, keepdims=False)
        for s in range(size)
    ]
    return jnp.concatenate(blocks, axis=1)


def scatter_features(partial, axis_name, size, position, extra=None, ties=()):
    width = partial.shape[1] // size
    if not _is_pow2(size):
        summed = lax.psum_scatter(
            partial.astype(jnp.bfloat16), axis_name, scatter_dimension=1, tiled=True
        )
        if extra is not None:
            extra = lax.psum(extra, axis_name)
        return summed.astype(jnp.float32), extra, ties
    held = [
        lax.dynamic_slice_in_dim(partial, (position ^ m) * width, width, axis=1)
        for m in range(size)
    ]
    masks = list(range(size))
    done_ties = []
    bit = 1
    while bit < size:
        keep = [i for i, m in enumerate(masks) if not m & bit]
        send = [i for i, m in enumerate(masks) if m & bit]
        outgoing = jnp.stack([held[i] for i in send]).astype(jnp.bfloat16)
        if extra is None:
            incoming = lax.ppermute(outgoing, axis_name, _xor_pairs(size, bit))
        else:
            incoming, extra_in = lax.ppermute((outgoing, extra), axis_name, _xor_pairs(size, bit))
            extra = extra + extra_in
        if ties:
            incoming, first = lax.optimization_barrier((incoming, ties[0]))
            ties = ties[1:]
            done_ties.append(first)
        sent_masks = [masks[i] ^ bit for i in send]
        held = [
            held[i] + incoming[sent_masks.index(masks[i])].astype(jnp.float32) for i in keep
        ]
        masks = [masks[i] for i in keep]
        bit <<= 1
    return held[0], extra, tuple(done_ties) + tuple(ties)


def per_device(
    tokens,
    norm_gain,
    w_query,
    key_weight,
    value_weight,
    w_out,
    grad_output,
    doc_lengths,
    block_owner,
):
    token_row_count, width_part = tokens.shape
    full_width = norm_gain.shape[0]
    sources = lax.axis_size("dp")
    tensor_size = lax.axis_size("tensor")
    data_index = lax.axis_index("dp")
    tensor_index = lax.axis_index("tensor")
    query_width = w_query.shape[1]
    key_width = key_weight.shape[1]
    heads_local = query_width // HEAD_SIZE
    kv_local = key_width // HEAD_SIZE
    query_group_width = heads_local // kv_local
    scale_factor = 1.0 / math.sqrt(HEAD_SIZE)
    gain_part = lax.dynamic_slice_in_dim(norm_gain, tensor_index * width_part, width_part)
    x_float = tokens.astype(jnp.float32)

    block_count = block_owner.shape[1]
    owner_row = lax.dynamic_slice_in_dim(block_owner, data_index, 1, 0)[0]
    slot_index = jnp.arange(sources, dtype=jnp.int32)
    send_table = (owner_row[None, :] == slot_index[:, None]).astype(jnp.bfloat16)

    home_rows = token_row_count // block_count
    owned_blocks = grad_output.reshape(block_count, home_rows, width_part)
    if sources <= 16:
        returned = [lax.dynamic_index_in_dim(owned_blocks, data_index, 0, keepdims=False)]
        for shift in range(1, sources):
            pairs = [(a, (a + shift) % sources) for a in range(sources)]
            piece = lax.dynamic_index_in_dim(
                owned_blocks, (data_index + shift) % sources, 0, keepdims=False
            )
            returned.append(lax.ppermute(piece, "dp", pairs))
        returned = jnp.stack(returned)
        came_over = (
            ((data_index - owner_row) % sources)[:, None] == slot_index[None, :]
        ).astype(jnp.bfloat16)
        grad_home = (
            jnp.einsum("js,srw->jrw", came_over, returned, preferred_element_type=jnp.float32)
            .astype(jnp.bfloat16)
            .reshape(token_row_count, width_part)
        )
    else:
        arrived = lax.all_to_all(
            owned_blocks.reshape(block_count, -1), "dp", split_axis=0, concat_axis=0, tiled=True
        )
        grad_home = (
            lax.dot_general(
                send_table, arrived, (((0,), (0,)), ((), ())), preferred_element_type=jnp.float32
            )
            .astype(jnp.bfloat16)
            .reshape(token_row_count, width_part)
        )

    gathered = lax.all_gather(tokens, "tensor", axis=1, tiled=True)
    gathered_float = gathered.astype(jnp.float32)
    inverse = lax.rsqrt(jnp.mean(gathered_float * gathered_float, axis=1) + NORM_EPSILON)
    normed_input = (gathered_float * inverse[:, None] * norm_gain[None, :]).astype(jnp.bfloat16)
    query_raw = jnp.dot(normed_input, w_query, preferred_element_type=jnp.float32)
    key_raw = jnp.dot(normed_input, key_weight, preferred_element_type=jnp.float32)
    value_raw = jnp.dot(normed_input, value_weight, preferred_element_type=jnp.float32)
    doc_ids, positions = doc_tables(doc_lengths[0], token_row_count)
    token_index = jnp.arange(token_row_count, dtype=jnp.int32)
    allowed = (doc_ids[:, None] == doc_ids[None, :]) & (
        token_index[None, :] <= token_index[:, None]
    )
    cosine, sine_table = rope_tables(positions, HEAD_SIZE)
    query_rows = rotate(
        query_raw.reshape(token_row_count, heads_local, HEAD_SIZE), cosine, sine_table
    ).astype(jnp.bfloat16)
    keys = rotate(
        key_raw.reshape(token_row_count, kv_local, HEAD_SIZE), cosine, sine_table
    ).astype(jnp.bfloat16)
    value_rows = value_raw.astype(jnp.bfloat16).reshape(token_row_count, kv_local, HEAD_SIZE)
    grouped_query = query_rows.reshape(token_row_count, kv_local, query_group_width, HEAD_SIZE)
    scores = (
        jnp.einsum("qkgd,skd->kgqs", grouped_query, keys, preferred_element_type=jnp.float32)
        * scale_factor
    )
    weights = jnp.where(allowed[None, None], jnp.exp(scores), 0.0)
    probs = weights / jnp.sum(weights, axis=-1, keepdims=True)
    probs_low = probs.astype(jnp.bfloat16)
    attended = jnp.einsum(
        "kgqs,skd->qkgd", probs_low, value_rows, preferred_element_type=jnp.float32
    ).astype(jnp.bfloat16)
    attended_flat = attended.reshape(token_row_count, query_width)
    mixed_partial = jnp.dot(attended_flat, w_out, preferred_element_type=jnp.float32)
    grad_full = lax.all_gather(grad_home, "tensor", axis=1, tiled=True)
    mixed_partial, grad_full = lax.optimization_barrier((mixed_partial, grad_full))
    attended_gradient = (
        lax.dot_general(
            w_out,
            grad_full,
            (((1,), (1,)), ((), ())),
            preferred_element_type=jnp.float32,
        )
        .astype(jnp.bfloat16)
        .T
    )
    mixed, _, (attended_gradient,) = scatter_features(
        mixed_partial, "tensor", tensor_size, tensor_index, ties=(attended_gradient,)
    )
    output_home = (x_float + mixed).astype(jnp.bfloat16)
    grouped_gradient = attended_gradient.reshape(
        token_row_count, kv_local, query_group_width, HEAD_SIZE
    )
    delta = jnp.sum(grouped_gradient.astype(jnp.float32) * attended.astype(jnp.float32), axis=-1)
    grad_probs = jnp.einsum(
        "qkgd,skd->kgqs", grouped_gradient, value_rows, preferred_element_type=jnp.float32
    )
    grad_scores = (probs * (grad_probs - jnp.transpose(delta, (1, 2, 0))[..., None])).astype(
        jnp.bfloat16
    )
    grad_query_rot = (
        jnp.einsum("kgqs,skd->qkgd", grad_scores, keys, preferred_element_type=jnp.float32)
        * scale_factor
    )
    grad_keys_rot = (
        jnp.einsum("kgqs,qkgd->skd", grad_scores, grouped_query, preferred_element_type=jnp.float32)
        * scale_factor
    )
    value_gradient = jnp.einsum(
        "kgqs,qkgd->skd", probs_low, grouped_gradient, preferred_element_type=jnp.float32
    )
    grad_query = unrotate(
        grad_query_rot.reshape(token_row_count, heads_local, HEAD_SIZE), cosine, sine_table
    ).astype(jnp.bfloat16)
    key_gradient = unrotate(grad_keys_rot, cosine, sine_table).astype(jnp.bfloat16)
    contract_out = (((1,), (1,)), ((), ()))
    normed_partial = (
        lax.dot_general(
            grad_query.reshape(token_row_count, query_width),
            w_query,
            contract_out,
            preferred_element_type=jnp.float32,
        )
        + lax.dot_general(
            key_gradient.reshape(token_row_count, key_width),
            key_weight,
            contract_out,
            preferred_element_type=jnp.float32,
        )
        + lax.dot_general(
            value_gradient.astype(jnp.bfloat16).reshape(token_row_count, key_width),
            value_weight,
            contract_out,
            preferred_element_type=jnp.float32,
        )
    )
    output_home, normed_partial = lax.optimization_barrier((output_home, normed_partial))
    stat_partial = jnp.sum(normed_partial * norm_gain[None, :] * gathered_float, axis=1)
    home_blocks = output_home.reshape(block_count, home_rows, width_part)
    outgoing = jnp.einsum(
        "dj,jrw->drw", send_table, home_blocks, preferred_element_type=jnp.float32
    ).astype(jnp.bfloat16)
    normed_gradient, stat_sum, (outgoing,) = scatter_features(
        normed_partial, "tensor", tensor_size, tensor_index, extra=stat_partial, ties=(outgoing,)
    )
    relaid = lax.all_to_all(outgoing, "dp", split_axis=0, concat_axis=0, tiled=True).reshape(
        token_row_count, width_part
    )
    stat = stat_sum / full_width
    cubed = inverse * inverse * inverse
    grad_x = (
        grad_home.astype(jnp.float32)
        + inverse[:, None] * gain_part[None, :] * normed_gradient
        - x_float * cubed[:, None] * stat[:, None]
    )
    return (relaid, grad_x.astype(jnp.bfloat16))


def solution(mesh):
    placed = (
        P("dp", "tensor"),
        P(),
        P(None, "tensor"),
        P(None, "tensor"),
        P(None, "tensor"),
        P("tensor", None),
        P("dp", "tensor"),
        P("dp", None),
        P(),
    )
    return jax.shard_map(
        per_device,
        mesh=mesh,
        in_specs=placed,
        out_specs=(P("dp", "tensor"), P("dp", "tensor")),
        check_vma=False,
    )
```

```python
import math

import jax
import jax.numpy as jnp
from jax import lax
from jax.sharding import PartitionSpec as P

HEAD_SIZE = 128


ROPE_BASE = 500000.0
NORM_EPSILON = 1e-05


def doc_tables(lengths_row, token_row_count):
    ends = jnp.cumsum(lengths_row)
    token_index = jnp.arange(token_row_count, dtype=jnp.int32)
    passed = (token_index[:, None] >= ends[None, :]).astype(jnp.int32)
    doc_ids = jnp.sum(passed, axis=1)
    starts = jnp.max(jnp.where(passed > 0, ends[None, :], 0), axis=1)
    return (doc_ids, token_index - starts)


def rope_tables(positions, head_size):
    half_dim = head_size // 2
    steps = jnp.arange(half_dim, dtype=jnp.float32)
    inverse_freq = jnp.power(ROPE_BASE, -2.0 * steps / head_size)
    angles = positions.astype(jnp.float32)[:, None] * inverse_freq[None, :]
    return (jnp.cos(angles), jnp.sin(angles))


def rotate(vectors, cosine, sine_table):
    half_dim = vectors.shape[-1] // 2
    former = vectors[..., :half_dim]
    latter = vectors[..., half_dim:]
    cos_part = cosine[:, None, :]
    sin_part = sine_table[:, None, :]
    return jnp.concatenate(
        [former * cos_part - latter * sin_part, latter * cos_part + former * sin_part], axis=-1
    )


def unrotate(vectors, cosine, sine_table):
    half_dim = vectors.shape[-1] // 2
    former = vectors[..., :half_dim]
    latter = vectors[..., half_dim:]
    cos_part = cosine[:, None, :]
    sin_part = sine_table[:, None, :]
    return jnp.concatenate(
        [former * cos_part + latter * sin_part, latter * cos_part - former * sin_part], axis=-1
    )


def _is_pow2(n):
    return n > 1 and (n & (n - 1)) == 0


def _xor_pairs(size, bit):
    return [(i, i ^ bit) for i in range(size)]


def gather_features(shard, axis_name, size, position):
    if not _is_pow2(size):
        return lax.all_gather(shard, axis_name, axis=1, tiled=True)
    held = shard[None]
    masks = [0]
    bit = size >> 1
    while bit:
        incoming = lax.ppermute(held, axis_name, _xor_pairs(size, bit))
        held = jnp.concatenate([held, incoming], axis=0)
        masks = masks + [m ^ bit for m in masks]
        bit >>= 1
    table = jnp.asarray([masks.index(m) for m in range(size)], jnp.int32)
    blocks = [
        lax.dynamic_index_in_dim(held, table[s ^ position], axis=0, keepdims=False)
        for s in range(size)
    ]
    return jnp.concatenate(blocks, axis=1)


def scatter_features(partial, axis_name, size, position, extra=None, ties=()):
    width = partial.shape[1] // size
    if not _is_pow2(size):
        summed = lax.psum_scatter(
            partial.astype(jnp.bfloat16), axis_name, scatter_dimension=1, tiled=True
        )
        if extra is not None:
            extra = lax.psum(extra, axis_name)
        return summed.astype(jnp.float32), extra, ties
    held = [
        lax.dynamic_slice_in_dim(partial, (position ^ m) * width, width, axis=1)
        for m in range(size)
    ]
    masks = list(range(size))
    done_ties = []
    bit = 1
    while bit < size:
        keep = [i for i, m in enumerate(masks) if not m & bit]
        send = [i for i, m in enumerate(masks) if m & bit]
        outgoing = jnp.stack([held[i] for i in send]).astype(jnp.bfloat16)
        if extra is None:
            incoming = lax.ppermute(outgoing, axis_name, _xor_pairs(size, bit))
        else:
            incoming, extra_in = lax.ppermute((outgoing, extra), axis_name, _xor_pairs(size, bit))
            extra = extra + extra_in
        if ties:
            incoming, first = lax.optimization_barrier((incoming, ties[0]))
            ties = ties[1:]
            done_ties.append(first)
        sent_masks = [masks[i] ^ bit for i in send]
        held = [
            held[i] + incoming[sent_masks.index(masks[i])].astype(jnp.float32) for i in keep
        ]
        masks = [masks[i] for i in keep]
        bit <<= 1
    return held[0], extra, tuple(done_ties) + tuple(ties)


def per_device(
    tokens,
    norm_gain,
    w_query,
    key_weight,
    value_weight,
    w_out,
    grad_output,
    doc_lengths,
    block_owner,
):
    token_row_count, width_part = tokens.shape
    full_width = norm_gain.shape[0]
    sources = lax.axis_size("dp")
    tensor_size = lax.axis_size("tensor")
    data_index = lax.axis_index("dp")
    tensor_index = lax.axis_index("tensor")
    query_width = w_query.shape[1]
    key_width = key_weight.shape[1]
    heads_local = query_width // HEAD_SIZE
    kv_local = key_width // HEAD_SIZE
    query_group_width = heads_local // kv_local
    scale_factor = 1.0 / math.sqrt(HEAD_SIZE)
    gain_part = lax.dynamic_slice_in_dim(norm_gain, tensor_index * width_part, width_part)
    x_float = tokens.astype(jnp.float32)

    block_count = block_owner.shape[1]
    owner_row = lax.dynamic_slice_in_dim(block_owner, data_index, 1, 0)[0]
    slot_index = jnp.arange(sources, dtype=jnp.int32)
    send_table = (owner_row[None, :] == slot_index[:, None]).astype(jnp.bfloat16)

    home_rows = token_row_count // block_count
    owned_blocks = grad_output.reshape(block_count, home_rows, width_part)
    if sources <= 16:
        returned = [lax.dynamic_index_in_dim(owned_blocks, data_index, 0, keepdims=False)]
        for shift in range(1, sources):
            pairs = [(a, (a + shift) % sources) for a in range(sources)]
            piece = lax.dynamic_index_in_dim(
                owned_blocks, (data_index + shift) % sources, 0, keepdims=False
            )
            returned.append(lax.ppermute(piece, "dp", pairs))
        returned = jnp.stack(returned)
        came_over = (
            ((data_index - owner_row) % sources)[:, None] == slot_index[None, :]
        ).astype(jnp.bfloat16)
        grad_home = (
            jnp.einsum("js,srw->jrw", came_over, returned, preferred_element_type=jnp.float32)
            .astype(jnp.bfloat16)
            .reshape(token_row_count, width_part)
        )
    else:
        arrived = lax.all_to_all(
            owned_blocks.reshape(block_count, -1), "dp", split_axis=0, concat_axis=0, tiled=True
        )
        grad_home = (
            lax.dot_general(
                send_table, arrived, (((0,), (0,)), ((), ())), preferred_element_type=jnp.float32
            )
            .astype(jnp.bfloat16)
            .reshape(token_row_count, width_part)
        )

    gathered = lax.all_gather(tokens, "tensor", axis=1, tiled=True)
    gathered_float = gathered.astype(jnp.float32)
    inverse = lax.rsqrt(jnp.mean(gathered_float * gathered_float, axis=1) + NORM_EPSILON)
    normed_input = (gathered_float * inverse[:, None] * norm_gain[None, :]).astype(jnp.bfloat16)
    query_raw = jnp.dot(normed_input, w_query, preferred_element_type=jnp.float32)
    key_raw = jnp.dot(normed_input, key_weight, preferred_element_type=jnp.float32)
    value_raw = jnp.dot(normed_input, value_weight, preferred_element_type=jnp.float32)
    doc_ids, positions = doc_tables(doc_lengths[0], token_row_count)
    token_index = jnp.arange(token_row_count, dtype=jnp.int32)
    allowed = (doc_ids[:, None] == doc_ids[None, :]) & (
        token_index[None, :] <= token_index[:, None]
    )
    cosine, sine_table = rope_tables(positions, HEAD_SIZE)
    query_rows = rotate(
        query_raw.reshape(token_row_count, heads_local, HEAD_SIZE), cosine, sine_table
    ).astype(jnp.bfloat16)
    keys = rotate(
        key_raw.reshape(token_row_count, kv_local, HEAD_SIZE), cosine, sine_table
    ).astype(jnp.bfloat16)
    value_rows = value_raw.astype(jnp.bfloat16).reshape(token_row_count, kv_local, HEAD_SIZE)
    grouped_query = query_rows.reshape(token_row_count, kv_local, query_group_width, HEAD_SIZE)
    scores = (
        jnp.einsum("qkgd,skd->kgqs", grouped_query, keys, preferred_element_type=jnp.float32)
        * scale_factor
    )
    weights = jnp.where(allowed[None, None], jnp.exp(scores), 0.0)
    probs = weights / jnp.sum(weights, axis=-1, keepdims=True)
    probs_low = probs.astype(jnp.bfloat16)
    attended = jnp.einsum(
        "kgqs,skd->qkgd", probs_low, value_rows, preferred_element_type=jnp.float32
    ).astype(jnp.bfloat16)
    attended_flat = attended.reshape(token_row_count, query_width)
    mixed_partial = jnp.dot(attended_flat, w_out, preferred_element_type=jnp.float32)
    grad_full = lax.all_gather(grad_home, "tensor", axis=1, tiled=True)
    mixed_partial, grad_full = lax.optimization_barrier((mixed_partial, grad_full))
    attended_gradient = (
        lax.dot_general(
            w_out,
            grad_full,
            (((1,), (1,)), ((), ())),
            preferred_element_type=jnp.float32,
        )
        .astype(jnp.bfloat16)
        .T
    )
    mixed, _, (attended_gradient,) = scatter_features(
        mixed_partial, "tensor", tensor_size, tensor_index, ties=(attended_gradient,)
    )
    output_home = (x_float + mixed).astype(jnp.bfloat16)
    grouped_gradient = attended_gradient.reshape(
        token_row_count, kv_local, query_group_width, HEAD_SIZE
    )
    delta = jnp.sum(grouped_gradient.astype(jnp.float32) * attended.astype(jnp.float32), axis=-1)
    grad_probs = jnp.einsum(
        "qkgd,skd->kgqs", grouped_gradient, value_rows, preferred_element_type=jnp.float32
    )
    grad_scores = (probs * (grad_probs - jnp.transpose(delta, (1, 2, 0))[..., None])).astype(
        jnp.bfloat16
    )
    half = HEAD_SIZE // 2

    def halves_product(spec, left, right):
        return [
            jnp.einsum(spec, left, piece, preferred_element_type=jnp.float32) * scale_factor
            for piece in (right[..., :half], right[..., half:])
        ]

    query_former, query_latter = halves_product("kgqs,skd->qkgd", grad_scores, keys)
    query_former = query_former.reshape(token_row_count, heads_local, half)
    query_latter = query_latter.reshape(token_row_count, heads_local, half)
    cos_part = cosine[:, None, :]
    sin_part = sine_table[:, None, :]
    grad_query = jnp.concatenate(
        [
            query_former * cos_part + query_latter * sin_part,
            query_latter * cos_part - query_former * sin_part,
        ],
        axis=-1,
    ).astype(jnp.bfloat16)
    key_former, key_latter = halves_product("kgqs,qkgd->skd", grad_scores, grouped_query)
    key_gradient = jnp.concatenate(
        [
            key_former * cos_part + key_latter * sin_part,
            key_latter * cos_part - key_former * sin_part,
        ],
        axis=-1,
    ).astype(jnp.bfloat16)
    value_gradient = jnp.einsum(
        "kgqs,qkgd->skd", probs_low, grouped_gradient, preferred_element_type=jnp.float32
    )
    contract_out = (((1,), (1,)), ((), ()))
    normed_partial = (
        lax.dot_general(
            grad_query.reshape(token_row_count, query_width),
            w_query,
            contract_out,
            preferred_element_type=jnp.float32,
        )
        + lax.dot_general(
            key_gradient.reshape(token_row_count, key_width),
            key_weight,
            contract_out,
            preferred_element_type=jnp.float32,
        )
        + lax.dot_general(
            value_gradient.astype(jnp.bfloat16).reshape(token_row_count, key_width),
            value_weight,
            contract_out,
            preferred_element_type=jnp.float32,
        )
    )
    output_home, normed_partial = lax.optimization_barrier((output_home, normed_partial))
    stat_partial = jnp.sum(normed_partial * norm_gain[None, :] * gathered_float, axis=1)
    home_blocks = output_home.reshape(block_count, home_rows, width_part)
    outgoing = jnp.einsum(
        "dj,jrw->drw", send_table, home_blocks, preferred_element_type=jnp.float32
    ).astype(jnp.bfloat16)
    normed_gradient, stat_sum, (outgoing,) = scatter_features(
        normed_partial, "tensor", tensor_size, tensor_index, extra=stat_partial, ties=(outgoing,)
    )
    relaid = lax.all_to_all(outgoing, "dp", split_axis=0, concat_axis=0, tiled=True).reshape(
        token_row_count, width_part
    )
    stat = stat_sum / full_width
    cubed = inverse * inverse * inverse
    grad_x = (
        grad_home.astype(jnp.float32)
        + inverse[:, None] * gain_part[None, :] * normed_gradient
        - x_float * cubed[:, None] * stat[:, None]
    )
    return (relaid, grad_x.astype(jnp.bfloat16))


def solution(mesh):
    placed = (
        P("dp", "tensor"),
        P(),
        P(None, "tensor"),
        P(None, "tensor"),
        P(None, "tensor"),
        P("tensor", None),
        P("dp", "tensor"),
        P("dp", None),
        P(),
    )
    return jax.shard_map(
        per_device,
        mesh=mesh,
        in_specs=placed,
        out_specs=(P("dp", "tensor"), P("dp", "tensor")),
        check_vma=False,
    )
```

```python
import math

import jax
import jax.numpy as jnp
from jax import lax
from jax.sharding import PartitionSpec as P

HEAD_SIZE = 128


ROPE_BASE = 500000.0
NORM_EPSILON = 1e-05


def doc_tables(lengths_row, token_row_count):
    ends = jnp.cumsum(lengths_row)
    token_index = jnp.arange(token_row_count, dtype=jnp.int32)
    passed = (token_index[:, None] >= ends[None, :]).astype(jnp.int32)
    doc_ids = jnp.sum(passed, axis=1)
    starts = jnp.max(jnp.where(passed > 0, ends[None, :], 0), axis=1)
    return (doc_ids, token_index - starts)


def rope_tables(positions, head_size):
    half_dim = head_size // 2
    steps = jnp.arange(half_dim, dtype=jnp.float32)
    inverse_freq = jnp.power(ROPE_BASE, -2.0 * steps / head_size)
    angles = positions.astype(jnp.float32)[:, None] * inverse_freq[None, :]
    return (jnp.cos(angles), jnp.sin(angles))


def rotate(vectors, cosine, sine_table):
    half_dim = vectors.shape[-1] // 2
    former = vectors[..., :half_dim]
    latter = vectors[..., half_dim:]
    cos_part = cosine[:, None, :]
    sin_part = sine_table[:, None, :]
    return jnp.concatenate(
        [former * cos_part - latter * sin_part, latter * cos_part + former * sin_part], axis=-1
    )


def unrotate(vectors, cosine, sine_table):
    half_dim = vectors.shape[-1] // 2
    former = vectors[..., :half_dim]
    latter = vectors[..., half_dim:]
    cos_part = cosine[:, None, :]
    sin_part = sine_table[:, None, :]
    return jnp.concatenate(
        [former * cos_part + latter * sin_part, latter * cos_part - former * sin_part], axis=-1
    )


def _is_pow2(n):
    return n > 1 and (n & (n - 1)) == 0


def _xor_pairs(size, bit):
    return [(i, i ^ bit) for i in range(size)]


def gather_features(shard, axis_name, size, position):
    if not _is_pow2(size):
        return lax.all_gather(shard, axis_name, axis=1, tiled=True)
    held = shard[None]
    masks = [0]
    bit = size >> 1
    while bit:
        incoming = lax.ppermute(held, axis_name, _xor_pairs(size, bit))
        held = jnp.concatenate([held, incoming], axis=0)
        masks = masks + [m ^ bit for m in masks]
        bit >>= 1
    table = jnp.asarray([masks.index(m) for m in range(size)], jnp.int32)
    blocks = [
        lax.dynamic_index_in_dim(held, table[s ^ position], axis=0, keepdims=False)
        for s in range(size)
    ]
    return jnp.concatenate(blocks, axis=1)


def scatter_features(partial, axis_name, size, position, extra=None, ties=()):
    width = partial.shape[1] // size
    if not _is_pow2(size):
        summed = lax.psum_scatter(
            partial.astype(jnp.bfloat16), axis_name, scatter_dimension=1, tiled=True
        )
        if extra is not None:
            extra = lax.psum(extra, axis_name)
        return summed.astype(jnp.float32), extra, ties
    held = [
        lax.dynamic_slice_in_dim(partial, (position ^ m) * width, width, axis=1)
        for m in range(size)
    ]
    masks = list(range(size))
    done_ties = []
    bit = 1
    while bit < size:
        keep = [i for i, m in enumerate(masks) if not m & bit]
        send = [i for i, m in enumerate(masks) if m & bit]
        outgoing = jnp.stack([held[i] for i in send]).astype(jnp.bfloat16)
        if extra is None:
            incoming = lax.ppermute(outgoing, axis_name, _xor_pairs(size, bit))
        else:
            incoming, extra_in = lax.ppermute((outgoing, extra), axis_name, _xor_pairs(size, bit))
            extra = extra + extra_in
            if ties and bit == 1:
                extra, first = lax.optimization_barrier((extra, ties[0]))
                ties = ties[1:]
                done_ties.append(first)
        if ties:
            incoming, first = lax.optimization_barrier((incoming, ties[0]))
            ties = ties[1:]
            done_ties.append(first)
        sent_masks = [masks[i] ^ bit for i in send]
        held = [
            held[i] + incoming[sent_masks.index(masks[i])].astype(jnp.float32) for i in keep
        ]
        masks = [masks[i] for i in keep]
        bit <<= 1
    return held[0], extra, tuple(done_ties) + tuple(ties)


def per_device(
    tokens,
    norm_gain,
    w_query,
    key_weight,
    value_weight,
    w_out,
    grad_output,
    doc_lengths,
    block_owner,
):
    token_row_count, width_part = tokens.shape
    full_width = norm_gain.shape[0]
    sources = lax.axis_size("dp")
    tensor_size = lax.axis_size("tensor")
    data_index = lax.axis_index("dp")
    tensor_index = lax.axis_index("tensor")
    query_width = w_query.shape[1]
    key_width = key_weight.shape[1]
    heads_local = query_width // HEAD_SIZE
    kv_local = key_width // HEAD_SIZE
    query_group_width = heads_local // kv_local
    scale_factor = 1.0 / math.sqrt(HEAD_SIZE)
    gain_part = lax.dynamic_slice_in_dim(norm_gain, tensor_index * width_part, width_part)
    x_float = tokens.astype(jnp.float32)

    block_count = block_owner.shape[1]
    owner_row = lax.dynamic_slice_in_dim(block_owner, data_index, 1, 0)[0]
    slot_index = jnp.arange(sources, dtype=jnp.int32)
    send_table = (owner_row[None, :] == slot_index[:, None]).astype(jnp.bfloat16)

    home_rows = token_row_count // block_count
    owned_blocks = grad_output.reshape(block_count, home_rows, width_part)
    if sources <= 16:
        returned = [lax.dynamic_index_in_dim(owned_blocks, data_index, 0, keepdims=False)]
        for shift in range(1, sources):
            pairs = [(a, (a + shift) % sources) for a in range(sources)]
            piece = lax.dynamic_index_in_dim(
                owned_blocks, (data_index + shift) % sources, 0, keepdims=False
            )
            returned.append(lax.ppermute(piece, "dp", pairs))
        returned = jnp.stack(returned)
        came_over = (
            ((data_index - owner_row) % sources)[:, None] == slot_index[None, :]
        ).astype(jnp.bfloat16)
        grad_home = (
            jnp.einsum("js,srw->jrw", came_over, returned, preferred_element_type=jnp.float32)
            .astype(jnp.bfloat16)
            .reshape(token_row_count, width_part)
        )
    else:
        arrived = lax.all_to_all(
            owned_blocks.reshape(block_count, -1), "dp", split_axis=0, concat_axis=0, tiled=True
        )
        grad_home = (
            lax.dot_general(
                send_table, arrived, (((0,), (0,)), ((), ())), preferred_element_type=jnp.float32
            )
            .astype(jnp.bfloat16)
            .reshape(token_row_count, width_part)
        )

    gathered = lax.all_gather(tokens, "tensor", axis=1, tiled=True)
    gathered_float = gathered.astype(jnp.float32)
    inverse = lax.rsqrt(jnp.mean(gathered_float * gathered_float, axis=1) + NORM_EPSILON)
    normed_input = (gathered_float * inverse[:, None] * norm_gain[None, :]).astype(jnp.bfloat16)
    query_raw = jnp.dot(normed_input, w_query, preferred_element_type=jnp.float32)
    key_raw = jnp.dot(normed_input, key_weight, preferred_element_type=jnp.float32)
    value_raw = jnp.dot(normed_input, value_weight, preferred_element_type=jnp.float32)
    doc_ids, positions = doc_tables(doc_lengths[0], token_row_count)
    token_index = jnp.arange(token_row_count, dtype=jnp.int32)
    allowed = (doc_ids[:, None] == doc_ids[None, :]) & (
        token_index[None, :] <= token_index[:, None]
    )
    cosine, sine_table = rope_tables(positions, HEAD_SIZE)
    query_rows = rotate(
        query_raw.reshape(token_row_count, heads_local, HEAD_SIZE), cosine, sine_table
    ).astype(jnp.bfloat16)
    keys = rotate(
        key_raw.reshape(token_row_count, kv_local, HEAD_SIZE), cosine, sine_table
    ).astype(jnp.bfloat16)
    value_rows = value_raw.astype(jnp.bfloat16).reshape(token_row_count, kv_local, HEAD_SIZE)
    grouped_query = query_rows.reshape(token_row_count, kv_local, query_group_width, HEAD_SIZE)
    scores = (
        jnp.einsum("qkgd,skd->kgqs", grouped_query, keys, preferred_element_type=jnp.float32)
        * scale_factor
    )
    weights = jnp.where(allowed[None, None], jnp.exp(scores), 0.0)
    probs = weights / jnp.sum(weights, axis=-1, keepdims=True)
    probs_low = probs.astype(jnp.bfloat16)
    attended = jnp.einsum(
        "kgqs,skd->qkgd", probs_low, value_rows, preferred_element_type=jnp.float32
    ).astype(jnp.bfloat16)
    attended_flat = attended.reshape(token_row_count, query_width)
    mixed_partial = jnp.dot(attended_flat, w_out, preferred_element_type=jnp.float32)
    grad_full = lax.all_gather(grad_home, "tensor", axis=1, tiled=True)
    mixed_partial, grad_full = lax.optimization_barrier((mixed_partial, grad_full))
    attended_gradient = (
        lax.dot_general(
            w_out,
            grad_full,
            (((1,), (1,)), ((), ())),
            preferred_element_type=jnp.float32,
        )
        .astype(jnp.bfloat16)
        .T
    )
    mixed, _, (attended_gradient,) = scatter_features(
        mixed_partial, "tensor", tensor_size, tensor_index, ties=(attended_gradient,)
    )
    output_home = (x_float + mixed).astype(jnp.bfloat16)
    grouped_gradient = attended_gradient.reshape(
        token_row_count, kv_local, query_group_width, HEAD_SIZE
    )
    delta = jnp.sum(grouped_gradient.astype(jnp.float32) * attended.astype(jnp.float32), axis=-1)
    grad_probs = jnp.einsum(
        "qkgd,skd->kgqs", grouped_gradient, value_rows, preferred_element_type=jnp.float32
    )
    grad_scores = (probs * (grad_probs - jnp.transpose(delta, (1, 2, 0))[..., None])).astype(
        jnp.bfloat16
    )
    half = HEAD_SIZE // 2

    def halves_product(spec, left, right):
        return [
            jnp.einsum(spec, left, piece, preferred_element_type=jnp.float32) * scale_factor
            for piece in (right[..., :half], right[..., half:])
        ]

    query_former, query_latter = halves_product("kgqs,skd->qkgd", grad_scores, keys)
    query_former = query_former.reshape(token_row_count, heads_local, half)
    query_latter = query_latter.reshape(token_row_count, heads_local, half)
    cos_part = cosine[:, None, :]
    sin_part = sine_table[:, None, :]
    grad_query = jnp.concatenate(
        [
            query_former * cos_part + query_latter * sin_part,
            query_latter * cos_part - query_former * sin_part,
        ],
        axis=-1,
    ).astype(jnp.bfloat16)
    key_former, key_latter = halves_product("kgqs,qkgd->skd", grad_scores, grouped_query)
    key_gradient = jnp.concatenate(
        [
            key_former * cos_part + key_latter * sin_part,
            key_latter * cos_part - key_former * sin_part,
        ],
        axis=-1,
    ).astype(jnp.bfloat16)
    value_gradient = jnp.einsum(
        "kgqs,qkgd->skd", probs_low, grouped_gradient, preferred_element_type=jnp.float32
    )
    contract_out = (((1,), (1,)), ((), ()))
    normed_partial = (
        lax.dot_general(
            grad_query.reshape(token_row_count, query_width),
            w_query,
            contract_out,
            preferred_element_type=jnp.float32,
        )
        + lax.dot_general(
            key_gradient.reshape(token_row_count, key_width),
            key_weight,
            contract_out,
            preferred_element_type=jnp.float32,
        )
        + lax.dot_general(
            value_gradient.astype(jnp.bfloat16).reshape(token_row_count, key_width),
            value_weight,
            contract_out,
            preferred_element_type=jnp.float32,
        )
    )
    output_home, normed_partial = lax.optimization_barrier((output_home, normed_partial))
    stat_partial = jnp.sum(normed_partial * norm_gain[None, :] * gathered_float, axis=1)
    home_blocks = output_home.reshape(block_count, home_rows, width_part)
    outgoing = jnp.einsum(
        "dj,jrw->drw", send_table, home_blocks, preferred_element_type=jnp.float32
    ).astype(jnp.bfloat16)
    normed_gradient, stat_sum, (outgoing,) = scatter_features(
        normed_partial, "tensor", tensor_size, tensor_index, extra=stat_partial, ties=(outgoing,)
    )
    relaid = lax.all_to_all(outgoing, "dp", split_axis=0, concat_axis=0, tiled=True).reshape(
        token_row_count, width_part
    )
    stat = stat_sum / full_width
    cubed = inverse * inverse * inverse
    grad_x = (
        grad_home.astype(jnp.float32)
        + inverse[:, None] * gain_part[None, :] * normed_gradient
        - x_float * cubed[:, None] * stat[:, None]
    )
    return (relaid, grad_x.astype(jnp.bfloat16))


def solution(mesh):
    placed = (
        P("dp", "tensor"),
        P(),
        P(None, "tensor"),
        P(None, "tensor"),
        P(None, "tensor"),
        P("tensor", None),
        P("dp", "tensor"),
        P("dp", None),
        P(),
    )
    return jax.shard_map(
        per_device,
        mesh=mesh,
        in_specs=placed,
        out_specs=(P("dp", "tensor"), P("dp", "tensor")),
        check_vma=False,
    )
```

```python
import math

import jax
import jax.numpy as jnp
from jax import lax
from jax.sharding import PartitionSpec as P

HEAD_SIZE = 128


ROPE_BASE = 500000.0
NORM_EPSILON = 1e-05


def doc_tables(lengths_row, token_row_count):
    ends = jnp.cumsum(lengths_row)
    token_index = jnp.arange(token_row_count, dtype=jnp.int32)
    passed = (token_index[:, None] >= ends[None, :]).astype(jnp.int32)
    doc_ids = jnp.sum(passed, axis=1)
    starts = jnp.max(jnp.where(passed > 0, ends[None, :], 0), axis=1)
    return (doc_ids, token_index - starts)


def rope_tables(positions, head_size):
    half_dim = head_size // 2
    steps = jnp.arange(half_dim, dtype=jnp.float32)
    inverse_freq = jnp.power(ROPE_BASE, -2.0 * steps / head_size)
    angles = positions.astype(jnp.float32)[:, None] * inverse_freq[None, :]
    return (jnp.cos(angles), jnp.sin(angles))


def rotate(vectors, cosine, sine_table):
    half_dim = vectors.shape[-1] // 2
    former = vectors[..., :half_dim]
    latter = vectors[..., half_dim:]
    cos_part = cosine[:, None, :]
    sin_part = sine_table[:, None, :]
    return jnp.concatenate(
        [former * cos_part - latter * sin_part, latter * cos_part + former * sin_part], axis=-1
    )


def unrotate(vectors, cosine, sine_table):
    half_dim = vectors.shape[-1] // 2
    former = vectors[..., :half_dim]
    latter = vectors[..., half_dim:]
    cos_part = cosine[:, None, :]
    sin_part = sine_table[:, None, :]
    return jnp.concatenate(
        [former * cos_part + latter * sin_part, latter * cos_part - former * sin_part], axis=-1
    )


def _is_pow2(n):
    return n > 1 and (n & (n - 1)) == 0


def _xor_pairs(size, bit):
    return [(i, i ^ bit) for i in range(size)]


def gather_features(shard, axis_name, size, position):
    if not _is_pow2(size):
        return lax.all_gather(shard, axis_name, axis=1, tiled=True)
    held = shard[None]
    masks = [0]
    bit = size >> 1
    while bit:
        incoming = lax.ppermute(held, axis_name, _xor_pairs(size, bit))
        held = jnp.concatenate([held, incoming], axis=0)
        masks = masks + [m ^ bit for m in masks]
        bit >>= 1
    table = jnp.asarray([masks.index(m) for m in range(size)], jnp.int32)
    blocks = [
        lax.dynamic_index_in_dim(held, table[s ^ position], axis=0, keepdims=False)
        for s in range(size)
    ]
    return jnp.concatenate(blocks, axis=1)


def scatter_features(partial, axis_name, size, position, extra=None, ties=(), split_last=False):
    width = partial.shape[1] // size
    if not _is_pow2(size):
        summed = lax.psum_scatter(
            partial.astype(jnp.bfloat16), axis_name, scatter_dimension=1, tiled=True
        )
        if extra is not None:
            extra = lax.psum(extra, axis_name)
        summed = summed.astype(jnp.float32)
        if split_last:
            summed = (summed, jnp.zeros(summed.shape, jnp.bfloat16))
        return summed, extra, ties
    held = [
        lax.dynamic_slice_in_dim(partial, (position ^ m) * width, width, axis=1)
        for m in range(size)
    ]
    masks = list(range(size))
    done_ties = []
    bit = 1
    while bit < size:
        keep = [i for i, m in enumerate(masks) if not m & bit]
        send = [i for i, m in enumerate(masks) if m & bit]
        outgoing = jnp.stack([held[i] for i in send]).astype(jnp.bfloat16)
        if extra is None:
            incoming = lax.ppermute(outgoing, axis_name, _xor_pairs(size, bit))
        else:
            incoming, extra_in = lax.ppermute((outgoing, extra), axis_name, _xor_pairs(size, bit))
            extra = extra + extra_in
        if ties:
            incoming, first = lax.optimization_barrier((incoming, ties[0]))
            ties = ties[1:]
            done_ties.append(first)
        sent_masks = [masks[i] ^ bit for i in send]
        if split_last and bit * 2 >= size:
            own = held[keep[0]]
            return (own, incoming[0]), extra, tuple(done_ties) + tuple(ties)
        held = [
            held[i] + incoming[sent_masks.index(masks[i])].astype(jnp.float32) for i in keep
        ]
        masks = [masks[i] for i in keep]
        bit <<= 1
    return held[0], extra, tuple(done_ties) + tuple(ties)


def per_device(
    tokens,
    norm_gain,
    w_query,
    key_weight,
    value_weight,
    w_out,
    grad_output,
    doc_lengths,
    block_owner,
):
    token_row_count, width_part = tokens.shape
    full_width = norm_gain.shape[0]
    sources = lax.axis_size("dp")
    tensor_size = lax.axis_size("tensor")
    data_index = lax.axis_index("dp")
    tensor_index = lax.axis_index("tensor")
    query_width = w_query.shape[1]
    key_width = key_weight.shape[1]
    heads_local = query_width // HEAD_SIZE
    kv_local = key_width // HEAD_SIZE
    query_group_width = heads_local // kv_local
    scale_factor = 1.0 / math.sqrt(HEAD_SIZE)
    gain_part = lax.dynamic_slice_in_dim(norm_gain, tensor_index * width_part, width_part)
    x_float = tokens.astype(jnp.float32)

    block_count = block_owner.shape[1]
    owner_row = lax.dynamic_slice_in_dim(block_owner, data_index, 1, 0)[0]
    slot_index = jnp.arange(sources, dtype=jnp.int32)
    send_table = (owner_row[None, :] == slot_index[:, None]).astype(jnp.bfloat16)

    home_rows = token_row_count // block_count
    owned_blocks = grad_output.reshape(block_count, home_rows, width_part)
    if sources <= 16:
        returned = [lax.dynamic_index_in_dim(owned_blocks, data_index, 0, keepdims=False)]
        for shift in range(1, sources):
            pairs = [(a, (a + shift) % sources) for a in range(sources)]
            piece = lax.dynamic_index_in_dim(
                owned_blocks, (data_index + shift) % sources, 0, keepdims=False
            )
            returned.append(lax.ppermute(piece, "dp", pairs))
        returned = jnp.stack(returned)
        came_over = (
            ((data_index - owner_row) % sources)[:, None] == slot_index[None, :]
        ).astype(jnp.bfloat16)
        grad_home = (
            jnp.einsum("js,srw->jrw", came_over, returned, preferred_element_type=jnp.float32)
            .astype(jnp.bfloat16)
            .reshape(token_row_count, width_part)
        )
    else:
        arrived = lax.all_to_all(
            owned_blocks.reshape(block_count, -1), "dp", split_axis=0, concat_axis=0, tiled=True
        )
        grad_home = (
            lax.dot_general(
                send_table, arrived, (((0,), (0,)), ((), ())), preferred_element_type=jnp.float32
            )
            .astype(jnp.bfloat16)
            .reshape(token_row_count, width_part)
        )

    gathered = lax.all_gather(tokens, "tensor", axis=1, tiled=True)
    gathered_float = gathered.astype(jnp.float32)
    inverse = lax.rsqrt(jnp.mean(gathered_float * gathered_float, axis=1) + NORM_EPSILON)
    normed_input = (gathered_float * inverse[:, None] * norm_gain[None, :]).astype(jnp.bfloat16)
    query_raw = jnp.dot(normed_input, w_query, preferred_element_type=jnp.float32)
    key_raw = jnp.dot(normed_input, key_weight, preferred_element_type=jnp.float32)
    value_raw = jnp.dot(normed_input, value_weight, preferred_element_type=jnp.float32)
    doc_ids, positions = doc_tables(doc_lengths[0], token_row_count)
    token_index = jnp.arange(token_row_count, dtype=jnp.int32)
    allowed = (doc_ids[:, None] == doc_ids[None, :]) & (
        token_index[None, :] <= token_index[:, None]
    )
    cosine, sine_table = rope_tables(positions, HEAD_SIZE)
    query_rows = rotate(
        query_raw.reshape(token_row_count, heads_local, HEAD_SIZE), cosine, sine_table
    ).astype(jnp.bfloat16)
    keys = rotate(
        key_raw.reshape(token_row_count, kv_local, HEAD_SIZE), cosine, sine_table
    ).astype(jnp.bfloat16)
    value_rows = value_raw.astype(jnp.bfloat16).reshape(token_row_count, kv_local, HEAD_SIZE)
    grouped_query = query_rows.reshape(token_row_count, kv_local, query_group_width, HEAD_SIZE)
    scores = (
        jnp.einsum("qkgd,skd->kgqs", grouped_query, keys, preferred_element_type=jnp.float32)
        * scale_factor
    )
    weights = jnp.where(allowed[None, None], jnp.exp(scores), 0.0)
    probs = weights / jnp.sum(weights, axis=-1, keepdims=True)
    probs_low = probs.astype(jnp.bfloat16)
    attended = jnp.einsum(
        "kgqs,skd->qkgd", probs_low, value_rows, preferred_element_type=jnp.float32
    ).astype(jnp.bfloat16)
    attended_flat = attended.reshape(token_row_count, query_width)
    mixed_partial = jnp.dot(attended_flat, w_out, preferred_element_type=jnp.float32)
    grad_full = lax.all_gather(grad_home, "tensor", axis=1, tiled=True)
    mixed_partial, grad_full = lax.optimization_barrier((mixed_partial, grad_full))
    attended_gradient = (
        lax.dot_general(
            w_out,
            grad_full,
            (((1,), (1,)), ((), ())),
            preferred_element_type=jnp.float32,
        )
        .astype(jnp.bfloat16)
        .T
    )
    mixed, _, (attended_gradient,) = scatter_features(
        mixed_partial, "tensor", tensor_size, tensor_index, ties=(attended_gradient,)
    )
    output_home = (x_float + mixed).astype(jnp.bfloat16)
    grouped_gradient = attended_gradient.reshape(
        token_row_count, kv_local, query_group_width, HEAD_SIZE
    )
    delta = jnp.sum(grouped_gradient.astype(jnp.float32) * attended.astype(jnp.float32), axis=-1)
    grad_probs = jnp.einsum(
        "qkgd,skd->kgqs", grouped_gradient, value_rows, preferred_element_type=jnp.float32
    )
    grad_scores = (probs * (grad_probs - jnp.transpose(delta, (1, 2, 0))[..., None])).astype(
        jnp.bfloat16
    )
    half = HEAD_SIZE // 2

    def halves_product(spec, left, right):
        return [
            jnp.einsum(spec, left, piece, preferred_element_type=jnp.float32) * scale_factor
            for piece in (right[..., :half], right[..., half:])
        ]

    query_former, query_latter = halves_product("kgqs,skd->qkgd", grad_scores, keys)
    query_former = query_former.reshape(token_row_count, heads_local, half)
    query_latter = query_latter.reshape(token_row_count, heads_local, half)
    cos_part = cosine[:, None, :]
    sin_part = sine_table[:, None, :]
    grad_query = jnp.concatenate(
        [
            query_former * cos_part + query_latter * sin_part,
            query_latter * cos_part - query_former * sin_part,
        ],
        axis=-1,
    ).astype(jnp.bfloat16)
    key_former, key_latter = halves_product("kgqs,qkgd->skd", grad_scores, grouped_query)
    key_gradient = jnp.concatenate(
        [
            key_former * cos_part + key_latter * sin_part,
            key_latter * cos_part - key_former * sin_part,
        ],
        axis=-1,
    ).astype(jnp.bfloat16)
    value_gradient = jnp.einsum(
        "kgqs,qkgd->skd", probs_low, grouped_gradient, preferred_element_type=jnp.float32
    )
    contract_out = (((1,), (1,)), ((), ()))
    normed_partial = (
        lax.dot_general(
            grad_query.reshape(token_row_count, query_width),
            w_query,
            contract_out,
            preferred_element_type=jnp.float32,
        )
        + lax.dot_general(
            key_gradient.reshape(token_row_count, key_width),
            key_weight,
            contract_out,
            preferred_element_type=jnp.float32,
        )
        + lax.dot_general(
            value_gradient.astype(jnp.bfloat16).reshape(token_row_count, key_width),
            value_weight,
            contract_out,
            preferred_element_type=jnp.float32,
        )
    )
    output_home, normed_partial = lax.optimization_barrier((output_home, normed_partial))
    stat_partial = jnp.sum(normed_partial * norm_gain[None, :] * gathered_float, axis=1)
    home_blocks = output_home.reshape(block_count, home_rows, width_part)
    outgoing = jnp.einsum(
        "dj,jrw->drw", send_table, home_blocks, preferred_element_type=jnp.float32
    ).astype(jnp.bfloat16)
    normed_gradient, stat_sum, (outgoing,) = scatter_features(
        normed_partial,
        "tensor",
        tensor_size,
        tensor_index,
        extra=stat_partial,
        ties=(outgoing,),
        split_last=True,
    )
    relaid = lax.all_to_all(outgoing, "dp", split_axis=0, concat_axis=0, tiled=True).reshape(
        token_row_count, width_part
    )
    stat = stat_sum / full_width
    cubed = inverse * inverse * inverse
    own_part, last_part = normed_gradient
    scale_rows = inverse[:, None] * gain_part[None, :]
    base = grad_home.astype(jnp.float32) + scale_rows * own_part
    base, last_part = lax.optimization_barrier((base, last_part))
    grad_x = (
        base
        + scale_rows * last_part.astype(jnp.float32)
        - x_float * cubed[:, None] * stat[:, None]
    )
    return (relaid, grad_x.astype(jnp.bfloat16))


def solution(mesh):
    placed = (
        P("dp", "tensor"),
        P(),
        P(None, "tensor"),
        P(None, "tensor"),
        P(None, "tensor"),
        P("tensor", None),
        P("dp", "tensor"),
        P("dp", None),
        P(),
    )
    return jax.shard_map(
        per_device,
        mesh=mesh,
        in_specs=placed,
        out_specs=(P("dp", "tensor"), P("dp", "tensor")),
        check_vma=False,
    )
```

```python
import math

import jax
import jax.numpy as jnp
from jax import lax
from jax.sharding import PartitionSpec as P

HEAD_SIZE = 128


ROPE_BASE = 500000.0
NORM_EPSILON = 1e-05


def doc_tables(lengths_row, token_row_count):
    ends = jnp.cumsum(lengths_row)
    token_index = jnp.arange(token_row_count, dtype=jnp.int32)
    passed = (token_index[:, None] >= ends[None, :]).astype(jnp.int32)
    doc_ids = jnp.sum(passed, axis=1)
    starts = jnp.max(jnp.where(passed > 0, ends[None, :], 0), axis=1)
    return (doc_ids, token_index - starts)


def rope_tables(positions, head_size):
    half_dim = head_size // 2
    steps = jnp.arange(half_dim, dtype=jnp.float32)
    inverse_freq = jnp.power(ROPE_BASE, -2.0 * steps / head_size)
    angles = positions.astype(jnp.float32)[:, None] * inverse_freq[None, :]
    return (jnp.cos(angles), jnp.sin(angles))


def rotate(vectors, cosine, sine_table):
    half_dim = vectors.shape[-1] // 2
    former = vectors[..., :half_dim]
    latter = vectors[..., half_dim:]
    cos_part = cosine[:, None, :]
    sin_part = sine_table[:, None, :]
    return jnp.concatenate(
        [former * cos_part - latter * sin_part, latter * cos_part + former * sin_part], axis=-1
    )


def unrotate(vectors, cosine, sine_table):
    half_dim = vectors.shape[-1] // 2
    former = vectors[..., :half_dim]
    latter = vectors[..., half_dim:]
    cos_part = cosine[:, None, :]
    sin_part = sine_table[:, None, :]
    return jnp.concatenate(
        [former * cos_part + latter * sin_part, latter * cos_part - former * sin_part], axis=-1
    )


def _is_pow2(n):
    return n > 1 and (n & (n - 1)) == 0


def _xor_pairs(size, bit):
    return [(i, i ^ bit) for i in range(size)]


def gather_features(shard, axis_name, size, position):
    if not _is_pow2(size):
        return lax.all_gather(shard, axis_name, axis=1, tiled=True)
    held = shard[None]
    masks = [0]
    bit = size >> 1
    while bit:
        incoming = lax.ppermute(held, axis_name, _xor_pairs(size, bit))
        held = jnp.concatenate([held, incoming], axis=0)
        masks = masks + [m ^ bit for m in masks]
        bit >>= 1
    table = jnp.asarray([masks.index(m) for m in range(size)], jnp.int32)
    blocks = [
        lax.dynamic_index_in_dim(held, table[s ^ position], axis=0, keepdims=False)
        for s in range(size)
    ]
    return jnp.concatenate(blocks, axis=1)


def scatter_features(partial, axis_name, size, position, extra=None, ties=()):
    width = partial.shape[1] // size
    if not _is_pow2(size):
        summed = lax.psum_scatter(
            partial.astype(jnp.bfloat16), axis_name, scatter_dimension=1, tiled=True
        )
        if extra is not None:
            extra = lax.psum(extra, axis_name)
        return summed.astype(jnp.float32), extra, ties
    held = [
        lax.dynamic_slice_in_dim(partial, (position ^ m) * width, width, axis=1)
        for m in range(size)
    ]
    masks = list(range(size))
    done_ties = []
    bit = 1
    while bit < size:
        keep = [i for i, m in enumerate(masks) if not m & bit]
        send = [i for i, m in enumerate(masks) if m & bit]
        outgoing = jnp.stack([held[i] for i in send]).astype(jnp.bfloat16)
        if extra is None:
            incoming = lax.ppermute(outgoing, axis_name, _xor_pairs(size, bit))
        else:
            incoming, extra_in = lax.ppermute((outgoing, extra), axis_name, _xor_pairs(size, bit))
            extra = extra + extra_in
        if ties:
            incoming, first = lax.optimization_barrier((incoming, ties[0]))
            ties = ties[1:]
            done_ties.append(first)
        sent_masks = [masks[i] ^ bit for i in send]
        held = [
            held[i] + incoming[sent_masks.index(masks[i])].astype(jnp.float32) for i in keep
        ]
        masks = [masks[i] for i in keep]
        bit <<= 1
    return held[0], extra, tuple(done_ties) + tuple(ties)


def per_device(
    tokens,
    norm_gain,
    w_query,
    key_weight,
    value_weight,
    w_out,
    grad_output,
    doc_lengths,
    block_owner,
):
    token_row_count, width_part = tokens.shape
    full_width = norm_gain.shape[0]
    sources = lax.axis_size("dp")
    tensor_size = lax.axis_size("tensor")
    data_index = lax.axis_index("dp")
    tensor_index = lax.axis_index("tensor")
    query_width = w_query.shape[1]
    key_width = key_weight.shape[1]
    heads_local = query_width // HEAD_SIZE
    kv_local = key_width // HEAD_SIZE
    query_group_width = heads_local // kv_local
    scale_factor = 1.0 / math.sqrt(HEAD_SIZE)
    gain_part = lax.dynamic_slice_in_dim(norm_gain, tensor_index * width_part, width_part)
    x_float = tokens.astype(jnp.float32)

    block_count = block_owner.shape[1]
    owner_row = lax.dynamic_slice_in_dim(block_owner, data_index, 1, 0)[0]
    slot_index = jnp.arange(sources, dtype=jnp.int32)
    send_table = (owner_row[None, :] == slot_index[:, None]).astype(jnp.bfloat16)

    home_rows = token_row_count // block_count
    owned_blocks = grad_output.reshape(block_count, home_rows, width_part)
    if sources <= 16:
        returned = [lax.dynamic_index_in_dim(owned_blocks, data_index, 0, keepdims=False)]
        for shift in range(1, sources):
            pairs = [(a, (a + shift) % sources) for a in range(sources)]
            piece = lax.dynamic_index_in_dim(
                owned_blocks, (data_index + shift) % sources, 0, keepdims=False
            )
            returned.append(lax.ppermute(piece, "dp", pairs))
        returned = jnp.stack(returned)
        came_over = (
            ((data_index - owner_row) % sources)[:, None] == slot_index[None, :]
        ).astype(jnp.bfloat16)
        grad_home = (
            jnp.einsum("js,srw->jrw", came_over, returned, preferred_element_type=jnp.float32)
            .astype(jnp.bfloat16)
            .reshape(token_row_count, width_part)
        )
    else:
        arrived = lax.all_to_all(
            owned_blocks.reshape(block_count, -1), "dp", split_axis=0, concat_axis=0, tiled=True
        )
        grad_home = (
            lax.dot_general(
                send_table, arrived, (((0,), (0,)), ((), ())), preferred_element_type=jnp.float32
            )
            .astype(jnp.bfloat16)
            .reshape(token_row_count, width_part)
        )

    gathered = lax.all_gather(tokens, "tensor", axis=1, tiled=True)
    gathered_float = gathered.astype(jnp.float32)
    inverse = lax.rsqrt(jnp.mean(gathered_float * gathered_float, axis=1) + NORM_EPSILON)
    normed_input = (gathered_float * inverse[:, None] * norm_gain[None, :]).astype(jnp.bfloat16)
    query_raw = jnp.dot(normed_input, w_query, preferred_element_type=jnp.float32)
    key_raw = jnp.dot(normed_input, key_weight, preferred_element_type=jnp.float32)
    value_raw = jnp.dot(normed_input, value_weight, preferred_element_type=jnp.float32)
    doc_ids, positions = doc_tables(doc_lengths[0], token_row_count)
    token_index = jnp.arange(token_row_count, dtype=jnp.int32)
    allowed = (doc_ids[:, None] == doc_ids[None, :]) & (
        token_index[None, :] <= token_index[:, None]
    )
    cosine, sine_table = rope_tables(positions, HEAD_SIZE)
    query_rows = rotate(
        query_raw.reshape(token_row_count, heads_local, HEAD_SIZE), cosine, sine_table
    ).astype(jnp.bfloat16)
    keys = rotate(
        key_raw.reshape(token_row_count, kv_local, HEAD_SIZE), cosine, sine_table
    ).astype(jnp.bfloat16)
    value_rows = value_raw.astype(jnp.bfloat16).reshape(token_row_count, kv_local, HEAD_SIZE)
    grouped_query = query_rows.reshape(token_row_count, kv_local, query_group_width, HEAD_SIZE)
    scores = (
        jnp.einsum("qkgd,skd->kgqs", grouped_query, keys, preferred_element_type=jnp.float32)
        * scale_factor
    )
    weights = jnp.where(allowed[None, None], jnp.exp(scores), 0.0)
    probs = weights / jnp.sum(weights, axis=-1, keepdims=True)
    probs_low = probs.astype(jnp.bfloat16)
    attended = jnp.einsum(
        "kgqs,skd->qkgd", probs_low, value_rows, preferred_element_type=jnp.float32
    ).astype(jnp.bfloat16)
    attended_flat = attended.reshape(token_row_count, query_width)
    mixed_partial = jnp.dot(attended_flat, w_out, preferred_element_type=jnp.float32)
    grad_full = lax.all_gather(grad_home, "tensor", axis=1, tiled=True)
    mixed_partial, grad_full = lax.optimization_barrier((mixed_partial, grad_full))
    attended_gradient = (
        lax.dot_general(
            w_out,
            grad_full,
            (((1,), (1,)), ((), ())),
            preferred_element_type=jnp.float32,
        )
        .astype(jnp.bfloat16)
        .T
    )
    mixed, _, (attended_gradient,) = scatter_features(
        mixed_partial, "tensor", tensor_size, tensor_index, ties=(attended_gradient,)
    )
    output_home = (x_float + mixed).astype(jnp.bfloat16)
    grouped_gradient = attended_gradient.reshape(
        token_row_count, kv_local, query_group_width, HEAD_SIZE
    )
    delta = jnp.sum(grouped_gradient.astype(jnp.float32) * attended.astype(jnp.float32), axis=-1)
    grad_probs = jnp.einsum(
        "qkgd,skd->kgqs", grouped_gradient, value_rows, preferred_element_type=jnp.float32
    )
    grad_scores = (probs * (grad_probs - jnp.transpose(delta, (1, 2, 0))[..., None])).astype(
        jnp.bfloat16
    )
    half = HEAD_SIZE // 2

    def halves_product(spec, left, right):
        return [
            jnp.einsum(spec, left, piece, preferred_element_type=jnp.float32) * scale_factor
            for piece in (right[..., :half], right[..., half:])
        ]

    query_former, query_latter = halves_product("kgqs,skd->qkgd", grad_scores, keys)
    query_former = query_former.reshape(token_row_count, heads_local, half)
    query_latter = query_latter.reshape(token_row_count, heads_local, half)
    cos_part = cosine[:, None, :]
    sin_part = sine_table[:, None, :]
    grad_query = jnp.concatenate(
        [
            query_former * cos_part + query_latter * sin_part,
            query_latter * cos_part - query_former * sin_part,
        ],
        axis=-1,
    ).astype(jnp.bfloat16)
    key_former, key_latter = halves_product("kgqs,qkgd->skd", grad_scores, grouped_query)
    key_gradient = jnp.concatenate(
        [
            key_former * cos_part + key_latter * sin_part,
            key_latter * cos_part - key_former * sin_part,
        ],
        axis=-1,
    ).astype(jnp.bfloat16)
    value_gradient = jnp.einsum(
        "kgqs,qkgd->skd", probs_low, grouped_gradient, preferred_element_type=jnp.float32
    )
    contract_out = (((1,), (1,)), ((), ()))
    normed_partial = (
        lax.dot_general(
            grad_query.reshape(token_row_count, query_width),
            w_query,
            contract_out,
            preferred_element_type=jnp.float32,
        )
        + lax.dot_general(
            key_gradient.reshape(token_row_count, key_width),
            key_weight,
            contract_out,
            preferred_element_type=jnp.float32,
        )
        + lax.dot_general(
            value_gradient.astype(jnp.bfloat16).reshape(token_row_count, key_width),
            value_weight,
            contract_out,
            preferred_element_type=jnp.float32,
        )
    )
    stat_partial = jnp.sum(normed_partial * norm_gain[None, :] * gathered_float, axis=1)
    home_blocks = output_home.reshape(block_count, home_rows, width_part)
    outgoing = jnp.einsum(
        "dj,jrw->drw", send_table, home_blocks, preferred_element_type=jnp.float32
    ).astype(jnp.bfloat16)
    normed_gradient, stat_sum, (outgoing,) = scatter_features(
        normed_partial, "tensor", tensor_size, tensor_index, extra=stat_partial, ties=(outgoing,)
    )
    relaid = lax.all_to_all(outgoing, "dp", split_axis=0, concat_axis=0, tiled=True).reshape(
        token_row_count, width_part
    )
    stat = stat_sum / full_width
    cubed = inverse * inverse * inverse
    grad_x = (
        grad_home.astype(jnp.float32)
        + inverse[:, None] * gain_part[None, :] * normed_gradient
        - x_float * cubed[:, None] * stat[:, None]
    )
    return (relaid, grad_x.astype(jnp.bfloat16))


def solution(mesh):
    placed = (
        P("dp", "tensor"),
        P(),
        P(None, "tensor"),
        P(None, "tensor"),
        P(None, "tensor"),
        P("tensor", None),
        P("dp", "tensor"),
        P("dp", None),
        P(),
    )
    return jax.shard_map(
        per_device,
        mesh=mesh,
        in_specs=placed,
        out_specs=(P("dp", "tensor"), P("dp", "tensor")),
        check_vma=False,
    )
```
